128 devices in a mesh: segment: 4 (over x), dp: 32 (over z, y, core).
Axes of the slice: x: 4, y: 4, z: 4, core: 2. Of those that a mesh axis runs over, the one named last changes fastest.
Arguments:
- segment_inputs: bfloat16 [4, 64, 256, 1024], P('segment', 'dp'), may hold values from -6 to 6
- cotangent: bfloat16 [64, 256, 1024], P('dp'), may hold values from -6 to 6
- order: int32 [32, 2], P('dp'), may hold values from 0 to 1, each once within a row
- norm_gain: float32 [4, 1024], P('segment'), may hold values from 0.1 to 1.9
- w_qkv: bfloat16 [4, 1024, 1536], P('segment'), may hold values from -1 to 1
- w_out: bfloat16 [4, 512, 1024], P('segment'), may hold values from -0.25 to 0.25
- global_blocks: int32 [4, 2], P('segment'), may hold values from 0 to 3
- random_blocks: int32 [4, 8, 4, 3], P('segment'), may hold values from 0 to 3
Outputs:
- grad_inputs: bfloat16 [4, 64, 256, 1024], P('segment', 'dp')
- query_key_value_gradient: float32 [4, 1024, 1536], P('segment', 'dp')
- grad_out: float32 [4, 512, 1024], P('segment', 'dp')
- grad_gain: float32 [4, 1024], P('segment', 'dp')
The draws below stay inside these ranges and needn't reach their ends.
Inputs may be any that keep to these rules, and one draw needn't show every extreme that they name: Each row of order holds every number of 0 .. 1 once. `global_blocks`: global block ids, any block of a passage. `random_blocks`: random block ids, any block of a passage.
All inputs are finite; a program needn't handle non-finite values.
Results may differ from the reference program's by a relative error of at most 0.035.
Values may be sent and summed in bfloat16 or wider, within the bound.
No kernel may reach another device: no remote copies, remote signals or barrier semaphores. Data moves between devices by JAX's collectives and lax.ppermute only.
A program may use at most 128 MiB of HBM per device.

```python
import math
import jax
import jax.numpy as jnp
from jax import lax

D = 1024
HEADS = 8
BLOCK = 64
GLOB = 2
RAND = 3
MICRO = 2
SEQ = 256
HD = 512
NBLK = 4
PASSAGES = 64
SEGMENTS = 4
N_DP = 32


def draw_segment_inputs(key, part):
    shape = (SEGMENTS, PASSAGES, SEQ, D)
    base = jax.random.truncated_normal(jax.random.fold_in(key, 101), -6.0, 6.0, shape, jnp.float32)
    return base.astype(jnp.bfloat16)


def draw_w_qkv(key, part):
    shape = (SEGMENTS, D, 3 * HD)
    base = jax.random.truncated_normal(jax.random.fold_in(key, 204), -6.0, 6.0, shape, jnp.float32) * D ** (-0.5)
    return base.astype(jnp.bfloat16)


def with_ends(array, stream_key, least, top_value):
    longest = array.shape.index(max(array.shape))
    spots = []
    for shift in (0, 1):
        where = [jax.random.randint(jax.random.fold_in(stream_key, axis), (), 0, length) for axis, length in enumerate(array.shape)]
        where[longest] = (where[longest] + shift) % array.shape[longest]
        spots.append(tuple(where))
    return array.at[spots[0]].set(least).at[spots[1]].set(top_value)


def steps_of(key, extent, pieces, smallest, largest):
    def one(position, blocks):
        heights = jax.random.uniform(jax.random.fold_in(jax.random.fold_in(key, 6), position), (blocks,), jnp.float32, smallest / len(pieces), largest / len(pieces))
        return jnp.repeat(jnp.exp(heights), extent[position] // blocks).reshape((-1,) + (1,) * (len(extent) - position - 1))

    factor_of = one(*pieces[0])
    for cut in pieces[1:]:
        factor_of = factor_of * one(*cut)
    return factor_of


def centred(key, shape, scale, most, pieces=(), kind=jnp.bfloat16):
    drawn = scale * jax.random.normal(key, shape, jnp.float32)
    if pieces:
        drawn = drawn * steps_of(key, shape, pieces, -0.22, 0.18)
    return jnp.clip(drawn, -most, most).astype(kind)


def setup_inputs(seed: int = 0) -> dict:
    key_list = jax.random.split(jax.random.key(seed), 9)
    return {
        "segment_inputs": draw_segment_inputs(jax.random.fold_in(key_list[8], 71), 0),
        "cotangent": centred(key_list[1], (PASSAGES, SEQ, D), 1.0, 6.0, ((0, 32),)),
        "order": jax.vmap(lambda own: jax.random.permutation(own, MICRO))(jax.random.split(key_list[2], N_DP)).reshape((N_DP, MICRO)).astype(jnp.int32),
        "norm_gain": jnp.clip(1.0 + 0.18 * jax.random.normal(key_list[3], (SEGMENTS, D), jnp.float32), 0.1, 1.9),
        "w_qkv": draw_w_qkv(jax.random.fold_in(key_list[8], 71), 0),
        "w_out": centred(key_list[5], (SEGMENTS, HD, D), HD ** -0.5, 0.25, ((0, 4),)),
        "global_blocks": with_ends(jax.random.randint(key_list[6], (SEGMENTS, GLOB), 0, NBLK), jax.random.fold_in(key_list[6], 1), 0, NBLK - 1).astype(jnp.int32),
        "random_blocks": with_ends(jax.random.randint(key_list[7], (SEGMENTS, HEADS, NBLK, RAND), 0, NBLK), jax.random.fold_in(key_list[7], 1), 0, NBLK - 1).astype(jnp.int32),
    }


EPS = 1e-05

def block_ids(glob_ids, rand_ids, block_count):
    head_count = rand_ids.shape[0]
    block_rows = jnp.arange(block_count, dtype=jnp.int32)
    window = block_rows[:, None] + jnp.arange(-1, 2, dtype=jnp.int32)[None, :]
    inside = (window >= 0) & (window < block_count)
    window_ids = jnp.where(inside, window, jnp.int32(-1))
    global_ids = jnp.broadcast_to(glob_ids[None, :], (block_count, glob_ids.shape[0]))
    fixed_ids = jnp.concatenate([window_ids, global_ids], axis=1)
    fixed_ids = jnp.broadcast_to(fixed_ids[None], (head_count, block_count, fixed_ids.shape[1]))
    listed_blocks = jnp.concatenate([fixed_ids, rand_ids], axis=2)
    list_len = listed_blocks.shape[2]
    earlier = jnp.arange(list_len, dtype=jnp.int32)[:, None] > jnp.arange(list_len, dtype=jnp.int32)[None, :]
    equal_prior = (listed_blocks[..., :, None] == listed_blocks[..., None, :]) & earlier
    repeated = jnp.any(equal_prior, axis=-1)
    usable = (listed_blocks >= 0) & jnp.logical_not(repeated)
    block_index = jnp.clip(listed_blocks, 0, block_count - 1).astype(jnp.int32)
    return (block_index, usable)

def attend(qkv_in, block_index, usable):
    head_count = block_index.shape[0]
    block_count = block_index.shape[1]
    seq_len = qkv_in.shape[0]
    width = qkv_in.shape[1] // 3
    head_features = width // head_count
    block_extent = seq_len // block_count
    split_qkv = jnp.transpose(qkv_in.reshape(block_count, block_extent, 3, head_count, head_features), (2, 3, 0, 1, 4))
    query_rows = split_qkv[0]
    key_float = split_qkv[1].astype(jnp.float32)
    value_float = split_qkv[2].astype(jnp.float32)
    select_rows = jax.vmap(lambda block_set, id_rows: block_set[id_rows])
    key_sel = select_rows(key_float, block_index).astype(jnp.bfloat16).reshape(head_count, block_count, -1, head_features)
    value_sel = select_rows(value_float, block_index).astype(jnp.bfloat16).reshape(head_count, block_count, -1, head_features)
    scores = jnp.einsum('hiqd,hikd->hiqk', query_rows.astype(jnp.float32), key_sel.astype(jnp.float32))
    scores = scores * (1.0 / math.sqrt(head_features))
    key_mask = jnp.repeat(usable, block_extent, axis=2)
    scores = jnp.where(key_mask[:, :, None, :], scores, -1e+30)
    row_max = lax.optimization_barrier(jnp.max(scores, axis=-1, keepdims=True))
    weights = jnp.exp(scores - row_max)
    row_sum = lax.optimization_barrier(jnp.sum(weights, axis=-1, keepdims=True))
    attn_probs = (weights / row_sum).astype(jnp.bfloat16)
    context = jnp.einsum('hiqk,hikd->hiqd', attn_probs.astype(jnp.float32), value_sel.astype(jnp.float32))
    context = context.astype(jnp.bfloat16)
    return jnp.transpose(context, (1, 2, 0, 3)).reshape(seq_len, width)

def layer_backward(layer_x, grad_y, gain_vec, qkv_weight, out_weight, block_index, usable):
    x_float = layer_x.astype(jnp.float32)
    row_mean = lax.optimization_barrier(jnp.mean(x_float, axis=-1, keepdims=True))
    centered = x_float - row_mean
    inv_std = lax.rsqrt(lax.optimization_barrier(jnp.mean(centered * centered, axis=-1, keepdims=True)) + EPS)
    x_norm = centered * inv_std
    normed = (x_norm * gain_vec).astype(jnp.bfloat16)
    qkv_rows = jnp.dot(normed, qkv_weight, preferred_element_type=jnp.float32).astype(jnp.bfloat16)
    context, attend_back = jax.vjp(lambda qkv_in: attend(qkv_in, block_index, usable), qkv_rows)
    grad_ctx = lax.dot_general(grad_y, out_weight, (((1,), (1,)), ((), ())), preferred_element_type=jnp.float32).astype(jnp.bfloat16)
    part_out = lax.dot_general(context, grad_y, (((0,), (0,)), ((), ())), preferred_element_type=jnp.float32)
    grad_rows = attend_back(grad_ctx)[0]
    part_qkv = lax.dot_general(normed, grad_rows, (((0,), (0,)), ((), ())), preferred_element_type=jnp.float32)
    grad_normed = lax.dot_general(grad_rows, qkv_weight, (((1,), (1,)), ((), ())), preferred_element_type=jnp.float32)
    part_gain = lax.optimization_barrier(jnp.sum(grad_normed * x_norm, axis=0))
    grad_hat = grad_normed * gain_vec
    grad_in = grad_y.astype(jnp.float32) + inv_std * (grad_hat - lax.optimization_barrier(jnp.mean(grad_hat, axis=-1, keepdims=True)) - x_norm * lax.optimization_barrier(jnp.mean(grad_hat * x_norm, axis=-1, keepdims=True)))
    return (grad_in.astype(jnp.bfloat16), part_qkv, part_out, part_gain)

def reference(segment_inputs, cotangent, order, norm_gain, w_qkv, w_out, global_blocks, random_blocks):
    segments = segment_inputs.shape[0]
    groups = order.shape[0]
    per_device = order.shape[1]
    seq_len = segment_inputs.shape[2]
    block_count = seq_len // BLOCK
    slot_indices = jnp.arange(per_device, dtype=jnp.int32)
    matched = order[:, :, None] == slot_indices[None, None, :]
    inverse = lax.optimization_barrier(jnp.sum(jnp.where(matched, slot_indices[None, :, None], jnp.int32(0)), axis=1)).astype(jnp.int32)
    cot_rows = (jnp.arange(groups, dtype=jnp.int32)[:, None] * per_device + inverse).reshape(-1).astype(jnp.int32)
    grad_now = cotangent[cot_rows]
    grad_scale = 1.0 / math.sqrt(groups * per_device * seq_len)
    inputs_list = [None] * segments
    qkv_list = [None] * segments
    out_list = [None] * segments
    gain_list = [None] * segments
    for segment_id in range(segments - 1, -1, -1):
        block_index, usable = block_ids(global_blocks[segment_id], random_blocks[segment_id], block_count)
        gain_vec = norm_gain[segment_id]
        qkv_weight = w_qkv[segment_id]
        out_weight = w_out[segment_id]

        def per_passage(running, pair_in):
            grad_in, part_qkv, part_out, part_gain = layer_backward(pair_in[0], pair_in[1], gain_vec, qkv_weight, out_weight, block_index, usable)
            return ((running[0] + part_qkv, running[1] + part_out, running[2] + part_gain), grad_in)
        starts = (jnp.zeros(qkv_weight.shape, jnp.float32), jnp.zeros(out_weight.shape, jnp.float32), jnp.zeros(gain_vec.shape, jnp.float32))
        totals, grads_in = lax.scan(per_passage, starts, (segment_inputs[segment_id], grad_now))
        grad_now = grads_in
        inputs_list[segment_id] = grads_in
        qkv_list[segment_id] = totals[0] * grad_scale
        out_list[segment_id] = totals[1] * grad_scale
        gain_list[segment_id] = totals[2] * grad_scale
    return (jnp.stack(inputs_list), jnp.stack(qkv_list), jnp.stack(out_list), jnp.stack(gain_list))
```

```python
import math

import jax
import jax.numpy as jnp
from jax import lax
from jax.experimental import pallas as pl
from jax.experimental.pallas import tpu as pltpu
from jax.sharding import PartitionSpec as P

BLOCK = 64
HEAD_DIM = 64
EPS = 1e-05
F32 = jnp.float32
BF16 = jnp.bfloat16
NT = (((1,), (1,)), ((), ()))
TN = (((0,), (0,)), ((), ()))


def from_behind(value, axis, by):
    count = lax.axis_size(axis)
    pairs = [(i, i + by) for i in range(count) if 0 <= i + by < count]
    return lax.ppermute(value, axis, pairs)


def block_ids(glob_ids, rand_ids, block_count):
    head_count = rand_ids.shape[0]
    block_rows = jnp.arange(block_count, dtype=jnp.int32)
    window = block_rows[:, None] + jnp.arange(-1, 2, dtype=jnp.int32)[None, :]
    inside = (window >= 0) & (window < block_count)
    window_ids = jnp.where(inside, window, jnp.int32(-1))
    global_ids = jnp.broadcast_to(glob_ids[None, :], (block_count, glob_ids.shape[0]))
    fixed_ids = jnp.concatenate([window_ids, global_ids], axis=1)
    fixed_ids = jnp.broadcast_to(fixed_ids[None], (head_count, block_count, fixed_ids.shape[1]))
    listed_blocks = jnp.concatenate([fixed_ids, rand_ids], axis=2)
    list_len = listed_blocks.shape[2]
    earlier = (
        jnp.arange(list_len, dtype=jnp.int32)[:, None]
        > jnp.arange(list_len, dtype=jnp.int32)[None, :]
    )
    equal_prior = (listed_blocks[..., :, None] == listed_blocks[..., None, :]) & earlier
    repeated = jnp.any(equal_prior, axis=-1)
    usable = (listed_blocks >= 0) & jnp.logical_not(repeated)
    block_index = jnp.clip(listed_blocks, 0, block_count - 1)
    return (block_index, usable)


def dense_bias(block_index, usable, block_count, seq_len):
    names = block_index[..., None] == jnp.arange(block_count, dtype=jnp.int32)
    allowed = jnp.any(names & usable[..., None], axis=2)
    small = jnp.where(allowed, F32(0.0), F32(-1e30))
    extent = seq_len // block_count
    return jnp.repeat(jnp.repeat(small, extent, axis=1), extent, axis=2)


def layer_kernel(x_ref, gy_ref, gain_ref, wqkv_ref, wout_ref, bias_ref,
                 gin_ref, normed_ref, rows_ref, ctx_ref, pgain_ref, qkv_scr, gctx_scr):
    width = ctx_ref.shape[1]
    pair_w = 2 * HEAD_DIM
    scale = 1.0 / math.sqrt(HEAD_DIM)
    x = x_ref[...].astype(F32)
    mean = jnp.mean(x, axis=-1, keepdims=True)
    cen = x - mean
    inv = lax.rsqrt(jnp.mean(cen * cen, axis=-1, keepdims=True) + EPS)
    xn = cen * inv
    gain = gain_ref[...]
    normed = (xn * gain).astype(BF16)
    normed_ref[...] = normed
    qkv_scr[...] = jnp.dot(normed, wqkv_ref[...], preferred_element_type=F32).astype(BF16)
    gctx_scr[...] = lax.dot_general(
        gy_ref[...], wout_ref[...], NT, preferred_element_type=F32).astype(BF16)
    lane = lax.broadcasted_iota(jnp.int32, (1, pair_w), 1)
    low = lane < HEAD_DIM
    for pair in range(width // pair_w):
        cols = pl.ds(pair * pair_w, pair_w)
        q2 = qkv_scr[:, pl.ds(pair * pair_w, pair_w)]
        k2 = qkv_scr[:, pl.ds(width + pair * pair_w, pair_w)]
        v2 = qkv_scr[:, pl.ds(2 * width + pair * pair_w, pair_w)]
        g2 = gctx_scr[:, cols]
        outs = []
        for half in range(2):
            mine = low if half == 0 else jnp.logical_not(low)
            qh = jnp.where(mine, q2, jnp.zeros_like(q2))
            gh = jnp.where(mine, g2, jnp.zeros_like(g2))
            s = lax.dot_general(qh, k2, NT, preferred_element_type=F32) * scale
            s = s + bias_ref[2 * pair + half]
            m = jnp.max(s, axis=-1, keepdims=True)
            e = jnp.exp(s - m)
            p = e / jnp.sum(e, axis=-1, keepdims=True)
            pb = p.astype(BF16)
            ctx = jnp.dot(pb, v2, preferred_element_type=F32)
            dp = lax.dot_general(gh, v2, NT, preferred_element_type=F32).astype(BF16).astype(F32)
            rd = jnp.sum(dp * p, axis=-1, keepdims=True)
            ds = (p * (dp - rd) * scale).astype(BF16)
            dq = jnp.dot(ds, k2, preferred_element_type=F32)
            dk = lax.dot_general(ds, q2, TN, preferred_element_type=F32)
            dv = lax.dot_general(pb, g2, TN, preferred_element_type=F32)
            outs.append((ctx, dq, dk, dv))
        lo, hi = outs
        ctx_ref[:, cols] = jnp.where(low, lo[0], hi[0]).astype(BF16)
        rows_ref[:, pl.ds(pair * pair_w, pair_w)] = jnp.where(low, lo[1], hi[1]).astype(BF16)
        rows_ref[:, pl.ds(width + pair * pair_w, pair_w)] = jnp.where(low, lo[2], hi[2]).astype(BF16)
        rows_ref[:, pl.ds(2 * width + pair * pair_w, pair_w)] = jnp.where(low, lo[3], hi[3]).astype(BF16)
    gn = lax.dot_general(rows_ref[...], wqkv_ref[...], NT, preferred_element_type=F32)
    x = x_ref[...].astype(F32)
    mean = jnp.mean(x, axis=-1, keepdims=True)
    cen = x - mean
    inv = lax.rsqrt(jnp.mean(cen * cen, axis=-1, keepdims=True) + EPS)
    xn = cen * inv
    pgain_ref[...] = jnp.sum(gn * xn, axis=0, keepdims=True)
    gh = gn * gain_ref[...]
    gin = gy_ref[...].astype(F32) + inv * (
        gh
        - jnp.mean(gh, axis=-1, keepdims=True)
        - xn * jnp.mean(gh * xn, axis=-1, keepdims=True)
    )
    gin_ref[...] = gin.astype(BF16)


def layer_backward(layer_x, grad_y, gain_row, qkv_weight, out_weight, bias):
    seq_len, width_model = layer_x.shape
    qkv_cols = qkv_weight.shape[1]
    ctx_cols = out_weight.shape[0]
    flops = 2 * seq_len * width_model * (2 * qkv_cols + ctx_cols) + 12 * 2 * seq_len * seq_len * ctx_cols
    return pl.pallas_call(
        layer_kernel,
        out_shape=(
            jax.ShapeDtypeStruct((seq_len, width_model), BF16),
            jax.ShapeDtypeStruct((seq_len, width_model), BF16),
            jax.ShapeDtypeStruct((seq_len, qkv_cols), BF16),
            jax.ShapeDtypeStruct((seq_len, ctx_cols), BF16),
            jax.ShapeDtypeStruct((1, width_model), F32),
        ),
        scratch_shapes=[
            pltpu.VMEM((seq_len, qkv_cols), BF16),
            pltpu.VMEM((seq_len, ctx_cols), BF16),
        ],
        cost_estimate=pl.CostEstimate(
            flops=flops, transcendentals=bias.size, bytes_accessed=12 * 1024 * 1024),
    )(layer_x, grad_y, gain_row, qkv_weight, out_weight, bias)


def on_device(
    segment_inputs, cotangent, order, norm_gain, w_qkv, w_out, global_blocks, random_blocks
):
    segments = lax.axis_size("segment")
    my_segment = lax.axis_index("segment")
    layer_in = segment_inputs[0]
    micro_count = layer_in.shape[0]
    seq_len = layer_in.shape[1]
    width_model = layer_in.shape[2]
    gain_row = norm_gain[0][None, :]
    qkv_weight = w_qkv[0]
    out_weight = w_out[0]
    slot_order = order[0]
    block_total = seq_len // BLOCK
    block_index, usable = block_ids(global_blocks[0], random_blocks[0], block_total)
    bias = dense_bias(block_index, usable, block_total, seq_len)
    grad_scale = 1.0 / math.sqrt(lax.axis_size("dp") * micro_count * seq_len)
    qkv_cols = qkv_weight.shape[1]
    ctx_cols = out_weight.shape[0]

    def do_work(layer_x, grad_y):
        return layer_backward(layer_x, grad_y, gain_row, qkv_weight, out_weight, bias)

    def no_work(layer_x, grad_y):
        return (
            jnp.zeros(grad_y.shape, BF16),
            jnp.zeros((seq_len, width_model), BF16),
            jnp.zeros((seq_len, qkv_cols), BF16),
            jnp.zeros((seq_len, ctx_cols), BF16),
            jnp.zeros((1, width_model), F32),
        )

    grad_x = jnp.zeros((micro_count + 1, seq_len, width_model), BF16)
    normed_buf = jnp.zeros((micro_count + 1, seq_len, width_model), BF16)
    rows_buf = jnp.zeros((micro_count + 1, seq_len, qkv_cols), BF16)
    ctx_buf = jnp.zeros((micro_count + 1, seq_len, ctx_cols), BF16)
    upper_buf = jnp.zeros((micro_count + 1, seq_len, width_model), BF16)
    gain_total = jnp.zeros((1, width_model), F32)
    received = jnp.zeros(layer_in.shape[1:], BF16)
    last_tick = micro_count + segments - 1
    for timestep in range(last_tick):
        slot_now = timestep - (segments - 1) + my_segment
        active = (slot_now >= 0) & (slot_now < micro_count)
        slot_clip = jnp.clip(slot_now, 0, micro_count - 1)
        batch_id = slot_order[slot_clip]
        write_id = jnp.where(active, batch_id, jnp.int32(micro_count))
        from_output = lax.dynamic_index_in_dim(cotangent, slot_clip, 0, keepdims=False)
        incoming = jnp.where(my_segment == segments - 1, from_output, received)
        layer_x = lax.dynamic_index_in_dim(layer_in, batch_id, 0, keepdims=False)
        grad_in, normed, grad_rows, context, part_gain = lax.cond(
            active, do_work, no_work, layer_x, incoming
        )
        grad_x = lax.dynamic_update_index_in_dim(grad_x, grad_in, write_id, 0)
        gain_total = gain_total + part_gain
        normed_buf = lax.dynamic_update_index_in_dim(normed_buf, normed, write_id, 0)
        rows_buf = lax.dynamic_update_index_in_dim(rows_buf, grad_rows, write_id, 0)
        ctx_buf = lax.dynamic_update_index_in_dim(ctx_buf, context, write_id, 0)
        upper_buf = lax.dynamic_update_index_in_dim(upper_buf, incoming, write_id, 0)
        if timestep + 1 < last_tick:
            received = from_behind(grad_in, "segment", -1)
    all_normed = normed_buf[:micro_count].reshape(micro_count * seq_len, width_model)
    all_rows = rows_buf[:micro_count].reshape(micro_count * seq_len, qkv_cols)
    all_ctx = ctx_buf[:micro_count].reshape(micro_count * seq_len, ctx_cols)
    all_upper = upper_buf[:micro_count].reshape(micro_count * seq_len, width_model)
    sum_qkv = lax.dot_general(all_normed, all_rows, TN, preferred_element_type=F32)
    sum_out = lax.dot_general(all_ctx, all_upper, TN, preferred_element_type=F32)
    rows_total = qkv_weight.shape[0]
    fold = rows_total // ctx_cols
    out_folded = sum_out.reshape(rows_total, ctx_cols * width_model // rows_total)
    gain_col = gain_total.reshape(rows_total, width_model // rows_total)
    pad = jnp.zeros((rows_total, 128 - gain_col.shape[1]), F32)
    packed = jnp.concatenate([sum_qkv, out_folded, gain_col, pad], axis=1) * grad_scale
    share = lax.psum_scatter(packed.astype(BF16), "dp", scatter_dimension=0, tiled=True).astype(F32)
    share_rows = share.shape[0]
    qkv_share = share[:, :qkv_cols]
    out_share = share[:, qkv_cols:qkv_cols + out_folded.shape[1]].reshape(share_rows // fold, width_model)
    gain_share = share[:, qkv_cols + out_folded.shape[1]:qkv_cols + out_folded.shape[1] + gain_col.shape[1]].reshape(-1)
    return (grad_x[:micro_count][None], qkv_share[None], out_share[None], gain_share[None])


def solution(mesh):
    in_specs = (
        P("segment", "dp", None, None),
        P("dp", None, None),
        P("dp", None),
        P("segment", None),
        P("segment", None, None),
        P("segment", None, None),
        P("segment", None),
        P("segment", None, None, None),
    )
    out_specs = (
        P("segment", "dp", None, None),
        P("segment", "dp", None),
        P("segment", "dp", None),
        P("segment", "dp"),
    )
    return jax.shard_map(
        on_device, mesh=mesh, in_specs=in_specs, out_specs=out_specs, check_vma=False
    )
```

```python
import math

import jax
import jax.numpy as jnp
from jax import lax
from jax.experimental import pallas as pl
from jax.experimental.pallas import tpu as pltpu
from jax.sharding import PartitionSpec as P

BLOCK = 64
HEAD_DIM = 64
EPS = 1e-05
F32 = jnp.float32
BF16 = jnp.bfloat16
NT = (((1,), (1,)), ((), ()))
TN = (((0,), (0,)), ((), ()))


def from_behind(value, axis, by):
    count = lax.axis_size(axis)
    pairs = [(i, i + by) for i in range(count) if 0 <= i + by < count]
    return lax.ppermute(value, axis, pairs)


def block_ids(glob_ids, rand_ids, block_count):
    head_count = rand_ids.shape[0]
    block_rows = jnp.arange(block_count, dtype=jnp.int32)
    window = block_rows[:, None] + jnp.arange(-1, 2, dtype=jnp.int32)[None, :]
    inside = (window >= 0) & (window < block_count)
    window_ids = jnp.where(inside, window, jnp.int32(-1))
    global_ids = jnp.broadcast_to(glob_ids[None, :], (block_count, glob_ids.shape[0]))
    fixed_ids = jnp.concatenate([window_ids, global_ids], axis=1)
    fixed_ids = jnp.broadcast_to(fixed_ids[None], (head_count, block_count, fixed_ids.shape[1]))
    listed_blocks = jnp.concatenate([fixed_ids, rand_ids], axis=2)
    list_len = listed_blocks.shape[2]
    earlier = (
        jnp.arange(list_len, dtype=jnp.int32)[:, None]
        > jnp.arange(list_len, dtype=jnp.int32)[None, :]
    )
    equal_prior = (listed_blocks[..., :, None] == listed_blocks[..., None, :]) & earlier
    repeated = jnp.any(equal_prior, axis=-1)
    usable = (listed_blocks >= 0) & jnp.logical_not(repeated)
    block_index = jnp.clip(listed_blocks, 0, block_count - 1)
    return (block_index, usable)


def dense_bias(block_index, usable, block_count, seq_len):
    names = block_index[..., None] == jnp.arange(block_count, dtype=jnp.int32)
    allowed = jnp.any(names & usable[..., None], axis=2)
    small = jnp.where(allowed, F32(0.0), F32(-1e30))
    extent = seq_len // block_count
    return jnp.repeat(jnp.repeat(small, extent, axis=1), extent, axis=2)


def layer_kernel(x_ref, gy_ref, gain_ref, wqkv_ref, wout_ref, bias_ref,
                 gin_ref, normed_ref, rows_ref, ctx_ref, pgain_ref, qkv_scr, gctx_scr):
    width = ctx_ref.shape[1]
    pair_w = 2 * HEAD_DIM
    scale = 1.0 / math.sqrt(HEAD_DIM)
    x = x_ref[...].astype(F32)
    mean = jnp.mean(x, axis=-1, keepdims=True)
    cen = x - mean
    inv = lax.rsqrt(jnp.mean(cen * cen, axis=-1, keepdims=True) + EPS)
    xn = cen * inv
    gain = gain_ref[...]
    normed = (xn * gain).astype(BF16)
    normed_ref[...] = normed
    qkv_scr[...] = jnp.dot(normed, wqkv_ref[...], preferred_element_type=F32).astype(BF16)
    gctx_scr[...] = lax.dot_general(
        gy_ref[...], wout_ref[...], NT, preferred_element_type=F32).astype(BF16)
    lane = lax.broadcasted_iota(jnp.int32, (1, pair_w), 1)
    low = lane < HEAD_DIM
    for pair in range(width // pair_w):
        cols = pl.ds(pair * pair_w, pair_w)
        q2 = qkv_scr[:, pl.ds(pair * pair_w, pair_w)]
        k2 = qkv_scr[:, pl.ds(width + pair * pair_w, pair_w)]
        v2 = qkv_scr[:, pl.ds(2 * width + pair * pair_w, pair_w)]
        g2 = gctx_scr[:, cols]
        outs = []
        for half in range(2):
            mine = low if half == 0 else jnp.logical_not(low)
            qh = jnp.where(mine, q2, jnp.zeros_like(q2))
            gh = jnp.where(mine, g2, jnp.zeros_like(g2))
            s = lax.dot_general(qh, k2, NT, preferred_element_type=F32) * scale
            s = s + bias_ref[2 * pair + half]
            m = jnp.max(s, axis=-1, keepdims=True)
            e = jnp.exp(s - m)
            p = e / jnp.sum(e, axis=-1, keepdims=True)
            pb = p.astype(BF16)
            ctx = jnp.dot(pb, v2, preferred_element_type=F32)
            dp = lax.dot_general(gh, v2, NT, preferred_element_type=F32).astype(BF16).astype(F32)
            rd = jnp.sum(dp * p, axis=-1, keepdims=True)
            ds = (p * (dp - rd) * scale).astype(BF16)
            dq = jnp.dot(ds, k2, preferred_element_type=F32)
            dk = lax.dot_general(ds, q2, TN, preferred_element_type=F32)
            dv = lax.dot_general(pb, g2, TN, preferred_element_type=F32)
            outs.append((ctx, dq, dk, dv))
        lo, hi = outs
        ctx_ref[:, cols] = jnp.where(low, lo[0], hi[0]).astype(BF16)
        rows_ref[:, pl.ds(pair * pair_w, pair_w)] = jnp.where(low, lo[1], hi[1]).astype(BF16)
        rows_ref[:, pl.ds(width + pair * pair_w, pair_w)] = jnp.where(low, lo[2], hi[2]).astype(BF16)
        rows_ref[:, pl.ds(2 * width + pair * pair_w, pair_w)] = jnp.where(low, lo[3], hi[3]).astype(BF16)
    gn = lax.dot_general(rows_ref[...], wqkv_ref[...], NT, preferred_element_type=F32)
    x = x_ref[...].astype(F32)
    mean = jnp.mean(x, axis=-1, keepdims=True)
    cen = x - mean
    inv = lax.rsqrt(jnp.mean(cen * cen, axis=-1, keepdims=True) + EPS)
    xn = cen * inv
    pgain_ref[...] = jnp.sum(gn * xn, axis=0, keepdims=True)
    gh = gn * gain_ref[...]
    gin = gy_ref[...].astype(F32) + inv * (
        gh
        - jnp.mean(gh, axis=-1, keepdims=True)
        - xn * jnp.mean(gh * xn, axis=-1, keepdims=True)
    )
    gin_ref[...] = gin.astype(BF16)


def layer_backward(layer_x, grad_y, gain_row, qkv_weight, out_weight, bias):
    seq_len, width_model = layer_x.shape
    qkv_cols = qkv_weight.shape[1]
    ctx_cols = out_weight.shape[0]
    flops = 2 * seq_len * width_model * (2 * qkv_cols + ctx_cols) + 12 * 2 * seq_len * seq_len * ctx_cols
    return pl.pallas_call(
        layer_kernel,
        out_shape=(
            jax.ShapeDtypeStruct((seq_len, width_model), BF16),
            jax.ShapeDtypeStruct((seq_len, width_model), BF16),
            jax.ShapeDtypeStruct((seq_len, qkv_cols), BF16),
            jax.ShapeDtypeStruct((seq_len, ctx_cols), BF16),
            jax.ShapeDtypeStruct((1, width_model), F32),
        ),
        scratch_shapes=[
            pltpu.VMEM((seq_len, qkv_cols), BF16),
            pltpu.VMEM((seq_len, ctx_cols), BF16),
        ],
        cost_estimate=pl.CostEstimate(
            flops=flops, transcendentals=bias.size, bytes_accessed=12 * 1024 * 1024),
    )(layer_x, grad_y, gain_row, qkv_weight, out_weight, bias)


def on_device(
    segment_inputs, cotangent, order, norm_gain, w_qkv, w_out, global_blocks, random_blocks
):
    segments = lax.axis_size("segment")
    my_segment = lax.axis_index("segment")
    layer_in = segment_inputs[0]
    micro_count = layer_in.shape[0]
    seq_len = layer_in.shape[1]
    width_model = layer_in.shape[2]
    gain_row = norm_gain[0][None, :]
    qkv_weight = w_qkv[0]
    out_weight = w_out[0]
    slot_order = order[0]
    block_total = seq_len // BLOCK
    block_index, usable = block_ids(global_blocks[0], random_blocks[0], block_total)
    bias = dense_bias(block_index, usable, block_total, seq_len)
    grad_scale = 1.0 / math.sqrt(lax.axis_size("dp") * micro_count * seq_len)
    qkv_cols = qkv_weight.shape[1]
    ctx_cols = out_weight.shape[0]

    grad_x = jnp.zeros((micro_count + 1, seq_len, width_model), BF16)
    normed_buf = jnp.zeros((micro_count + 1, seq_len, width_model), BF16)
    rows_buf = jnp.zeros((micro_count + 1, seq_len, qkv_cols), BF16)
    ctx_buf = jnp.zeros((micro_count + 1, seq_len, ctx_cols), BF16)
    upper_buf = jnp.zeros((micro_count + 1, seq_len, width_model), BF16)
    gain_total = jnp.zeros((1, width_model), F32)
    received = jnp.zeros(layer_in.shape[1:], BF16)
    last_tick = micro_count + segments - 1
    for timestep in range(last_tick):
        slot_now = timestep - (segments - 1) + my_segment
        active = (slot_now >= 0) & (slot_now < micro_count)
        slot_clip = jnp.clip(slot_now, 0, micro_count - 1)
        batch_id = slot_order[slot_clip]
        write_id = jnp.where(active, batch_id, jnp.int32(micro_count))
        from_output = lax.dynamic_index_in_dim(cotangent, slot_clip, 0, keepdims=False)
        incoming = jnp.where(my_segment == segments - 1, from_output, received)
        layer_x = lax.dynamic_index_in_dim(layer_in, batch_id, 0, keepdims=False)
        grad_in, normed, grad_rows, context, part_gain = layer_backward(
            layer_x, incoming, gain_row, qkv_weight, out_weight, bias
        )
        grad_x = lax.dynamic_update_index_in_dim(grad_x, grad_in, write_id, 0)
        gain_total = gain_total + jnp.where(active, part_gain, jnp.zeros_like(part_gain))
        normed_buf = lax.dynamic_update_index_in_dim(normed_buf, normed, write_id, 0)
        rows_buf = lax.dynamic_update_index_in_dim(rows_buf, grad_rows, write_id, 0)
        ctx_buf = lax.dynamic_update_index_in_dim(ctx_buf, context, write_id, 0)
        upper_buf = lax.dynamic_update_index_in_dim(upper_buf, incoming, write_id, 0)
        if timestep + 1 < last_tick:
            received = from_behind(grad_in, "segment", -1)
    all_normed = normed_buf[:micro_count].reshape(micro_count * seq_len, width_model)
    all_rows = rows_buf[:micro_count].reshape(micro_count * seq_len, qkv_cols)
    all_ctx = ctx_buf[:micro_count].reshape(micro_count * seq_len, ctx_cols)
    all_upper = upper_buf[:micro_count].reshape(micro_count * seq_len, width_model)
    sum_qkv = lax.dot_general(all_normed, all_rows, TN, preferred_element_type=F32)
    sum_out = lax.dot_general(all_ctx, all_upper, TN, preferred_element_type=F32)
    rows_total = qkv_weight.shape[0]
    fold = rows_total // ctx_cols
    out_folded = sum_out.reshape(rows_total, ctx_cols * width_model // rows_total)
    gain_col = gain_total.reshape(rows_total, width_model // rows_total)
    pad = jnp.zeros((rows_total, 128 - gain_col.shape[1]), BF16)
    packed = jnp.concatenate(
        [(sum_qkv * grad_scale).astype(BF16), (out_folded * grad_scale).astype(BF16),
         (gain_col * grad_scale).astype(BF16), pad], axis=1)
    share = lax.psum_scatter(packed, "dp", scatter_dimension=0, tiled=True).astype(F32)
    share_rows = share.shape[0]
    qkv_share = share[:, :qkv_cols]
    out_share = share[:, qkv_cols:qkv_cols + out_folded.shape[1]].reshape(share_rows // fold, width_model)
    gain_share = share[:, qkv_cols + out_folded.shape[1]:qkv_cols + out_folded.shape[1] + gain_col.shape[1]].reshape(-1)
    return (grad_x[:micro_count][None], qkv_share[None], out_share[None], gain_share[None])


def solution(mesh):
    in_specs = (
        P("segment", "dp", None, None),
        P("dp", None, None),
        P("dp", None),
        P("segment", None),
        P("segment", None, None),
        P("segment", None, None),
        P("segment", None),
        P("segment", None, None, None),
    )
    out_specs = (
        P("segment", "dp", None, None),
        P("segment", "dp", None),
        P("segment", "dp", None),
        P("segment", "dp"),
    )
    return jax.shard_map(
        on_device, mesh=mesh, in_specs=in_specs, out_specs=out_specs, check_vma=False
    )
```

```python
import math

import jax
import jax.numpy as jnp
from jax import lax
from jax.experimental import pallas as pl
from jax.experimental.pallas import tpu as pltpu
from jax.sharding import Mesh, PartitionSpec as P

BLOCK = 64
HEAD_DIM = 64
EPS = 1e-05
F32 = jnp.float32
BF16 = jnp.bfloat16
NT = (((1,), (1,)), ((), ()))
TN = (((0,), (0,)), ((), ()))


def from_behind(value, axis, by):
    count = lax.axis_size(axis)
    pairs = [(i, i + by) for i in range(count) if 0 <= i + by < count]
    return lax.ppermute(value, axis, pairs)


def block_ids(glob_ids, rand_ids, block_count):
    head_count = rand_ids.shape[0]
    block_rows = jnp.arange(block_count, dtype=jnp.int32)
    window = block_rows[:, None] + jnp.arange(-1, 2, dtype=jnp.int32)[None, :]
    inside = (window >= 0) & (window < block_count)
    window_ids = jnp.where(inside, window, jnp.int32(-1))
    global_ids = jnp.broadcast_to(glob_ids[None, :], (block_count, glob_ids.shape[0]))
    fixed_ids = jnp.concatenate([window_ids, global_ids], axis=1)
    fixed_ids = jnp.broadcast_to(fixed_ids[None], (head_count, block_count, fixed_ids.shape[1]))
    listed_blocks = jnp.concatenate([fixed_ids, rand_ids], axis=2)
    list_len = listed_blocks.shape[2]
    earlier = (
        jnp.arange(list_len, dtype=jnp.int32)[:, None]
        > jnp.arange(list_len, dtype=jnp.int32)[None, :]
    )
    equal_prior = (listed_blocks[..., :, None] == listed_blocks[..., None, :]) & earlier
    repeated = jnp.any(equal_prior, axis=-1)
    usable = (listed_blocks >= 0) & jnp.logical_not(repeated)
    block_index = jnp.clip(listed_blocks, 0, block_count - 1)
    return (block_index, usable)


def ring_rs(blocks, axis, sign):
    n = lax.axis_size(axis)
    me = lax.axis_index(axis)
    perm = [(i, (i + sign) % n) for i in range(n)]
    acc = lax.dynamic_index_in_dim(blocks, (me - sign) % n, 0, keepdims=False).astype(F32)
    for step in range(n - 1):
        recv = lax.ppermute(acc.astype(BF16), axis, perm)
        pick = (me - sign * (step + 2)) % n
        acc = recv.astype(F32) + lax.dynamic_index_in_dim(blocks, pick, 0, keepdims=False).astype(F32)
    return acc


def dp_reduce_scatter(packed):
    cores = lax.axis_size("core")
    ys = lax.axis_size("y")
    zs = lax.axis_size("z")
    rows, cols = packed.shape
    chunk = rows // (zs * ys * cores)
    c = lax.axis_index("core")
    v = packed.reshape(zs * ys, cores, chunk, cols)
    mine = lax.dynamic_index_in_dim(v, c, 1, keepdims=False)
    other = lax.dynamic_index_in_dim(v, 1 - c, 1, keepdims=False)
    got = lax.ppermute(other, "core", [(0, 1), (1, 0)])
    s1 = (mine.astype(F32) + got.astype(F32)).astype(BF16).reshape(zs, ys, chunk, cols)
    cuts = [0, 512, 1024, 1536, cols]
    parts = [s1[..., cuts[i]:cuts[i + 1]] for i in range(4)]
    a1 = ring_rs(parts[0].transpose(1, 0, 2, 3), "y", 1)
    a2 = ring_rs(parts[1].transpose(1, 0, 2, 3), "y", -1)
    b1 = ring_rs(parts[2], "z", 1)
    b2 = ring_rs(parts[3], "z", -1)
    a1 = ring_rs(a1.astype(BF16), "z", 1)
    a2 = ring_rs(a2.astype(BF16), "z", -1)
    b1 = ring_rs(b1.astype(BF16), "y", 1)
    b2 = ring_rs(b2.astype(BF16), "y", -1)
    return jnp.concatenate([a1, a2, b1, b2], axis=-1)


def dense_bias(block_index, usable, block_count, seq_len):
    names = block_index[..., None] == jnp.arange(block_count, dtype=jnp.int32)
    allowed = jnp.any(names & usable[..., None], axis=2)
    small = jnp.where(allowed, F32(0.0), F32(-1e30))
    extent = seq_len // block_count
    return jnp.repeat(jnp.repeat(small, extent, axis=1), extent, axis=2)


def layer_kernel(x_ref, gy_ref, gain_ref, wqkv_ref, wout_ref, bias_ref,
                 gin_ref, normed_ref, rows_ref, ctx_ref, pgain_ref, qkv_scr, gctx_scr):
    width = ctx_ref.shape[1]
    pair_w = 2 * HEAD_DIM
    scale = 1.0 / math.sqrt(HEAD_DIM)
    x = x_ref[...].astype(F32)
    mean = jnp.mean(x, axis=-1, keepdims=True)
    cen = x - mean
    inv = lax.rsqrt(jnp.mean(cen * cen, axis=-1, keepdims=True) + EPS)
    xn = cen * inv
    gain = gain_ref[...]
    normed = (xn * gain).astype(BF16)
    normed_ref[...] = normed
    qkv_scr[...] = jnp.dot(normed, wqkv_ref[...], preferred_element_type=F32).astype(BF16)
    gctx_scr[...] = lax.dot_general(
        gy_ref[...], wout_ref[...], NT, preferred_element_type=F32).astype(BF16)
    lane = lax.broadcasted_iota(jnp.int32, (1, pair_w), 1)
    low = lane < HEAD_DIM
    for pair in range(width // pair_w):
        cols = pl.ds(pair * pair_w, pair_w)
        q2 = qkv_scr[:, pl.ds(pair * pair_w, pair_w)]
        k2 = qkv_scr[:, pl.ds(width + pair * pair_w, pair_w)]
        v2 = qkv_scr[:, pl.ds(2 * width + pair * pair_w, pair_w)]
        g2 = gctx_scr[:, cols]
        outs = []
        for half in range(2):
            mine = low if half == 0 else jnp.logical_not(low)
            qh = jnp.where(mine, q2, jnp.zeros_like(q2))
            gh = jnp.where(mine, g2, jnp.zeros_like(g2))
            s = lax.dot_general(qh, k2, NT, preferred_element_type=F32) * scale
            s = s + bias_ref[2 * pair + half]
            m = jnp.max(s, axis=-1, keepdims=True)
            e = jnp.exp(s - m)
            p = e / jnp.sum(e, axis=-1, keepdims=True)
            pb = p.astype(BF16)
            ctx = jnp.dot(pb, v2, preferred_element_type=F32)
            dp = lax.dot_general(gh, v2, NT, preferred_element_type=F32).astype(BF16).astype(F32)
            rd = jnp.sum(dp * p, axis=-1, keepdims=True)
            ds = (p * (dp - rd) * scale).astype(BF16)
            dq = jnp.dot(ds, k2, preferred_element_type=F32)
            dk = lax.dot_general(ds, q2, TN, preferred_element_type=F32)
            dv = lax.dot_general(pb, g2, TN, preferred_element_type=F32)
            outs.append((ctx, dq, dk, dv))
        lo, hi = outs
        ctx_ref[:, cols] = jnp.where(low, lo[0], hi[0]).astype(BF16)
        rows_ref[:, pl.ds(pair * pair_w, pair_w)] = jnp.where(low, lo[1], hi[1]).astype(BF16)
        rows_ref[:, pl.ds(width + pair * pair_w, pair_w)] = jnp.where(low, lo[2], hi[2]).astype(BF16)
        rows_ref[:, pl.ds(2 * width + pair * pair_w, pair_w)] = jnp.where(low, lo[3], hi[3]).astype(BF16)
    gn = lax.dot_general(rows_ref[...], wqkv_ref[...], NT, preferred_element_type=F32)
    x = x_ref[...].astype(F32)
    mean = jnp.mean(x, axis=-1, keepdims=True)
    cen = x - mean
    inv = lax.rsqrt(jnp.mean(cen * cen, axis=-1, keepdims=True) + EPS)
    xn = cen * inv
    pgain_ref[...] = jnp.sum(gn * xn, axis=0, keepdims=True)
    gh = gn * gain_ref[...]
    gin = gy_ref[...].astype(F32) + inv * (
        gh
        - jnp.mean(gh, axis=-1, keepdims=True)
        - xn * jnp.mean(gh * xn, axis=-1, keepdims=True)
    )
    gin_ref[...] = gin.astype(BF16)


def layer_backward(layer_x, grad_y, gain_row, qkv_weight, out_weight, bias):
    seq_len, width_model = layer_x.shape
    qkv_cols = qkv_weight.shape[1]
    ctx_cols = out_weight.shape[0]
    flops = 2 * seq_len * width_model * (2 * qkv_cols + ctx_cols) + 12 * 2 * seq_len * seq_len * ctx_cols
    return pl.pallas_call(
        layer_kernel,
        out_shape=(
            jax.ShapeDtypeStruct((seq_len, width_model), BF16),
            jax.ShapeDtypeStruct((seq_len, width_model), BF16),
            jax.ShapeDtypeStruct((seq_len, qkv_cols), BF16),
            jax.ShapeDtypeStruct((seq_len, ctx_cols), BF16),
            jax.ShapeDtypeStruct((1, width_model), F32),
        ),
        scratch_shapes=[
            pltpu.VMEM((seq_len, qkv_cols), BF16),
            pltpu.VMEM((seq_len, ctx_cols), BF16),
        ],
        cost_estimate=pl.CostEstimate(
            flops=flops, transcendentals=bias.size, bytes_accessed=12 * 1024 * 1024),
    )(layer_x, grad_y, gain_row, qkv_weight, out_weight, bias)


def on_device(
    segment_inputs, cotangent, order, norm_gain, w_qkv, w_out, global_blocks, random_blocks
):
    segments = lax.axis_size("segment")
    my_segment = lax.axis_index("segment")
    layer_in = segment_inputs[0]
    micro_count = layer_in.shape[0]
    seq_len = layer_in.shape[1]
    width_model = layer_in.shape[2]
    gain_row = norm_gain[0][None, :]
    qkv_weight = w_qkv[0]
    out_weight = w_out[0]
    slot_order = order[0]
    block_total = seq_len // BLOCK
    block_index, usable = block_ids(global_blocks[0], random_blocks[0], block_total)
    bias = dense_bias(block_index, usable, block_total, seq_len)
    dp_size = lax.axis_size("z") * lax.axis_size("y") * lax.axis_size("core")
    grad_scale = 1.0 / math.sqrt(dp_size * micro_count * seq_len)
    qkv_cols = qkv_weight.shape[1]
    ctx_cols = out_weight.shape[0]

    grad_x = jnp.zeros((micro_count + 1, seq_len, width_model), BF16)
    normed_buf = jnp.zeros((micro_count + 1, seq_len, width_model), BF16)
    rows_buf = jnp.zeros((micro_count + 1, seq_len, qkv_cols), BF16)
    ctx_buf = jnp.zeros((micro_count + 1, seq_len, ctx_cols), BF16)
    upper_buf = jnp.zeros((micro_count + 1, seq_len, width_model), BF16)
    gain_total = jnp.zeros((1, width_model), F32)
    received = jnp.zeros(layer_in.shape[1:], BF16)
    last_tick = micro_count + segments - 1
    for timestep in range(last_tick):
        slot_now = timestep - (segments - 1) + my_segment
        active = (slot_now >= 0) & (slot_now < micro_count)
        slot_clip = jnp.clip(slot_now, 0, micro_count - 1)
        batch_id = slot_order[slot_clip]
        write_id = jnp.where(active, batch_id, jnp.int32(micro_count))
        from_output = lax.dynamic_index_in_dim(cotangent, slot_clip, 0, keepdims=False)
        incoming = jnp.where(my_segment == segments - 1, from_output, received)
        layer_x = lax.dynamic_index_in_dim(layer_in, batch_id, 0, keepdims=False)
        grad_in, normed, grad_rows, context, part_gain = layer_backward(
            layer_x, incoming, gain_row, qkv_weight, out_weight, bias
        )
        grad_x = lax.dynamic_update_index_in_dim(grad_x, grad_in, write_id, 0)
        gain_total = gain_total + jnp.where(active, part_gain, jnp.zeros_like(part_gain))
        normed_buf = lax.dynamic_update_index_in_dim(normed_buf, normed, write_id, 0)
        rows_buf = lax.dynamic_update_index_in_dim(rows_buf, grad_rows, write_id, 0)
        ctx_buf = lax.dynamic_update_index_in_dim(ctx_buf, context, write_id, 0)
        upper_buf = lax.dynamic_update_index_in_dim(upper_buf, incoming, write_id, 0)
        if timestep + 1 < last_tick:
            received = from_behind(grad_in, "segment", -1)
    all_normed = normed_buf[:micro_count].reshape(micro_count * seq_len, width_model)
    all_rows = rows_buf[:micro_count].reshape(micro_count * seq_len, qkv_cols)
    all_ctx = ctx_buf[:micro_count].reshape(micro_count * seq_len, ctx_cols)
    all_upper = upper_buf[:micro_count].reshape(micro_count * seq_len, width_model)
    sum_qkv = lax.dot_general(all_normed, all_rows, TN, preferred_element_type=F32)
    sum_out = lax.dot_general(all_ctx, all_upper, TN, preferred_element_type=F32)
    rows_total = qkv_weight.shape[0]
    fold = rows_total // ctx_cols
    out_folded = sum_out.reshape(rows_total, ctx_cols * width_model // rows_total)
    gain_col = gain_total.reshape(rows_total, width_model // rows_total)
    pad = jnp.zeros((rows_total, 128 - gain_col.shape[1]), BF16)
    packed = jnp.concatenate(
        [(sum_qkv * grad_scale).astype(BF16), (out_folded * grad_scale).astype(BF16),
         (gain_col * grad_scale).astype(BF16), pad], axis=1)
    share = dp_reduce_scatter(packed)
    share_rows = share.shape[0]
    qkv_share = share[:, :qkv_cols]
    out_share = share[:, qkv_cols:qkv_cols + out_folded.shape[1]].reshape(share_rows // fold, width_model)
    gain_share = share[:, qkv_cols + out_folded.shape[1]:qkv_cols + out_folded.shape[1] + gain_col.shape[1]].reshape(-1)
    return (grad_x[:micro_count][None], qkv_share[None], out_share[None], gain_share[None])


def solution(mesh):
    dp = ("z", "y", "core")
    segs = mesh.shape["segment"]
    cores = 2
    ys = 4
    zs = mesh.shape["dp"] // (cores * ys)
    mesh4 = Mesh(mesh.devices.reshape(segs, zs, ys, cores), ("segment", "z", "y", "core"))
    in_specs = (
        P("segment", dp, None, None),
        P(dp, None, None),
        P(dp, None),
        P("segment", None),
        P("segment", None, None),
        P("segment", None, None),
        P("segment", None),
        P("segment", None, None, None),
    )
    out_specs = (
        P("segment", dp, None, None),
        P("segment", dp, None),
        P("segment", dp, None),
        P("segment", dp),
    )
    return jax.shard_map(
        on_device, mesh=mesh4, in_specs=in_specs, out_specs=out_specs, check_vma=False
    )
```

```python
import math

import jax
import jax.numpy as jnp
from jax import lax
from jax.experimental import pallas as pl
from jax.experimental.pallas import tpu as pltpu
from jax.sharding import Mesh, PartitionSpec as P

BLOCK = 64
HEAD_DIM = 64
EPS = 1e-05
F32 = jnp.float32
BF16 = jnp.bfloat16
NT = (((1,), (1,)), ((), ()))
TN = (((0,), (0,)), ((), ()))


def from_behind(value, axis, by):
    count = lax.axis_size(axis)
    pairs = [(i, i + by) for i in range(count) if 0 <= i + by < count]
    return lax.ppermute(value, axis, pairs)


def block_ids(glob_ids, rand_ids, block_count):
    head_count = rand_ids.shape[0]
    block_rows = jnp.arange(block_count, dtype=jnp.int32)
    window = block_rows[:, None] + jnp.arange(-1, 2, dtype=jnp.int32)[None, :]
    inside = (window >= 0) & (window < block_count)
    window_ids = jnp.where(inside, window, jnp.int32(-1))
    global_ids = jnp.broadcast_to(glob_ids[None, :], (block_count, glob_ids.shape[0]))
    fixed_ids = jnp.concatenate([window_ids, global_ids], axis=1)
    fixed_ids = jnp.broadcast_to(fixed_ids[None], (head_count, block_count, fixed_ids.shape[1]))
    listed_blocks = jnp.concatenate([fixed_ids, rand_ids], axis=2)
    list_len = listed_blocks.shape[2]
    earlier = (
        jnp.arange(list_len, dtype=jnp.int32)[:, None]
        > jnp.arange(list_len, dtype=jnp.int32)[None, :]
    )
    equal_prior = (listed_blocks[..., :, None] == listed_blocks[..., None, :]) & earlier
    repeated = jnp.any(equal_prior, axis=-1)
    usable = (listed_blocks >= 0) & jnp.logical_not(repeated)
    block_index = jnp.clip(listed_blocks, 0, block_count - 1)
    return (block_index, usable)


def halving(cur, steps):
    for axis, dim, bit in steps:
        n = lax.axis_size(axis)
        half = cur.shape[dim] // 2
        mybit = (lax.axis_index(axis) // bit) % 2
        keep = lax.dynamic_slice_in_dim(cur, mybit * half, half, axis=dim)
        send = lax.dynamic_slice_in_dim(cur, (1 - mybit) * half, half, axis=dim)
        recv = lax.ppermute(send.astype(BF16), axis, [(i, i ^ bit) for i in range(n)])
        cur = keep.astype(F32) + recv.astype(F32)
    return cur


def dp_reduce_scatter(packed):
    cores = lax.axis_size("core")
    ys = lax.axis_size("y")
    zs = lax.axis_size("z")
    rows, cols = packed.shape
    chunk = rows // (zs * ys * cores)
    v = packed.reshape(zs, ys, cores, chunk, cols)
    v = halving(v, [("core", 2, 1)])
    z_steps = [("z", 0, zs // 2 ** (k + 1)) for k in range(int(math.log2(zs)))]
    y_steps = [("y", 1, ys // 2 ** (k + 1)) for k in range(int(math.log2(ys)))]
    split = 1024
    a = halving(v[..., :split], z_steps + y_steps)
    b = halving(v[..., split:], y_steps + z_steps)
    return jnp.concatenate([a.reshape(chunk, split), b.reshape(chunk, cols - split)], axis=-1)


def dense_bias(block_index, usable, block_count, seq_len):
    names = block_index[..., None] == jnp.arange(block_count, dtype=jnp.int32)
    allowed = jnp.any(names & usable[..., None], axis=2)
    small = jnp.where(allowed, F32(0.0), F32(-1e30))
    extent = seq_len // block_count
    return jnp.repeat(jnp.repeat(small, extent, axis=1), extent, axis=2)


def layer_kernel(x_ref, gy_ref, gain_ref, wqkv_ref, wout_ref, bias_ref,
                 gin_ref, normed_ref, rows_ref, ctx_ref, pgain_ref, qkv_scr, gctx_scr):
    width = ctx_ref.shape[1]
    pair_w = 2 * HEAD_DIM
    scale = 1.0 / math.sqrt(HEAD_DIM)
    x = x_ref[...].astype(F32)
    mean = jnp.mean(x, axis=-1, keepdims=True)
    cen = x - mean
    inv = lax.rsqrt(jnp.mean(cen * cen, axis=-1, keepdims=True) + EPS)
    xn = cen * inv
    gain = gain_ref[...]
    normed = (xn * gain).astype(BF16)
    normed_ref[...] = normed
    qkv_scr[...] = jnp.dot(normed, wqkv_ref[...], preferred_element_type=F32).astype(BF16)
    gctx_scr[...] = lax.dot_general(
        gy_ref[...], wout_ref[...], NT, preferred_element_type=F32).astype(BF16)
    lane = lax.broadcasted_iota(jnp.int32, (1, pair_w), 1)
    low = lane < HEAD_DIM
    for pair in range(width // pair_w):
        cols = pl.ds(pair * pair_w, pair_w)
        q2 = qkv_scr[:, pl.ds(pair * pair_w, pair_w)]
        k2 = qkv_scr[:, pl.ds(width + pair * pair_w, pair_w)]
        v2 = qkv_scr[:, pl.ds(2 * width + pair * pair_w, pair_w)]
        g2 = gctx_scr[:, cols]
        outs = []
        for half in range(2):
            mine = low if half == 0 else jnp.logical_not(low)
            qh = jnp.where(mine, q2, jnp.zeros_like(q2))
            gh = jnp.where(mine, g2, jnp.zeros_like(g2))
            s = lax.dot_general(qh, k2, NT, preferred_element_type=F32) * scale
            s = s + bias_ref[2 * pair + half]
            m = jnp.max(s, axis=-1, keepdims=True)
            e = jnp.exp(s - m)
            p = e / jnp.sum(e, axis=-1, keepdims=True)
            pb = p.astype(BF16)
            ctx = jnp.dot(pb, v2, preferred_element_type=F32)
            dp = lax.dot_general(gh, v2, NT, preferred_element_type=F32).astype(BF16).astype(F32)
            rd = jnp.sum(dp * p, axis=-1, keepdims=True)
            ds = (p * (dp - rd) * scale).astype(BF16)
            dq = jnp.dot(ds, k2, preferred_element_type=F32)
            dk = lax.dot_general(ds, q2, TN, preferred_element_type=F32)
            dv = lax.dot_general(pb, g2, TN, preferred_element_type=F32)
            outs.append((ctx, dq, dk, dv))
        lo, hi = outs
        ctx_ref[:, cols] = jnp.where(low, lo[0], hi[0]).astype(BF16)
        rows_ref[:, pl.ds(pair * pair_w, pair_w)] = jnp.where(low, lo[1], hi[1]).astype(BF16)
        rows_ref[:, pl.ds(width + pair * pair_w, pair_w)] = jnp.where(low, lo[2], hi[2]).astype(BF16)
        rows_ref[:, pl.ds(2 * width + pair * pair_w, pair_w)] = jnp.where(low, lo[3], hi[3]).astype(BF16)
    gn = lax.dot_general(rows_ref[...], wqkv_ref[...], NT, preferred_element_type=F32)
    x = x_ref[...].astype(F32)
    mean = jnp.mean(x, axis=-1, keepdims=True)
    cen = x - mean
    inv = lax.rsqrt(jnp.mean(cen * cen, axis=-1, keepdims=True) + EPS)
    xn = cen * inv
    pgain_ref[...] = jnp.sum(gn * xn, axis=0, keepdims=True)
    gh = gn * gain_ref[...]
    gin = gy_ref[...].astype(F32) + inv * (
        gh
        - jnp.mean(gh, axis=-1, keepdims=True)
        - xn * jnp.mean(gh * xn, axis=-1, keepdims=True)
    )
    gin_ref[...] = gin.astype(BF16)


def layer_backward(layer_x, grad_y, gain_row, qkv_weight, out_weight, bias):
    seq_len, width_model = layer_x.shape
    qkv_cols = qkv_weight.shape[1]
    ctx_cols = out_weight.shape[0]
    flops = 2 * seq_len * width_model * (2 * qkv_cols + ctx_cols) + 12 * 2 * seq_len * seq_len * ctx_cols
    return pl.pallas_call(
        layer_kernel,
        out_shape=(
            jax.ShapeDtypeStruct((seq_len, width_model), BF16),
            jax.ShapeDtypeStruct((seq_len, width_model), BF16),
            jax.ShapeDtypeStruct((seq_len, qkv_cols), BF16),
            jax.ShapeDtypeStruct((seq_len, ctx_cols), BF16),
            jax.ShapeDtypeStruct((1, width_model), F32),
        ),
        scratch_shapes=[
            pltpu.VMEM((seq_len, qkv_cols), BF16),
            pltpu.VMEM((seq_len, ctx_cols), BF16),
        ],
        cost_estimate=pl.CostEstimate(
            flops=flops, transcendentals=bias.size, bytes_accessed=12 * 1024 * 1024),
    )(layer_x, grad_y, gain_row, qkv_weight, out_weight, bias)


def on_device(
    segment_inputs, cotangent, order, norm_gain, w_qkv, w_out, global_blocks, random_blocks
):
    segments = lax.axis_size("segment")
    my_segment = lax.axis_index("segment")
    layer_in = segment_inputs[0]
    micro_count = layer_in.shape[0]
    seq_len = layer_in.shape[1]
    width_model = layer_in.shape[2]
    gain_row = norm_gain[0][None, :]
    qkv_weight = w_qkv[0]
    out_weight = w_out[0]
    slot_order = order[0]
    block_total = seq_len // BLOCK
    block_index, usable = block_ids(global_blocks[0], random_blocks[0], block_total)
    bias = dense_bias(block_index, usable, block_total, seq_len)
    dp_size = lax.axis_size("z") * lax.axis_size("y") * lax.axis_size("core")
    grad_scale = 1.0 / math.sqrt(dp_size * micro_count * seq_len)
    qkv_cols = qkv_weight.shape[1]
    ctx_cols = out_weight.shape[0]

    grad_x = jnp.zeros((micro_count + 1, seq_len, width_model), BF16)
    normed_buf = jnp.zeros((micro_count + 1, seq_len, width_model), BF16)
    rows_buf = jnp.zeros((micro_count + 1, seq_len, qkv_cols), BF16)
    ctx_buf = jnp.zeros((micro_count + 1, seq_len, ctx_cols), BF16)
    upper_buf = jnp.zeros((micro_count + 1, seq_len, width_model), BF16)
    gain_total = jnp.zeros((1, width_model), F32)
    received = jnp.zeros(layer_in.shape[1:], BF16)
    last_tick = micro_count + segments - 1
    for timestep in range(last_tick):
        slot_now = timestep - (segments - 1) + my_segment
        active = (slot_now >= 0) & (slot_now < micro_count)
        slot_clip = jnp.clip(slot_now, 0, micro_count - 1)
        batch_id = slot_order[slot_clip]
        write_id = jnp.where(active, batch_id, jnp.int32(micro_count))
        from_output = lax.dynamic_index_in_dim(cotangent, slot_clip, 0, keepdims=False)
        incoming = jnp.where(my_segment == segments - 1, from_output, received)
        layer_x = lax.dynamic_index_in_dim(layer_in, batch_id, 0, keepdims=False)
        grad_in, normed, grad_rows, context, part_gain = layer_backward(
            layer_x, incoming, gain_row, qkv_weight, out_weight, bias
        )
        grad_x = lax.dynamic_update_index_in_dim(grad_x, grad_in, write_id, 0)
        gain_total = gain_total + jnp.where(active, part_gain, jnp.zeros_like(part_gain))
        normed_buf = lax.dynamic_update_index_in_dim(normed_buf, normed, write_id, 0)
        rows_buf = lax.dynamic_update_index_in_dim(rows_buf, grad_rows, write_id, 0)
        ctx_buf = lax.dynamic_update_index_in_dim(ctx_buf, context, write_id, 0)
        upper_buf = lax.dynamic_update_index_in_dim(upper_buf, incoming, write_id, 0)
        if timestep + 1 < last_tick:
            received = from_behind(grad_in, "segment", -1)
    all_normed = normed_buf[:micro_count].reshape(micro_count * seq_len, width_model)
    all_rows = rows_buf[:micro_count].reshape(micro_count * seq_len, qkv_cols)
    all_ctx = ctx_buf[:micro_count].reshape(micro_count * seq_len, ctx_cols)
    all_upper = upper_buf[:micro_count].reshape(micro_count * seq_len, width_model)
    sum_qkv = lax.dot_general(all_normed, all_rows, TN, preferred_element_type=F32)
    sum_out = lax.dot_general(all_ctx, all_upper, TN, preferred_element_type=F32)
    rows_total = qkv_weight.shape[0]
    fold = rows_total // ctx_cols
    out_folded = sum_out.reshape(rows_total, ctx_cols * width_model // rows_total)
    gain_col = gain_total.reshape(rows_total, width_model // rows_total)
    pad = jnp.zeros((rows_total, 128 - gain_col.shape[1]), BF16)
    packed = jnp.concatenate(
        [(sum_qkv * grad_scale).astype(BF16), (out_folded * grad_scale).astype(BF16),
         (gain_col * grad_scale).astype(BF16), pad], axis=1)
    share = dp_reduce_scatter(packed)
    share_rows = share.shape[0]
    qkv_share = share[:, :qkv_cols]
    out_share = share[:, qkv_cols:qkv_cols + out_folded.shape[1]].reshape(share_rows // fold, width_model)
    gain_share = share[:, qkv_cols + out_folded.shape[1]:qkv_cols + out_folded.shape[1] + gain_col.shape[1]].reshape(-1)
    return (grad_x[:micro_count][None], qkv_share[None], out_share[None], gain_share[None])


def solution(mesh):
    dp = ("z", "y", "core")
    segs = mesh.shape["segment"]
    cores = 2
    ys = 4
    zs = mesh.shape["dp"] // (cores * ys)
    mesh4 = Mesh(mesh.devices.reshape(segs, zs, ys, cores), ("segment", "z", "y", "core"))
    in_specs = (
        P("segment", dp, None, None),
        P(dp, None, None),
        P(dp, None),
        P("segment", None),
        P("segment", None, None),
        P("segment", None, None),
        P("segment", None),
        P("segment", None, None, None),
    )
    out_specs = (
        P("segment", dp, None, None),
        P("segment", dp, None),
        P("segment", dp, None),
        P("segment", dp),
    )
    return jax.shard_map(
        on_device, mesh=mesh4, in_specs=in_specs, out_specs=out_specs, check_vma=False
    )
```

```python
import math

import jax
import jax.numpy as jnp
from jax import lax
from jax.experimental import pallas as pl
from jax.experimental.pallas import tpu as pltpu
from jax.sharding import Mesh, PartitionSpec as P

BLOCK = 64
HEAD_DIM = 64
EPS = 1e-05
F32 = jnp.float32
BF16 = jnp.bfloat16
NT = (((1,), (1,)), ((), ()))
TN = (((0,), (0,)), ((), ()))


def from_behind(value, axis, by):
    count = lax.axis_size(axis)
    pairs = [(i, i + by) for i in range(count) if 0 <= i + by < count]
    return lax.ppermute(value, axis, pairs)


def block_ids(glob_ids, rand_ids, block_count):
    head_count = rand_ids.shape[0]
    block_rows = jnp.arange(block_count, dtype=jnp.int32)
    window = block_rows[:, None] + jnp.arange(-1, 2, dtype=jnp.int32)[None, :]
    inside = (window >= 0) & (window < block_count)
    window_ids = jnp.where(inside, window, jnp.int32(-1))
    global_ids = jnp.broadcast_to(glob_ids[None, :], (block_count, glob_ids.shape[0]))
    fixed_ids = jnp.concatenate([window_ids, global_ids], axis=1)
    fixed_ids = jnp.broadcast_to(fixed_ids[None], (head_count, block_count, fixed_ids.shape[1]))
    listed_blocks = jnp.concatenate([fixed_ids, rand_ids], axis=2)
    list_len = listed_blocks.shape[2]
    earlier = (
        jnp.arange(list_len, dtype=jnp.int32)[:, None]
        > jnp.arange(list_len, dtype=jnp.int32)[None, :]
    )
    equal_prior = (listed_blocks[..., :, None] == listed_blocks[..., None, :]) & earlier
    repeated = jnp.any(equal_prior, axis=-1)
    usable = (listed_blocks >= 0) & jnp.logical_not(repeated)
    block_index = jnp.clip(listed_blocks, 0, block_count - 1)
    return (block_index, usable)


def halving(cur, steps):
    for axis, dim, bit in steps:
        n = lax.axis_size(axis)
        half = cur.shape[dim] // 2
        mybit = (lax.axis_index(axis) // bit) % 2
        keep = lax.dynamic_slice_in_dim(cur, mybit * half, half, axis=dim)
        send = lax.dynamic_slice_in_dim(cur, (1 - mybit) * half, half, axis=dim)
        recv = lax.ppermute(send.astype(BF16), axis, [(i, i ^ bit) for i in range(n)])
        cur = keep.astype(F32) + recv.astype(F32)
    return cur


def dp_reduce_scatter(packed):
    cores = lax.axis_size("core")
    ys = lax.axis_size("y")
    zs = lax.axis_size("z")
    rows, cols = packed.shape
    chunk = rows // (zs * ys * cores)
    v = packed.reshape(zs, ys, cores, chunk, cols)
    v = halving(v, [("core", 2, 1)])
    z_steps = [("z", 0, zs // 2 ** (k + 1)) for k in range(int(math.log2(zs)))]
    y_steps = [("y", 1, ys // 2 ** (k + 1)) for k in range(int(math.log2(ys)))]
    split = 1024
    a = halving(v[..., :split], z_steps + y_steps)
    b = halving(v[..., split:], y_steps + z_steps)
    return jnp.concatenate([a.reshape(chunk, split), b.reshape(chunk, cols - split)], axis=-1)


def dense_bias(block_index, usable, block_count, seq_len):
    names = block_index[..., None] == jnp.arange(block_count, dtype=jnp.int32)
    allowed = jnp.any(names & usable[..., None], axis=2)
    small = jnp.where(allowed, F32(0.0), F32(-1e30))
    extent = seq_len // block_count
    return jnp.repeat(jnp.repeat(small, extent, axis=1), extent, axis=2)


def layer_kernel(sc_ref, x_ref, cot_ref, recv_ref, gain_ref, wqkv_ref, wout_ref, bias_ref,
                 gx_in, nb_in, rb_in, cb_in, ub_in,
                 gin_ref, gx_ref, normed_ref, rows_ref, ctx_ref, upper_ref, pgain_ref,
                 qkv_scr, gctx_scr):
    del gx_in, nb_in, rb_in, cb_in, ub_in
    width = ctx_ref.shape[1]
    gy = jnp.where(sc_ref[3] > 0, cot_ref[...], recv_ref[...])
    upper_ref[...] = gy
    pair_w = 2 * HEAD_DIM
    scale = 1.0 / math.sqrt(HEAD_DIM)
    x = x_ref[...].astype(F32)
    mean = jnp.mean(x, axis=-1, keepdims=True)
    cen = x - mean
    inv = lax.rsqrt(jnp.mean(cen * cen, axis=-1, keepdims=True) + EPS)
    xn = cen * inv
    gain = gain_ref[...]
    normed = (xn * gain).astype(BF16)
    normed_ref[...] = normed
    qkv_scr[...] = jnp.dot(normed, wqkv_ref[...], preferred_element_type=F32).astype(BF16)
    gctx_scr[...] = lax.dot_general(
        gy, wout_ref[...], NT, preferred_element_type=F32).astype(BF16)
    lane = lax.broadcasted_iota(jnp.int32, (1, pair_w), 1)
    low = lane < HEAD_DIM
    for pair in range(width // pair_w):
        cols = pl.ds(pair * pair_w, pair_w)
        q2 = qkv_scr[:, pl.ds(pair * pair_w, pair_w)]
        k2 = qkv_scr[:, pl.ds(width + pair * pair_w, pair_w)]
        v2 = qkv_scr[:, pl.ds(2 * width + pair * pair_w, pair_w)]
        g2 = gctx_scr[:, cols]
        outs = []
        for half in range(2):
            mine = low if half == 0 else jnp.logical_not(low)
            qh = jnp.where(mine, q2, jnp.zeros_like(q2))
            gh = jnp.where(mine, g2, jnp.zeros_like(g2))
            s = lax.dot_general(qh, k2, NT, preferred_element_type=F32) * scale
            s = s + bias_ref[2 * pair + half]
            m = jnp.max(s, axis=-1, keepdims=True)
            e = jnp.exp(s - m)
            p = e / jnp.sum(e, axis=-1, keepdims=True)
            pb = p.astype(BF16)
            ctx = jnp.dot(pb, v2, preferred_element_type=F32)
            dp = lax.dot_general(gh, v2, NT, preferred_element_type=F32).astype(BF16).astype(F32)
            rd = jnp.sum(dp * p, axis=-1, keepdims=True)
            ds = (p * (dp - rd) * scale).astype(BF16)
            dq = jnp.dot(ds, k2, preferred_element_type=F32)
            dk = lax.dot_general(ds, q2, TN, preferred_element_type=F32)
            dv = lax.dot_general(pb, g2, TN, preferred_element_type=F32)
            outs.append((ctx, dq, dk, dv))
        lo, hi = outs
        ctx_ref[:, cols] = jnp.where(low, lo[0], hi[0]).astype(BF16)
        rows_ref[:, pl.ds(pair * pair_w, pair_w)] = jnp.where(low, lo[1], hi[1]).astype(BF16)
        rows_ref[:, pl.ds(width + pair * pair_w, pair_w)] = jnp.where(low, lo[2], hi[2]).astype(BF16)
        rows_ref[:, pl.ds(2 * width + pair * pair_w, pair_w)] = jnp.where(low, lo[3], hi[3]).astype(BF16)
    gn = lax.dot_general(rows_ref[...], wqkv_ref[...], NT, preferred_element_type=F32)
    x = x_ref[...].astype(F32)
    mean = jnp.mean(x, axis=-1, keepdims=True)
    cen = x - mean
    inv = lax.rsqrt(jnp.mean(cen * cen, axis=-1, keepdims=True) + EPS)
    xn = cen * inv
    pgain_ref[...] = jnp.sum(gn * xn, axis=0, keepdims=True)
    gh = gn * gain_ref[...]
    gin = upper_ref[...].astype(F32) + inv * (
        gh
        - jnp.mean(gh, axis=-1, keepdims=True)
        - xn * jnp.mean(gh * xn, axis=-1, keepdims=True)
    )
    gin = gin.astype(BF16)
    gin_ref[...] = gin
    gx_ref[...] = gin


def layer_backward(sc, layer_in, cotangent, received, gain_row, qkv_weight, out_weight, bias, bufs):
    micro, seq_len, width_model = layer_in.shape
    qkv_cols = qkv_weight.shape[1]
    ctx_cols = out_weight.shape[0]
    flops = 2 * seq_len * width_model * (2 * qkv_cols + ctx_cols) + 12 * 2 * seq_len * seq_len * ctx_cols
    full = lambda shape: pl.BlockSpec(shape, lambda i, sc: (0,) * len(shape))
    slot_of = lambda k, cols: pl.BlockSpec((None, seq_len, cols), lambda i, sc: (sc[k], 0, 0))
    anyspec = pl.BlockSpec(memory_space=pl.ANY)
    grid_spec = pltpu.PrefetchScalarGridSpec(
        num_scalar_prefetch=1,
        grid=(1,),
        in_specs=[
            slot_of(1, width_model),
            slot_of(2, width_model),
            full((seq_len, width_model)),
            full((1, width_model)),
            full(qkv_weight.shape),
            full(out_weight.shape),
            full(bias.shape),
            anyspec, anyspec, anyspec, anyspec, anyspec,
        ],
        out_specs=[
            full((seq_len, width_model)),
            slot_of(0, width_model),
            slot_of(0, width_model),
            slot_of(0, qkv_cols),
            slot_of(0, ctx_cols),
            slot_of(0, width_model),
            full((1, width_model)),
        ],
        scratch_shapes=[
            pltpu.VMEM((seq_len, qkv_cols), BF16),
            pltpu.VMEM((seq_len, ctx_cols), BF16),
        ],
    )
    return pl.pallas_call(
        layer_kernel,
        grid_spec=grid_spec,
        out_shape=(
            jax.ShapeDtypeStruct((seq_len, width_model), BF16),
            *[jax.ShapeDtypeStruct(b.shape, b.dtype) for b in bufs],
            jax.ShapeDtypeStruct((1, width_model), F32),
        ),
        input_output_aliases={8: 1, 9: 2, 10: 3, 11: 4, 12: 5},
        cost_estimate=pl.CostEstimate(
            flops=flops, transcendentals=bias.size, bytes_accessed=12 * 1024 * 1024),
    )(sc, layer_in, cotangent, received, gain_row, qkv_weight, out_weight, bias, *bufs)


def on_device(
    segment_inputs, cotangent, order, norm_gain, w_qkv, w_out, global_blocks, random_blocks
):
    segments = lax.axis_size("segment")
    my_segment = lax.axis_index("segment")
    layer_in = segment_inputs[0]
    micro_count = layer_in.shape[0]
    seq_len = layer_in.shape[1]
    width_model = layer_in.shape[2]
    gain_row = norm_gain[0][None, :]
    qkv_weight = w_qkv[0]
    out_weight = w_out[0]
    slot_order = order[0]
    block_total = seq_len // BLOCK
    block_index, usable = block_ids(global_blocks[0], random_blocks[0], block_total)
    bias = dense_bias(block_index, usable, block_total, seq_len)
    dp_size = lax.axis_size("z") * lax.axis_size("y") * lax.axis_size("core")
    grad_scale = 1.0 / math.sqrt(dp_size * micro_count * seq_len)
    qkv_cols = qkv_weight.shape[1]
    ctx_cols = out_weight.shape[0]

    grad_x = jnp.zeros((micro_count + 1, seq_len, width_model), BF16)
    normed_buf = jnp.zeros((micro_count + 1, seq_len, width_model), BF16)
    rows_buf = jnp.zeros((micro_count + 1, seq_len, qkv_cols), BF16)
    ctx_buf = jnp.zeros((micro_count + 1, seq_len, ctx_cols), BF16)
    upper_buf = jnp.zeros((micro_count + 1, seq_len, width_model), BF16)
    gain_total = jnp.zeros((1, width_model), F32)
    received = jnp.zeros(layer_in.shape[1:], BF16)
    last_tick = micro_count + segments - 1
    use_cot = (my_segment == segments - 1).astype(jnp.int32)
    for timestep in range(last_tick):
        slot_now = timestep - (segments - 1) + my_segment
        active = (slot_now >= 0) & (slot_now < micro_count)
        slot_clip = jnp.clip(slot_now, 0, micro_count - 1)
        batch_id = slot_order[slot_clip]
        write_id = jnp.where(active, batch_id, jnp.int32(micro_count))
        sc = jnp.stack([write_id, batch_id, slot_clip, use_cot]).astype(jnp.int32)
        grad_in, grad_x, normed_buf, rows_buf, ctx_buf, upper_buf, part_gain = layer_backward(
            sc, layer_in, cotangent, received, gain_row, qkv_weight, out_weight, bias,
            (grad_x, normed_buf, rows_buf, ctx_buf, upper_buf),
        )
        gain_total = gain_total + jnp.where(active, part_gain, jnp.zeros_like(part_gain))
        if timestep + 1 < last_tick:
            received = from_behind(grad_in, "segment", -1)
    all_normed = normed_buf[:micro_count].reshape(micro_count * seq_len, width_model)
    all_rows = rows_buf[:micro_count].reshape(micro_count * seq_len, qkv_cols)
    all_ctx = ctx_buf[:micro_count].reshape(micro_count * seq_len, ctx_cols)
    all_upper = upper_buf[:micro_count].reshape(micro_count * seq_len, width_model)
    sum_qkv = lax.dot_general(all_normed, all_rows, TN, preferred_element_type=F32)
    sum_out = lax.dot_general(all_ctx, all_upper, TN, preferred_element_type=F32)
    rows_total = qkv_weight.shape[0]
    fold = rows_total // ctx_cols
    out_folded = sum_out.reshape(rows_total, ctx_cols * width_model // rows_total)
    gain_col = gain_total.reshape(rows_total, width_model // rows_total)
    pad = jnp.zeros((rows_total, 128 - gain_col.shape[1]), BF16)
    packed = jnp.concatenate(
        [(sum_qkv * grad_scale).astype(BF16), (out_folded * grad_scale).astype(BF16),
         (gain_col * grad_scale).astype(BF16), pad], axis=1)
    share = dp_reduce_scatter(packed)
    share_rows = share.shape[0]
    qkv_share = share[:, :qkv_cols]
    out_share = share[:, qkv_cols:qkv_cols + out_folded.shape[1]].reshape(share_rows // fold, width_model)
    gain_share = share[:, qkv_cols + out_folded.shape[1]:qkv_cols + out_folded.shape[1] + gain_col.shape[1]].reshape(-1)
    return (grad_x[:micro_count][None], qkv_share[None], out_share[None], gain_share[None])


def solution(mesh):
    dp = ("z", "y", "core")
    segs = mesh.shape["segment"]
    cores = 2
    ys = 4
    zs = mesh.shape["dp"] // (cores * ys)
    mesh4 = Mesh(mesh.devices.reshape(segs, zs, ys, cores), ("segment", "z", "y", "core"))
    in_specs = (
        P("segment", dp, None, None),
        P(dp, None, None),
        P(dp, None),
        P("segment", None),
        P("segment", None, None),
        P("segment", None, None),
        P("segment", None),
        P("segment", None, None, None),
    )
    out_specs = (
        P("segment", dp, None, None),
        P("segment", dp, None),
        P("segment", dp, None),
        P("segment", dp),
    )
    return jax.shard_map(
        on_device, mesh=mesh4, in_specs=in_specs, out_specs=out_specs, check_vma=False
    )
```

```python
import math

import jax
import jax.numpy as jnp
from jax import lax
from jax.experimental import pallas as pl
from jax.experimental.pallas import tpu as pltpu
from jax.sharding import Mesh, PartitionSpec as P

BLOCK = 64
HEAD_DIM = 64
EPS = 1e-05
F32 = jnp.float32
BF16 = jnp.bfloat16
NT = (((1,), (1,)), ((), ()))
TN = (((0,), (0,)), ((), ()))


def from_behind(value, axis, by):
    count = lax.axis_size(axis)
    pairs = [(i, i + by) for i in range(count) if 0 <= i + by < count]
    return lax.ppermute(value, axis, pairs)


def block_ids(glob_ids, rand_ids, block_count):
    head_count = rand_ids.shape[0]
    block_rows = jnp.arange(block_count, dtype=jnp.int32)
    window = block_rows[:, None] + jnp.arange(-1, 2, dtype=jnp.int32)[None, :]
    inside = (window >= 0) & (window < block_count)
    window_ids = jnp.where(inside, window, jnp.int32(-1))
    global_ids = jnp.broadcast_to(glob_ids[None, :], (block_count, glob_ids.shape[0]))
    fixed_ids = jnp.concatenate([window_ids, global_ids], axis=1)
    fixed_ids = jnp.broadcast_to(fixed_ids[None], (head_count, block_count, fixed_ids.shape[1]))
    listed_blocks = jnp.concatenate([fixed_ids, rand_ids], axis=2)
    list_len = listed_blocks.shape[2]
    earlier = (
        jnp.arange(list_len, dtype=jnp.int32)[:, None]
        > jnp.arange(list_len, dtype=jnp.int32)[None, :]
    )
    equal_prior = (listed_blocks[..., :, None] == listed_blocks[..., None, :]) & earlier
    repeated = jnp.any(equal_prior, axis=-1)
    usable = (listed_blocks >= 0) & jnp.logical_not(repeated)
    block_index = jnp.clip(listed_blocks, 0, block_count - 1)
    return (block_index, usable)


def halving(cur, steps):
    for axis, dim, bit in steps:
        n = lax.axis_size(axis)
        half = cur.shape[dim] // 2
        mybit = (lax.axis_index(axis) // bit) % 2
        keep = lax.dynamic_slice_in_dim(cur, mybit * half, half, axis=dim)
        send = lax.dynamic_slice_in_dim(cur, (1 - mybit) * half, half, axis=dim)
        recv = lax.ppermute(send.astype(BF16), axis, [(i, i ^ bit) for i in range(n)])
        cur = keep.astype(F32) + recv.astype(F32)
    return cur


def dp_reduce_scatter(packed):
    cores = lax.axis_size("core")
    ys = lax.axis_size("y")
    zs = lax.axis_size("z")
    rows, cols = packed.shape
    chunk = rows // (zs * ys * cores)
    v = packed.reshape(zs, ys, cores, chunk, cols)
    v = halving(v, [("core", 2, 1)])
    z_steps = [("z", 0, zs // 2 ** (k + 1)) for k in range(int(math.log2(zs)))]
    y_steps = [("y", 1, ys // 2 ** (k + 1)) for k in range(int(math.log2(ys)))]
    split = 1024
    a = halving(v[..., :split], z_steps + y_steps)
    b = halving(v[..., split:], y_steps + z_steps)
    return jnp.concatenate([a.reshape(chunk, split), b.reshape(chunk, cols - split)], axis=-1)


def dense_bias(block_index, usable, block_count, seq_len):
    names = block_index[..., None] == jnp.arange(block_count, dtype=jnp.int32)
    allowed = jnp.any(names & usable[..., None], axis=2)
    small = jnp.where(allowed, F32(0.0), F32(-1e30))
    extent = seq_len // block_count
    return jnp.repeat(jnp.repeat(small, extent, axis=1), extent, axis=2)


def forward_kernel(sc_ref, x_ref, gain_ref, wqkv_ref, bias_ref, nb_in, cb_in,
                   qkv_ref, p_ref, normed_ref, ctx_ref):
    del sc_ref, nb_in, cb_in
    width = ctx_ref.shape[1]
    pair_w = 2 * HEAD_DIM
    scale = 1.0 / math.sqrt(HEAD_DIM)
    x = x_ref[...].astype(F32)
    mean = jnp.mean(x, axis=-1, keepdims=True)
    cen = x - mean
    inv = lax.rsqrt(jnp.mean(cen * cen, axis=-1, keepdims=True) + EPS)
    normed = (cen * inv * gain_ref[...]).astype(BF16)
    normed_ref[...] = normed
    qkv_ref[...] = jnp.dot(normed, wqkv_ref[...], preferred_element_type=F32).astype(BF16)
    lane = lax.broadcasted_iota(jnp.int32, (1, pair_w), 1)
    low = lane < HEAD_DIM
    for pair in range(width // pair_w):
        q2 = qkv_ref[:, pl.ds(pair * pair_w, pair_w)]
        k2 = qkv_ref[:, pl.ds(width + pair * pair_w, pair_w)]
        v2 = qkv_ref[:, pl.ds(2 * width + pair * pair_w, pair_w)]
        ctxs = []
        for half in range(2):
            mine = low if half == 0 else jnp.logical_not(low)
            qh = jnp.where(mine, q2, jnp.zeros_like(q2))
            s = lax.dot_general(qh, k2, NT, preferred_element_type=F32) * scale
            s = s + bias_ref[2 * pair + half]
            m = jnp.max(s, axis=-1, keepdims=True)
            e = jnp.exp(s - m)
            p = e / jnp.sum(e, axis=-1, keepdims=True)
            p_ref[2 * pair + half] = p
            ctxs.append(jnp.dot(p.astype(BF16), v2, preferred_element_type=F32))
        ctx_ref[:, pl.ds(pair * pair_w, pair_w)] = jnp.where(low, ctxs[0], ctxs[1]).astype(BF16)


def backward_kernel(sc_ref, x_ref, cot_ref, recv_ref, gain_ref, wqkv_ref, wout_ref, qkv_ref, p_ref,
                    gx_in, rb_in, ub_in,
                    gin_ref, gx_ref, rows_ref, upper_ref, pgain_ref, gctx_scr):
    del gx_in, rb_in, ub_in
    width = gctx_scr.shape[1]
    pair_w = 2 * HEAD_DIM
    scale = 1.0 / math.sqrt(HEAD_DIM)
    gy = jnp.where(sc_ref[3] > 0, cot_ref[...], recv_ref[...])
    upper_ref[...] = gy
    gctx_scr[...] = lax.dot_general(
        gy, wout_ref[...], NT, preferred_element_type=F32).astype(BF16)
    lane = lax.broadcasted_iota(jnp.int32, (1, pair_w), 1)
    low = lane < HEAD_DIM
    for pair in range(width // pair_w):
        cols = pl.ds(pair * pair_w, pair_w)
        q2 = qkv_ref[:, pl.ds(pair * pair_w, pair_w)]
        k2 = qkv_ref[:, pl.ds(width + pair * pair_w, pair_w)]
        v2 = qkv_ref[:, pl.ds(2 * width + pair * pair_w, pair_w)]
        g2 = gctx_scr[:, cols]
        outs = []
        for half in range(2):
            mine = low if half == 0 else jnp.logical_not(low)
            gh = jnp.where(mine, g2, jnp.zeros_like(g2))
            p = p_ref[2 * pair + half]
            pb = p.astype(BF16)
            dp = lax.dot_general(gh, v2, NT, preferred_element_type=F32).astype(BF16).astype(F32)
            rd = jnp.sum(dp * p, axis=-1, keepdims=True)
            ds = (p * (dp - rd) * scale).astype(BF16)
            dq = jnp.dot(ds, k2, preferred_element_type=F32)
            dk = lax.dot_general(ds, q2, TN, preferred_element_type=F32)
            dv = lax.dot_general(pb, g2, TN, preferred_element_type=F32)
            outs.append((dq, dk, dv))
        lo, hi = outs
        rows_ref[:, pl.ds(pair * pair_w, pair_w)] = jnp.where(low, lo[0], hi[0]).astype(BF16)
        rows_ref[:, pl.ds(width + pair * pair_w, pair_w)] = jnp.where(low, lo[1], hi[1]).astype(BF16)
        rows_ref[:, pl.ds(2 * width + pair * pair_w, pair_w)] = jnp.where(low, lo[2], hi[2]).astype(BF16)
    gn = lax.dot_general(rows_ref[...], wqkv_ref[...], NT, preferred_element_type=F32)
    x = x_ref[...].astype(F32)
    mean = jnp.mean(x, axis=-1, keepdims=True)
    cen = x - mean
    inv = lax.rsqrt(jnp.mean(cen * cen, axis=-1, keepdims=True) + EPS)
    xn = cen * inv
    pgain_ref[...] = jnp.sum(gn * xn, axis=0, keepdims=True)
    gh = gn * gain_ref[...]
    gin = gy.astype(F32) + inv * (
        gh
        - jnp.mean(gh, axis=-1, keepdims=True)
        - xn * jnp.mean(gh * xn, axis=-1, keepdims=True)
    )
    gin = gin.astype(BF16)
    gin_ref[...] = gin
    gx_ref[...] = gin


def full_spec(shape):
    return pl.BlockSpec(shape, lambda i, sc: (0,) * len(shape))


def slot_spec(k, rows, cols):
    return pl.BlockSpec((None, rows, cols), lambda i, sc: (sc[k], 0, 0))


def attention_forward(sc, layer_in, gain_row, qkv_weight, bias, normed_buf, ctx_buf):
    micro, seq_len, width_model = layer_in.shape
    qkv_cols = qkv_weight.shape[1]
    ctx_cols = ctx_buf.shape[2]
    heads = bias.shape[0]
    anyspec = pl.BlockSpec(memory_space=pl.ANY)
    flops = 2 * seq_len * width_model * qkv_cols + 4 * 2 * seq_len * seq_len * ctx_cols
    grid_spec = pltpu.PrefetchScalarGridSpec(
        num_scalar_prefetch=1,
        grid=(1,),
        in_specs=[
            slot_spec(1, seq_len, width_model),
            full_spec((1, width_model)),
            full_spec(qkv_weight.shape),
            full_spec(bias.shape),
            anyspec, anyspec,
        ],
        out_specs=[
            full_spec((seq_len, qkv_cols)),
            full_spec((heads, seq_len, seq_len)),
            slot_spec(0, seq_len, width_model),
            slot_spec(0, seq_len, ctx_cols),
        ],
    )
    return pl.pallas_call(
        forward_kernel,
        grid_spec=grid_spec,
        out_shape=(
            jax.ShapeDtypeStruct((seq_len, qkv_cols), BF16),
            jax.ShapeDtypeStruct((heads, seq_len, seq_len), F32),
            jax.ShapeDtypeStruct(normed_buf.shape, BF16),
            jax.ShapeDtypeStruct(ctx_buf.shape, BF16),
        ),
        input_output_aliases={5: 2, 6: 3},
        cost_estimate=pl.CostEstimate(
            flops=flops, transcendentals=bias.size, bytes_accessed=8 * 1024 * 1024),
    )(sc, layer_in, gain_row, qkv_weight, bias, normed_buf, ctx_buf)


def attention_backward(sc, layer_in, cotangent, received, gain_row, qkv_weight, out_weight,
                       qkv, probs, bufs):
    micro, seq_len, width_model = layer_in.shape
    qkv_cols = qkv_weight.shape[1]
    ctx_cols = out_weight.shape[0]
    anyspec = pl.BlockSpec(memory_space=pl.ANY)
    flops = 2 * seq_len * width_model * (qkv_cols + ctx_cols) + 8 * 2 * seq_len * seq_len * ctx_cols
    grid_spec = pltpu.PrefetchScalarGridSpec(
        num_scalar_prefetch=1,
        grid=(1,),
        in_specs=[
            slot_spec(1, seq_len, width_model),
            slot_spec(2, seq_len, width_model),
            full_spec((seq_len, width_model)),
            full_spec((1, width_model)),
            full_spec(qkv_weight.shape),
            full_spec(out_weight.shape),
            full_spec(qkv.shape),
            full_spec(probs.shape),
            anyspec, anyspec, anyspec,
        ],
        out_specs=[
            full_spec((seq_len, width_model)),
            slot_spec(0, seq_len, width_model),
            slot_spec(0, seq_len, qkv_cols),
            slot_spec(0, seq_len, width_model),
            full_spec((1, width_model)),
        ],
        scratch_shapes=[pltpu.VMEM((seq_len, ctx_cols), BF16)],
    )
    return pl.pallas_call(
        backward_kernel,
        grid_spec=grid_spec,
        out_shape=(
            jax.ShapeDtypeStruct((seq_len, width_model), BF16),
            *[jax.ShapeDtypeStruct(b.shape, b.dtype) for b in bufs],
            jax.ShapeDtypeStruct((1, width_model), F32),
        ),
        input_output_aliases={9: 1, 10: 2, 11: 3},
        cost_estimate=pl.CostEstimate(
            flops=flops, transcendentals=0, bytes_accessed=10 * 1024 * 1024),
    )(sc, layer_in, cotangent, received, gain_row, qkv_weight, out_weight, qkv, probs, *bufs)


def on_device(
    segment_inputs, cotangent, order, norm_gain, w_qkv, w_out, global_blocks, random_blocks
):
    segments = lax.axis_size("segment")
    my_segment = lax.axis_index("segment")
    layer_in = segment_inputs[0]
    micro_count = layer_in.shape[0]
    seq_len = layer_in.shape[1]
    width_model = layer_in.shape[2]
    gain_row = norm_gain[0][None, :]
    qkv_weight = w_qkv[0]
    out_weight = w_out[0]
    slot_order = order[0]
    block_total = seq_len // BLOCK
    block_index, usable = block_ids(global_blocks[0], random_blocks[0], block_total)
    bias = dense_bias(block_index, usable, block_total, seq_len)
    dp_size = lax.axis_size("z") * lax.axis_size("y") * lax.axis_size("core")
    grad_scale = 1.0 / math.sqrt(dp_size * micro_count * seq_len)
    qkv_cols = qkv_weight.shape[1]
    ctx_cols = out_weight.shape[0]

    grad_x = jnp.zeros((micro_count + 1, seq_len, width_model), BF16)
    normed_buf = jnp.zeros((micro_count + 1, seq_len, width_model), BF16)
    rows_buf = jnp.zeros((micro_count + 1, seq_len, qkv_cols), BF16)
    ctx_buf = jnp.zeros((micro_count + 1, seq_len, ctx_cols), BF16)
    upper_buf = jnp.zeros((micro_count + 1, seq_len, width_model), BF16)
    gain_total = jnp.zeros((1, width_model), F32)
    received = jnp.zeros(layer_in.shape[1:], BF16)
    last_tick = micro_count + segments - 1
    use_cot = (my_segment == segments - 1).astype(jnp.int32)
    for timestep in range(last_tick):
        slot_now = timestep - (segments - 1) + my_segment
        active = (slot_now >= 0) & (slot_now < micro_count)
        slot_clip = jnp.clip(slot_now, 0, micro_count - 1)
        batch_id = slot_order[slot_clip]
        write_id = jnp.where(active, batch_id, jnp.int32(micro_count))
        sc = jnp.stack([write_id, batch_id, slot_clip, use_cot]).astype(jnp.int32)
        qkv, probs, normed_buf, ctx_buf = attention_forward(
            sc, layer_in, gain_row, qkv_weight, bias, normed_buf, ctx_buf)
        grad_in, grad_x, rows_buf, upper_buf, part_gain = attention_backward(
            sc, layer_in, cotangent, received, gain_row, qkv_weight, out_weight, qkv, probs,
            (grad_x, rows_buf, upper_buf),
        )
        gain_total = gain_total + jnp.where(active, part_gain, jnp.zeros_like(part_gain))
        if timestep + 1 < last_tick:
            received = from_behind(grad_in, "segment", -1)
    all_normed = normed_buf[:micro_count].reshape(micro_count * seq_len, width_model)
    all_rows = rows_buf[:micro_count].reshape(micro_count * seq_len, qkv_cols)
    all_ctx = ctx_buf[:micro_count].reshape(micro_count * seq_len, ctx_cols)
    all_upper = upper_buf[:micro_count].reshape(micro_count * seq_len, width_model)
    sum_qkv = lax.dot_general(all_normed, all_rows, TN, preferred_element_type=F32)
    sum_out = lax.dot_general(all_ctx, all_upper, TN, preferred_element_type=F32)
    rows_total = qkv_weight.shape[0]
    fold = rows_total // ctx_cols
    out_folded = sum_out.reshape(rows_total, ctx_cols * width_model // rows_total)
    gain_col = gain_total.reshape(rows_total, width_model // rows_total)
    pad = jnp.zeros((rows_total, 128 - gain_col.shape[1]), BF16)
    packed = jnp.concatenate(
        [(sum_qkv * grad_scale).astype(BF16), (out_folded * grad_scale).astype(BF16),
         (gain_col * grad_scale).astype(BF16), pad], axis=1)
    share = dp_reduce_scatter(packed)
    share_rows = share.shape[0]
    qkv_share = share[:, :qkv_cols]
    out_share = share[:, qkv_cols:qkv_cols + out_folded.shape[1]].reshape(share_rows // fold, width_model)
    gain_share = share[:, qkv_cols + out_folded.shape[1]:qkv_cols + out_folded.shape[1] + gain_col.shape[1]].reshape(-1)
    return (grad_x[:micro_count][None], qkv_share[None], out_share[None], gain_share[None])


def solution(mesh):
    dp = ("z", "y", "core")
    segs = mesh.shape["segment"]
    cores = 2
    ys = 4
    zs = mesh.shape["dp"] // (cores * ys)
    mesh4 = Mesh(mesh.devices.reshape(segs, zs, ys, cores), ("segment", "z", "y", "core"))
    in_specs = (
        P("segment", dp, None, None),
        P(dp, None, None),
        P(dp, None),
        P("segment", None),
        P("segment", None, None),
        P("segment", None, None),
        P("segment", None),
        P("segment", None, None, None),
    )
    out_specs = (
        P("segment", dp, None, None),
        P("segment", dp, None),
        P("segment", dp, None),
        P("segment", dp),
    )
    return jax.shard_map(
        on_device, mesh=mesh4, in_specs=in_specs, out_specs=out_specs, check_vma=False
    )
```

```python
import math

import jax
import jax.numpy as jnp
from jax import lax
from jax.experimental import pallas as pl
from jax.experimental.pallas import tpu as pltpu
from jax.sharding import Mesh, PartitionSpec as P

BLOCK = 64
HEAD_DIM = 64
EPS = 1e-05
F32 = jnp.float32
BF16 = jnp.bfloat16
NT = (((1,), (1,)), ((), ()))
TN = (((0,), (0,)), ((), ()))


def from_behind(value, axis, by):
    count = lax.axis_size(axis)
    pairs = [(i, i + by) for i in range(count) if 0 <= i + by < count]
    return lax.ppermute(value, axis, pairs)


def block_ids(glob_ids, rand_ids, block_count):
    head_count = rand_ids.shape[0]
    block_rows = jnp.arange(block_count, dtype=jnp.int32)
    window = block_rows[:, None] + jnp.arange(-1, 2, dtype=jnp.int32)[None, :]
    inside = (window >= 0) & (window < block_count)
    window_ids = jnp.where(inside, window, jnp.int32(-1))
    global_ids = jnp.broadcast_to(glob_ids[None, :], (block_count, glob_ids.shape[0]))
    fixed_ids = jnp.concatenate([window_ids, global_ids], axis=1)
    fixed_ids = jnp.broadcast_to(fixed_ids[None], (head_count, block_count, fixed_ids.shape[1]))
    listed_blocks = jnp.concatenate([fixed_ids, rand_ids], axis=2)
    list_len = listed_blocks.shape[2]
    earlier = (
        jnp.arange(list_len, dtype=jnp.int32)[:, None]
        > jnp.arange(list_len, dtype=jnp.int32)[None, :]
    )
    equal_prior = (listed_blocks[..., :, None] == listed_blocks[..., None, :]) & earlier
    repeated = jnp.any(equal_prior, axis=-1)
    usable = (listed_blocks >= 0) & jnp.logical_not(repeated)
    block_index = jnp.clip(listed_blocks, 0, block_count - 1)
    return (block_index, usable)


def halving(cur, steps):
    for axis, dim, bit in steps:
        n = lax.axis_size(axis)
        half = cur.shape[dim] // 2
        mybit = (lax.axis_index(axis) // bit) % 2
        keep = lax.dynamic_slice_in_dim(cur, mybit * half, half, axis=dim)
        send = lax.dynamic_slice_in_dim(cur, (1 - mybit) * half, half, axis=dim)
        recv = lax.ppermute(send.astype(BF16), axis, [(i, i ^ bit) for i in range(n)])
        cur = keep.astype(F32) + recv.astype(F32)
    return cur


def dp_reduce_scatter(first, second):
    cores = lax.axis_size("core")
    ys = lax.axis_size("y")
    zs = lax.axis_size("z")
    chunk = first.shape[0] // (zs * ys * cores)
    z_steps = [("z", 0, zs // 2 ** (k + 1)) for k in range(int(math.log2(zs)))]
    y_steps = [("y", 1, ys // 2 ** (k + 1)) for k in range(int(math.log2(ys)))]
    core_step = [("core", 2, 1)]
    outs = []
    for part, steps in ((first, z_steps + y_steps), (second, y_steps + z_steps)):
        v = part.reshape(zs, ys, cores, chunk, part.shape[1])
        outs.append(halving(v, core_step + steps).reshape(chunk, part.shape[1]))
    return outs


def dense_bias(block_index, usable, block_count, seq_len):
    names = block_index[..., None] == jnp.arange(block_count, dtype=jnp.int32)
    allowed = jnp.any(names & usable[..., None], axis=2)
    small = jnp.where(allowed, F32(0.0), F32(-1e30))
    extent = seq_len // block_count
    return jnp.repeat(jnp.repeat(small, extent, axis=1), extent, axis=2)


def forward_kernel(sc_ref, x_ref, gain_ref, wqkv_ref, bias_ref, nb_in, cb_in,
                   qkv_ref, p_ref, normed_ref, ctx_ref):
    del sc_ref, nb_in, cb_in
    width = ctx_ref.shape[1]
    pair_w = 2 * HEAD_DIM
    scale = 1.0 / math.sqrt(HEAD_DIM)
    x = x_ref[...].astype(F32)
    mean = jnp.mean(x, axis=-1, keepdims=True)
    cen = x - mean
    inv = lax.rsqrt(jnp.mean(cen * cen, axis=-1, keepdims=True) + EPS)
    normed = (cen * inv * gain_ref[...]).astype(BF16)
    normed_ref[...] = normed
    qkv_ref[...] = jnp.dot(normed, wqkv_ref[...], preferred_element_type=F32).astype(BF16)
    lane = lax.broadcasted_iota(jnp.int32, (1, pair_w), 1)
    low = lane < HEAD_DIM
    for pair in range(width // pair_w):
        q2 = qkv_ref[:, pl.ds(pair * pair_w, pair_w)]
        k2 = qkv_ref[:, pl.ds(width + pair * pair_w, pair_w)]
        v2 = qkv_ref[:, pl.ds(2 * width + pair * pair_w, pair_w)]
        ctxs = []
        for half in range(2):
            mine = low if half == 0 else jnp.logical_not(low)
            qh = jnp.where(mine, q2, jnp.zeros_like(q2))
            s = lax.dot_general(qh, k2, NT, preferred_element_type=F32) * scale
            s = s + bias_ref[2 * pair + half]
            m = jnp.max(s, axis=-1, keepdims=True)
            e = jnp.exp(s - m)
            p = e / jnp.sum(e, axis=-1, keepdims=True)
            p_ref[2 * pair + half] = p
            ctxs.append(jnp.dot(p.astype(BF16), v2, preferred_element_type=F32))
        ctx_ref[:, pl.ds(pair * pair_w, pair_w)] = jnp.where(low, ctxs[0], ctxs[1]).astype(BF16)


def backward_kernel(sc_ref, x_ref, cot_ref, recv_ref, gain_ref, wqkv_ref, wout_ref, qkv_ref, p_ref,
                    gx_in, rb_in, ub_in,
                    gin_ref, gx_ref, rows_ref, upper_ref, pgain_ref, gctx_scr):
    del gx_in, rb_in, ub_in
    width = gctx_scr.shape[1]
    pair_w = 2 * HEAD_DIM
    scale = 1.0 / math.sqrt(HEAD_DIM)
    gy = jnp.where(sc_ref[3] > 0, cot_ref[...], recv_ref[...])
    upper_ref[...] = gy
    gctx_scr[...] = lax.dot_general(
        gy, wout_ref[...], NT, preferred_element_type=F32).astype(BF16)
    lane = lax.broadcasted_iota(jnp.int32, (1, pair_w), 1)
    low = lane < HEAD_DIM
    for pair in range(width // pair_w):
        cols = pl.ds(pair * pair_w, pair_w)
        q2 = qkv_ref[:, pl.ds(pair * pair_w, pair_w)]
        k2 = qkv_ref[:, pl.ds(width + pair * pair_w, pair_w)]
        v2 = qkv_ref[:, pl.ds(2 * width + pair * pair_w, pair_w)]
        g2 = gctx_scr[:, cols]
        outs = []
        for half in range(2):
            mine = low if half == 0 else jnp.logical_not(low)
            gh = jnp.where(mine, g2, jnp.zeros_like(g2))
            p = p_ref[2 * pair + half]
            pb = p.astype(BF16)
            dp = lax.dot_general(gh, v2, NT, preferred_element_type=F32).astype(BF16).astype(F32)
            rd = jnp.sum(dp * p, axis=-1, keepdims=True)
            ds = (p * (dp - rd) * scale).astype(BF16)
            dq = jnp.dot(ds, k2, preferred_element_type=F32)
            dk = lax.dot_general(ds, q2, TN, preferred_element_type=F32)
            dv = lax.dot_general(pb, g2, TN, preferred_element_type=F32)
            outs.append((dq, dk, dv))
        lo, hi = outs
        rows_ref[:, pl.ds(pair * pair_w, pair_w)] = jnp.where(low, lo[0], hi[0]).astype(BF16)
        rows_ref[:, pl.ds(width + pair * pair_w, pair_w)] = jnp.where(low, lo[1], hi[1]).astype(BF16)
        rows_ref[:, pl.ds(2 * width + pair * pair_w, pair_w)] = jnp.where(low, lo[2], hi[2]).astype(BF16)
    gn = lax.dot_general(rows_ref[...], wqkv_ref[...], NT, preferred_element_type=F32)
    x = x_ref[...].astype(F32)
    mean = jnp.mean(x, axis=-1, keepdims=True)
    cen = x - mean
    inv = lax.rsqrt(jnp.mean(cen * cen, axis=-1, keepdims=True) + EPS)
    xn = cen * inv
    pgain_ref[...] = jnp.sum(gn * xn, axis=0, keepdims=True)
    gh = gn * gain_ref[...]
    gin = gy.astype(F32) + inv * (
        gh
        - jnp.mean(gh, axis=-1, keepdims=True)
        - xn * jnp.mean(gh * xn, axis=-1, keepdims=True)
    )
    gin = gin.astype(BF16)
    gin_ref[...] = gin
    gx_ref[...] = gin


def full_spec(shape):
    return pl.BlockSpec(shape, lambda i, sc: (0,) * len(shape))


def slot_spec(k, rows, cols):
    return pl.BlockSpec((None, rows, cols), lambda i, sc: (sc[k], 0, 0))


def attention_forward(sc, layer_in, gain_row, qkv_weight, bias, normed_buf, ctx_buf):
    micro, seq_len, width_model = layer_in.shape
    qkv_cols = qkv_weight.shape[1]
    ctx_cols = ctx_buf.shape[2]
    heads = bias.shape[0]
    anyspec = pl.BlockSpec(memory_space=pl.ANY)
    flops = 2 * seq_len * width_model * qkv_cols + 4 * 2 * seq_len * seq_len * ctx_cols
    grid_spec = pltpu.PrefetchScalarGridSpec(
        num_scalar_prefetch=1,
        grid=(1,),
        in_specs=[
            slot_spec(1, seq_len, width_model),
            full_spec((1, width_model)),
            full_spec(qkv_weight.shape),
            full_spec(bias.shape),
            anyspec, anyspec,
        ],
        out_specs=[
            full_spec((seq_len, qkv_cols)),
            full_spec((heads, seq_len, seq_len)),
            slot_spec(0, seq_len, width_model),
            slot_spec(0, seq_len, ctx_cols),
        ],
    )
    return pl.pallas_call(
        forward_kernel,
        grid_spec=grid_spec,
        out_shape=(
            jax.ShapeDtypeStruct((seq_len, qkv_cols), BF16),
            jax.ShapeDtypeStruct((heads, seq_len, seq_len), F32),
            jax.ShapeDtypeStruct(normed_buf.shape, BF16),
            jax.ShapeDtypeStruct(ctx_buf.shape, BF16),
        ),
        input_output_aliases={5: 2, 6: 3},
        cost_estimate=pl.CostEstimate(
            flops=flops, transcendentals=bias.size, bytes_accessed=8 * 1024 * 1024),
    )(sc, layer_in, gain_row, qkv_weight, bias, normed_buf, ctx_buf)


def attention_backward(sc, layer_in, cotangent, received, gain_row, qkv_weight, out_weight,
                       qkv, probs, bufs):
    micro, seq_len, width_model = layer_in.shape
    qkv_cols = qkv_weight.shape[1]
    ctx_cols = out_weight.shape[0]
    anyspec = pl.BlockSpec(memory_space=pl.ANY)
    flops = 2 * seq_len * width_model * (qkv_cols + ctx_cols) + 8 * 2 * seq_len * seq_len * ctx_cols
    grid_spec = pltpu.PrefetchScalarGridSpec(
        num_scalar_prefetch=1,
        grid=(1,),
        in_specs=[
            slot_spec(1, seq_len, width_model),
            slot_spec(2, seq_len, width_model),
            full_spec((seq_len, width_model)),
            full_spec((1, width_model)),
            full_spec(qkv_weight.shape),
            full_spec(out_weight.shape),
            full_spec(qkv.shape),
            full_spec(probs.shape),
            anyspec, anyspec, anyspec,
        ],
        out_specs=[
            full_spec((seq_len, width_model)),
            slot_spec(0, seq_len, width_model),
            slot_spec(0, seq_len, qkv_cols),
            slot_spec(0, seq_len, width_model),
            full_spec((1, width_model)),
        ],
        scratch_shapes=[pltpu.VMEM((seq_len, ctx_cols), BF16)],
    )
    return pl.pallas_call(
        backward_kernel,
        grid_spec=grid_spec,
        out_shape=(
            jax.ShapeDtypeStruct((seq_len, width_model), BF16),
            *[jax.ShapeDtypeStruct(b.shape, b.dtype) for b in bufs],
            jax.ShapeDtypeStruct((1, width_model), F32),
        ),
        input_output_aliases={9: 1, 10: 2, 11: 3},
        cost_estimate=pl.CostEstimate(
            flops=flops, transcendentals=0, bytes_accessed=10 * 1024 * 1024),
    )(sc, layer_in, cotangent, received, gain_row, qkv_weight, out_weight, qkv, probs, *bufs)


def on_device(
    segment_inputs, cotangent, order, norm_gain, w_qkv, w_out, global_blocks, random_blocks
):
    segments = lax.axis_size("segment")
    my_segment = lax.axis_index("segment")
    layer_in = segment_inputs[0]
    micro_count = layer_in.shape[0]
    seq_len = layer_in.shape[1]
    width_model = layer_in.shape[2]
    gain_row = norm_gain[0][None, :]
    qkv_weight = w_qkv[0]
    out_weight = w_out[0]
    slot_order = order[0]
    block_total = seq_len // BLOCK
    block_index, usable = block_ids(global_blocks[0], random_blocks[0], block_total)
    bias = dense_bias(block_index, usable, block_total, seq_len)
    dp_size = lax.axis_size("z") * lax.axis_size("y") * lax.axis_size("core")
    grad_scale = 1.0 / math.sqrt(dp_size * micro_count * seq_len)
    qkv_cols = qkv_weight.shape[1]
    ctx_cols = out_weight.shape[0]

    grad_x = jnp.zeros((micro_count + 1, seq_len, width_model), BF16)
    normed_buf = jnp.zeros((micro_count + 1, seq_len, width_model), BF16)
    rows_buf = jnp.zeros((micro_count + 1, seq_len, qkv_cols), BF16)
    ctx_buf = jnp.zeros((micro_count + 1, seq_len, ctx_cols), BF16)
    upper_buf = jnp.zeros((micro_count + 1, seq_len, width_model), BF16)
    gain_total = jnp.zeros((1, width_model), F32)
    received = jnp.zeros(layer_in.shape[1:], BF16)
    last_tick = micro_count + segments - 1
    use_cot = (my_segment == segments - 1).astype(jnp.int32)
    for timestep in range(last_tick):
        slot_now = timestep - (segments - 1) + my_segment
        active = (slot_now >= 0) & (slot_now < micro_count)
        slot_clip = jnp.clip(slot_now, 0, micro_count - 1)
        batch_id = slot_order[slot_clip]
        write_id = jnp.where(active, batch_id, jnp.int32(micro_count))
        sc = jnp.stack([write_id, batch_id, slot_clip, use_cot]).astype(jnp.int32)
        qkv, probs, normed_buf, ctx_buf = attention_forward(
            sc, layer_in, gain_row, qkv_weight, bias, normed_buf, ctx_buf)
        grad_in, grad_x, rows_buf, upper_buf, part_gain = attention_backward(
            sc, layer_in, cotangent, received, gain_row, qkv_weight, out_weight, qkv, probs,
            (grad_x, rows_buf, upper_buf),
        )
        gain_total = gain_total + jnp.where(active, part_gain, jnp.zeros_like(part_gain))
        if timestep + 1 < last_tick:
            received = from_behind(grad_in, "segment", -1)
    all_normed = normed_buf[:micro_count].reshape(micro_count * seq_len, width_model)
    all_rows = rows_buf[:micro_count].reshape(micro_count * seq_len, qkv_cols)
    all_ctx = ctx_buf[:micro_count].reshape(micro_count * seq_len, ctx_cols)
    all_upper = upper_buf[:micro_count].reshape(micro_count * seq_len, width_model)
    sum_qkv = lax.dot_general(all_normed, all_rows, TN, preferred_element_type=F32)
    sum_out = lax.dot_general(all_ctx, all_upper, TN, preferred_element_type=F32)
    rows_total = qkv_weight.shape[0]
    fold = rows_total // ctx_cols
    out_folded = sum_out.reshape(rows_total, ctx_cols * width_model // rows_total)
    gain_col = gain_total.reshape(rows_total, width_model // rows_total)
    pad = jnp.zeros((rows_total, 128 - gain_col.shape[1]), BF16)
    out_gain = jnp.concatenate(
        [(out_folded * grad_scale).astype(BF16), (gain_col * grad_scale).astype(BF16), pad], axis=1)
    qkv_share, out_gain_share = dp_reduce_scatter((sum_qkv * grad_scale).astype(BF16), out_gain)
    share = jnp.concatenate([qkv_share, out_gain_share], axis=1)
    share_rows = share.shape[0]
    qkv_share = share[:, :qkv_cols]
    out_share = share[:, qkv_cols:qkv_cols + out_folded.shape[1]].reshape(share_rows // fold, width_model)
    gain_share = share[:, qkv_cols + out_folded.shape[1]:qkv_cols + out_folded.shape[1] + gain_col.shape[1]].reshape(-1)
    return (grad_x[:micro_count][None], qkv_share[None], out_share[None], gain_share[None])


def solution(mesh):
    dp = ("z", "y", "core")
    segs = mesh.shape["segment"]
    cores = 2
    ys = 4
    zs = mesh.shape["dp"] // (cores * ys)
    mesh4 = Mesh(mesh.devices.reshape(segs, zs, ys, cores), ("segment", "z", "y", "core"))
    in_specs = (
        P("segment", dp, None, None),
        P(dp, None, None),
        P(dp, None),
        P("segment", None),
        P("segment", None, None),
        P("segment", None, None),
        P("segment", None),
        P("segment", None, None, None),
    )
    out_specs = (
        P("segment", dp, None, None),
        P("segment", dp, None),
        P("segment", dp, None),
        P("segment", dp),
    )
    return jax.shard_map(
        on_device, mesh=mesh4, in_specs=in_specs, out_specs=out_specs, check_vma=False
    )
```

```python
import math

import jax
import jax.numpy as jnp
from jax import lax
from jax.experimental import pallas as pl
from jax.experimental.pallas import tpu as pltpu
from jax.sharding import Mesh, PartitionSpec as P

BLOCK = 64
HEAD_DIM = 64
EPS = 1e-05
F32 = jnp.float32
BF16 = jnp.bfloat16
NT = (((1,), (1,)), ((), ()))
TN = (((0,), (0,)), ((), ()))


def from_behind(value, axis, by):
    count = lax.axis_size(axis)
    pairs = [(i, i + by) for i in range(count) if 0 <= i + by < count]
    return lax.ppermute(value, axis, pairs)


def block_ids(glob_ids, rand_ids, block_count):
    head_count = rand_ids.shape[0]
    block_rows = jnp.arange(block_count, dtype=jnp.int32)
    window = block_rows[:, None] + jnp.arange(-1, 2, dtype=jnp.int32)[None, :]
    inside = (window >= 0) & (window < block_count)
    window_ids = jnp.where(inside, window, jnp.int32(-1))
    global_ids = jnp.broadcast_to(glob_ids[None, :], (block_count, glob_ids.shape[0]))
    fixed_ids = jnp.concatenate([window_ids, global_ids], axis=1)
    fixed_ids = jnp.broadcast_to(fixed_ids[None], (head_count, block_count, fixed_ids.shape[1]))
    listed_blocks = jnp.concatenate([fixed_ids, rand_ids], axis=2)
    list_len = listed_blocks.shape[2]
    earlier = (
        jnp.arange(list_len, dtype=jnp.int32)[:, None]
        > jnp.arange(list_len, dtype=jnp.int32)[None, :]
    )
    equal_prior = (listed_blocks[..., :, None] == listed_blocks[..., None, :]) & earlier
    repeated = jnp.any(equal_prior, axis=-1)
    usable = (listed_blocks >= 0) & jnp.logical_not(repeated)
    block_index = jnp.clip(listed_blocks, 0, block_count - 1)
    return (block_index, usable)


def halving(cur, steps):
    for axis, dim, bit in steps:
        n = lax.axis_size(axis)
        half = cur.shape[dim] // 2
        mybit = (lax.axis_index(axis) // bit) % 2
        keep = lax.dynamic_slice_in_dim(cur, mybit * half, half, axis=dim)
        send = lax.dynamic_slice_in_dim(cur, (1 - mybit) * half, half, axis=dim)
        recv = lax.ppermute(send.astype(BF16), axis, [(i, i ^ bit) for i in range(n)])
        cur = keep.astype(F32) + recv.astype(F32)
    return cur


def dp_reduce_scatter(first, second):
    cores = lax.axis_size("core")
    ys = lax.axis_size("y")
    zs = lax.axis_size("z")
    chunk = first.shape[0] // (zs * ys * cores)
    z_steps = [("z", 0, zs // 2 ** (k + 1)) for k in range(int(math.log2(zs)))]
    y_steps = [("y", 1, ys // 2 ** (k + 1)) for k in range(int(math.log2(ys)))]
    core_step = [("core", 2, 1)]
    outs = []
    for part, steps in ((first, z_steps + y_steps), (second, y_steps + z_steps)):
        v = part.reshape(zs, ys, cores, chunk, part.shape[1])
        outs.append(halving(v, core_step + steps).reshape(chunk, part.shape[1]))
    return outs


def dense_bias(block_index, usable, block_count, seq_len):
    names = block_index[..., None] == jnp.arange(block_count, dtype=jnp.int32)
    allowed = jnp.any(names & usable[..., None], axis=2)
    small = jnp.where(allowed, F32(0.0), F32(-1e30))
    extent = seq_len // block_count
    return jnp.repeat(jnp.repeat(small, extent, axis=1), extent, axis=2)


def forward_kernel(sc_ref, x_ref, gain_ref, wqkv_ref, bias_ref, nb_in, cb_in,
                   qkv_ref, p_ref, normed_ref, ctx_ref):
    del sc_ref, nb_in, cb_in
    width = ctx_ref.shape[1]
    pair_w = 2 * HEAD_DIM
    scale = 1.0 / math.sqrt(HEAD_DIM)
    x = x_ref[...].astype(F32)
    mean = jnp.mean(x, axis=-1, keepdims=True)
    cen = x - mean
    inv = lax.rsqrt(jnp.mean(cen * cen, axis=-1, keepdims=True) + EPS)
    normed = (cen * inv * gain_ref[...]).astype(BF16)
    normed_ref[...] = normed
    qkv_ref[...] = jnp.dot(normed, wqkv_ref[...], preferred_element_type=F32).astype(BF16)
    lane = lax.broadcasted_iota(jnp.int32, (1, pair_w), 1)
    low = lane < HEAD_DIM
    for pair in range(width // pair_w):
        q2 = qkv_ref[:, pl.ds(pair * pair_w, pair_w)]
        k2 = qkv_ref[:, pl.ds(width + pair * pair_w, pair_w)]
        v2 = qkv_ref[:, pl.ds(2 * width + pair * pair_w, pair_w)]
        ctxs = []
        for half in range(2):
            mine = low if half == 0 else jnp.logical_not(low)
            qh = jnp.where(mine, q2, jnp.zeros_like(q2))
            s = lax.dot_general(qh, k2, NT, preferred_element_type=F32) * scale
            s = s + bias_ref[2 * pair + half]
            m = jnp.max(s, axis=-1, keepdims=True)
            e = jnp.exp(s - m)
            p = e / jnp.sum(e, axis=-1, keepdims=True)
            p_ref[2 * pair + half] = p
            ctxs.append(jnp.dot(p.astype(BF16), v2, preferred_element_type=F32))
        ctx_ref[:, pl.ds(pair * pair_w, pair_w)] = jnp.where(low, ctxs[0], ctxs[1]).astype(BF16)


def backward_kernel(sc_ref, x_hbm, cot_ref, recv_ref, gain_ref, wqkv_hbm, wout_ref, qkv_ref, p_hbm,
                    gx_in, rb_in, ub_in,
                    gin_ref, gx_ref, rows_ref, upper_ref, pgain_ref, gctx_scr,
                    wqkv_ref, p_ref, x_ref, sems):
    del gx_in, rb_in, ub_in
    heads = p_ref.shape[0]
    p_copies = [pltpu.make_async_copy(p_hbm.at[h], p_ref.at[h], sems.at[h]) for h in range(heads)]
    for copy in p_copies:
        copy.start()
    w_copy = pltpu.make_async_copy(wqkv_hbm, wqkv_ref, sems.at[heads])
    w_copy.start()
    x_copy = pltpu.make_async_copy(x_hbm.at[sc_ref[1]], x_ref, sems.at[heads + 1])
    x_copy.start()
    width = gctx_scr.shape[1]
    pair_w = 2 * HEAD_DIM
    scale = 1.0 / math.sqrt(HEAD_DIM)
    gy = jnp.where(sc_ref[3] > 0, cot_ref[...], recv_ref[...])
    upper_ref[...] = gy
    gctx_scr[...] = lax.dot_general(
        gy, wout_ref[...], NT, preferred_element_type=F32).astype(BF16)
    lane = lax.broadcasted_iota(jnp.int32, (1, pair_w), 1)
    low = lane < HEAD_DIM
    for pair in range(width // pair_w):
        cols = pl.ds(pair * pair_w, pair_w)
        q2 = qkv_ref[:, pl.ds(pair * pair_w, pair_w)]
        k2 = qkv_ref[:, pl.ds(width + pair * pair_w, pair_w)]
        v2 = qkv_ref[:, pl.ds(2 * width + pair * pair_w, pair_w)]
        g2 = gctx_scr[:, cols]
        outs = []
        for half in range(2):
            mine = low if half == 0 else jnp.logical_not(low)
            gh = jnp.where(mine, g2, jnp.zeros_like(g2))
            p_copies[2 * pair + half].wait()
            p = p_ref[2 * pair + half]
            pb = p.astype(BF16)
            dp = lax.dot_general(gh, v2, NT, preferred_element_type=F32).astype(BF16).astype(F32)
            rd = jnp.sum(dp * p, axis=-1, keepdims=True)
            ds = (p * (dp - rd) * scale).astype(BF16)
            dq = jnp.dot(ds, k2, preferred_element_type=F32)
            dk = lax.dot_general(ds, q2, TN, preferred_element_type=F32)
            dv = lax.dot_general(pb, g2, TN, preferred_element_type=F32)
            outs.append((dq, dk, dv))
        lo, hi = outs
        rows_ref[:, pl.ds(pair * pair_w, pair_w)] = jnp.where(low, lo[0], hi[0]).astype(BF16)
        rows_ref[:, pl.ds(width + pair * pair_w, pair_w)] = jnp.where(low, lo[1], hi[1]).astype(BF16)
        rows_ref[:, pl.ds(2 * width + pair * pair_w, pair_w)] = jnp.where(low, lo[2], hi[2]).astype(BF16)
    w_copy.wait()
    gn = lax.dot_general(rows_ref[...], wqkv_ref[...], NT, preferred_element_type=F32)
    x_copy.wait()
    x = x_ref[...].astype(F32)
    mean = jnp.mean(x, axis=-1, keepdims=True)
    cen = x - mean
    inv = lax.rsqrt(jnp.mean(cen * cen, axis=-1, keepdims=True) + EPS)
    xn = cen * inv
    pgain_ref[...] = jnp.sum(gn * xn, axis=0, keepdims=True)
    gh = gn * gain_ref[...]
    gin = gy.astype(F32) + inv * (
        gh
        - jnp.mean(gh, axis=-1, keepdims=True)
        - xn * jnp.mean(gh * xn, axis=-1, keepdims=True)
    )
    gin = gin.astype(BF16)
    gin_ref[...] = gin
    gx_ref[...] = gin


def full_spec(shape):
    return pl.BlockSpec(shape, lambda i, sc: (0,) * len(shape))


def slot_spec(k, rows, cols):
    return pl.BlockSpec((None, rows, cols), lambda i, sc: (sc[k], 0, 0))


def attention_forward(sc, layer_in, gain_row, qkv_weight, bias, normed_buf, ctx_buf):
    micro, seq_len, width_model = layer_in.shape
    qkv_cols = qkv_weight.shape[1]
    ctx_cols = ctx_buf.shape[2]
    heads = bias.shape[0]
    anyspec = pl.BlockSpec(memory_space=pl.ANY)
    flops = 2 * seq_len * width_model * qkv_cols + 4 * 2 * seq_len * seq_len * ctx_cols
    grid_spec = pltpu.PrefetchScalarGridSpec(
        num_scalar_prefetch=1,
        grid=(1,),
        in_specs=[
            slot_spec(1, seq_len, width_model),
            full_spec((1, width_model)),
            full_spec(qkv_weight.shape),
            full_spec(bias.shape),
            anyspec, anyspec,
        ],
        out_specs=[
            full_spec((seq_len, qkv_cols)),
            full_spec((heads, seq_len, seq_len)),
            slot_spec(0, seq_len, width_model),
            slot_spec(0, seq_len, ctx_cols),
        ],
    )
    return pl.pallas_call(
        forward_kernel,
        grid_spec=grid_spec,
        out_shape=(
            jax.ShapeDtypeStruct((seq_len, qkv_cols), BF16),
            jax.ShapeDtypeStruct((heads, seq_len, seq_len), F32),
            jax.ShapeDtypeStruct(normed_buf.shape, BF16),
            jax.ShapeDtypeStruct(ctx_buf.shape, BF16),
        ),
        input_output_aliases={5: 2, 6: 3},
        cost_estimate=pl.CostEstimate(
            flops=flops, transcendentals=bias.size, bytes_accessed=8 * 1024 * 1024),
    )(sc, layer_in, gain_row, qkv_weight, bias, normed_buf, ctx_buf)


def attention_backward(sc, layer_in, cotangent, received, gain_row, qkv_weight, out_weight,
                       qkv, probs, bufs):
    micro, seq_len, width_model = layer_in.shape
    qkv_cols = qkv_weight.shape[1]
    ctx_cols = out_weight.shape[0]
    anyspec = pl.BlockSpec(memory_space=pl.ANY)
    flops = 2 * seq_len * width_model * (qkv_cols + ctx_cols) + 8 * 2 * seq_len * seq_len * ctx_cols
    grid_spec = pltpu.PrefetchScalarGridSpec(
        num_scalar_prefetch=1,
        grid=(1,),
        in_specs=[
            anyspec,
            slot_spec(2, seq_len, width_model),
            full_spec((seq_len, width_model)),
            full_spec((1, width_model)),
            anyspec,
            full_spec(out_weight.shape),
            full_spec(qkv.shape),
            anyspec,
            anyspec, anyspec, anyspec,
        ],
        out_specs=[
            full_spec((seq_len, width_model)),
            slot_spec(0, seq_len, width_model),
            slot_spec(0, seq_len, qkv_cols),
            slot_spec(0, seq_len, width_model),
            full_spec((1, width_model)),
        ],
        scratch_shapes=[
            pltpu.VMEM((seq_len, ctx_cols), BF16),
            pltpu.VMEM(qkv_weight.shape, BF16),
            pltpu.VMEM(probs.shape, F32),
            pltpu.VMEM((seq_len, width_model), BF16),
            pltpu.SemaphoreType.DMA((probs.shape[0] + 2,)),
        ],
    )
    return pl.pallas_call(
        backward_kernel,
        grid_spec=grid_spec,
        out_shape=(
            jax.ShapeDtypeStruct((seq_len, width_model), BF16),
            *[jax.ShapeDtypeStruct(b.shape, b.dtype) for b in bufs],
            jax.ShapeDtypeStruct((1, width_model), F32),
        ),
        input_output_aliases={9: 1, 10: 2, 11: 3},
        cost_estimate=pl.CostEstimate(
            flops=flops, transcendentals=0, bytes_accessed=10 * 1024 * 1024),
    )(sc, layer_in, cotangent, received, gain_row, qkv_weight, out_weight, qkv, probs, *bufs)


def on_device(
    segment_inputs, cotangent, order, norm_gain, w_qkv, w_out, global_blocks, random_blocks
):
    segments = lax.axis_size("segment")
    my_segment = lax.axis_index("segment")
    layer_in = segment_inputs[0]
    micro_count = layer_in.shape[0]
    seq_len = layer_in.shape[1]
    width_model = layer_in.shape[2]
    gain_row = norm_gain[0][None, :]
    qkv_weight = w_qkv[0]
    out_weight = w_out[0]
    slot_order = order[0]
    block_total = seq_len // BLOCK
    block_index, usable = block_ids(global_blocks[0], random_blocks[0], block_total)
    bias = dense_bias(block_index, usable, block_total, seq_len)
    dp_size = lax.axis_size("z") * lax.axis_size("y") * lax.axis_size("core")
    grad_scale = 1.0 / math.sqrt(dp_size * micro_count * seq_len)
    qkv_cols = qkv_weight.shape[1]
    ctx_cols = out_weight.shape[0]

    grad_x = jnp.zeros((micro_count + 1, seq_len, width_model), BF16)
    normed_buf = jnp.zeros((micro_count + 1, seq_len, width_model), BF16)
    rows_buf = jnp.zeros((micro_count + 1, seq_len, qkv_cols), BF16)
    ctx_buf = jnp.zeros((micro_count + 1, seq_len, ctx_cols), BF16)
    upper_buf = jnp.zeros((micro_count + 1, seq_len, width_model), BF16)
    gain_total = jnp.zeros((1, width_model), F32)
    received = jnp.zeros(layer_in.shape[1:], BF16)
    last_tick = micro_count + segments - 1
    use_cot = (my_segment == segments - 1).astype(jnp.int32)
    for timestep in range(last_tick):
        slot_now = timestep - (segments - 1) + my_segment
        active = (slot_now >= 0) & (slot_now < micro_count)
        slot_clip = jnp.clip(slot_now, 0, micro_count - 1)
        batch_id = slot_order[slot_clip]
        write_id = jnp.where(active, batch_id, jnp.int32(micro_count))
        sc = jnp.stack([write_id, batch_id, slot_clip, use_cot]).astype(jnp.int32)
        qkv, probs, normed_buf, ctx_buf = attention_forward(
            sc, layer_in, gain_row, qkv_weight, bias, normed_buf, ctx_buf)
        grad_in, grad_x, rows_buf, upper_buf, part_gain = attention_backward(
            sc, layer_in, cotangent, received, gain_row, qkv_weight, out_weight, qkv, probs,
            (grad_x, rows_buf, upper_buf),
        )
        gain_total = gain_total + jnp.where(active, part_gain, jnp.zeros_like(part_gain))
        if timestep + 1 < last_tick:
            received = from_behind(grad_in, "segment", -1)
    all_normed = normed_buf[:micro_count].reshape(micro_count * seq_len, width_model)
    all_rows = rows_buf[:micro_count].reshape(micro_count * seq_len, qkv_cols)
    all_ctx = ctx_buf[:micro_count].reshape(micro_count * seq_len, ctx_cols)
    all_upper = upper_buf[:micro_count].reshape(micro_count * seq_len, width_model)
    sum_qkv = lax.dot_general(all_normed, all_rows, TN, preferred_element_type=F32)
    sum_out = lax.dot_general(all_ctx, all_upper, TN, preferred_element_type=F32)
    rows_total = qkv_weight.shape[0]
    fold = rows_total // ctx_cols
    out_folded = sum_out.reshape(rows_total, ctx_cols * width_model // rows_total)
    gain_col = gain_total.reshape(rows_total, width_model // rows_total)
    pad = jnp.zeros((rows_total, 128 - gain_col.shape[1]), BF16)
    out_gain = jnp.concatenate(
        [(out_folded * grad_scale).astype(BF16), (gain_col * grad_scale).astype(BF16), pad], axis=1)
    qkv_share, out_gain_share = dp_reduce_scatter((sum_qkv * grad_scale).astype(BF16), out_gain)
    share = jnp.concatenate([qkv_share, out_gain_share], axis=1)
    share_rows = share.shape[0]
    qkv_share = share[:, :qkv_cols]
    out_share = share[:, qkv_cols:qkv_cols + out_folded.shape[1]].reshape(share_rows // fold, width_model)
    gain_share = share[:, qkv_cols + out_folded.shape[1]:qkv_cols + out_folded.shape[1] + gain_col.shape[1]].reshape(-1)
    return (grad_x[:micro_count][None], qkv_share[None], out_share[None], gain_share[None])


def solution(mesh):
    dp = ("z", "y", "core")
    segs = mesh.shape["segment"]
    cores = 2
    ys = 4
    zs = mesh.shape["dp"] // (cores * ys)
    mesh4 = Mesh(mesh.devices.reshape(segs, zs, ys, cores), ("segment", "z", "y", "core"))
    in_specs = (
        P("segment", dp, None, None),
        P(dp, None, None),
        P(dp, None),
        P("segment", None),
        P("segment", None, None),
        P("segment", None, None),
        P("segment", None),
        P("segment", None, None, None),
    )
    out_specs = (
        P("segment", dp, None, None),
        P("segment", dp, None),
        P("segment", dp, None),
        P("segment", dp),
    )
    return jax.shard_map(
        on_device, mesh=mesh4, in_specs=in_specs, out_specs=out_specs, check_vma=False
    )
```

```python
import math

import jax
import jax.numpy as jnp
from jax import lax
from jax.experimental import pallas as pl
from jax.experimental.pallas import tpu as pltpu
from jax.sharding import Mesh, PartitionSpec as P

BLOCK = 64
HEAD_DIM = 64
EPS = 1e-05
F32 = jnp.float32
BF16 = jnp.bfloat16
NT = (((1,), (1,)), ((), ()))
TN = (((0,), (0,)), ((), ()))


def from_behind(value, axis, by):
    count = lax.axis_size(axis)
    pairs = [(i, i + by) for i in range(count) if 0 <= i + by < count]
    return lax.ppermute(value, axis, pairs)


def block_ids(glob_ids, rand_ids, block_count):
    head_count = rand_ids.shape[0]
    block_rows = jnp.arange(block_count, dtype=jnp.int32)
    window = block_rows[:, None] + jnp.arange(-1, 2, dtype=jnp.int32)[None, :]
    inside = (window >= 0) & (window < block_count)
    window_ids = jnp.where(inside, window, jnp.int32(-1))
    global_ids = jnp.broadcast_to(glob_ids[None, :], (block_count, glob_ids.shape[0]))
    fixed_ids = jnp.concatenate([window_ids, global_ids], axis=1)
    fixed_ids = jnp.broadcast_to(fixed_ids[None], (head_count, block_count, fixed_ids.shape[1]))
    listed_blocks = jnp.concatenate([fixed_ids, rand_ids], axis=2)
    list_len = listed_blocks.shape[2]
    earlier = (
        jnp.arange(list_len, dtype=jnp.int32)[:, None]
        > jnp.arange(list_len, dtype=jnp.int32)[None, :]
    )
    equal_prior = (listed_blocks[..., :, None] == listed_blocks[..., None, :]) & earlier
    repeated = jnp.any(equal_prior, axis=-1)
    usable = (listed_blocks >= 0) & jnp.logical_not(repeated)
    block_index = jnp.clip(listed_blocks, 0, block_count - 1)
    return (block_index, usable)


def halving(cur, steps):
    for axis, dim, bit in steps:
        n = lax.axis_size(axis)
        half = cur.shape[dim] // 2
        mybit = (lax.axis_index(axis) // bit) % 2
        keep = lax.dynamic_slice_in_dim(cur, mybit * half, half, axis=dim)
        send = lax.dynamic_slice_in_dim(cur, (1 - mybit) * half, half, axis=dim)
        recv = lax.ppermute(send.astype(BF16), axis, [(i, i ^ bit) for i in range(n)])
        cur = keep.astype(F32) + recv.astype(F32)
    return cur


def dp_reduce_scatter(first, second):
    cores = lax.axis_size("core")
    ys = lax.axis_size("y")
    zs = lax.axis_size("z")
    chunk = first.shape[0] // (zs * ys * cores)
    z_steps = [("z", 0, zs // 2 ** (k + 1)) for k in range(int(math.log2(zs)))]
    y_steps = [("y", 1, ys // 2 ** (k + 1)) for k in range(int(math.log2(ys)))]
    core_step = [("core", 2, 1)]
    outs = []
    for part, steps in ((first, z_steps + y_steps), (second, y_steps + z_steps)):
        v = part.reshape(zs, ys, cores, chunk, part.shape[1])
        outs.append(halving(v, core_step + steps).reshape(chunk, part.shape[1]))
    return outs


def dense_bias(block_index, usable, block_count, seq_len):
    names = block_index[..., None] == jnp.arange(block_count, dtype=jnp.int32)
    allowed = jnp.any(names & usable[..., None], axis=2)
    small = jnp.where(allowed, F32(0.0), F32(-1e30))
    extent = seq_len // block_count
    return jnp.repeat(jnp.repeat(small, extent, axis=1), extent, axis=2)


def forward_kernel(sc_ref, x_ref, gain_ref, wqkv_ref, bias_ref, nb_in, cb_in,
                   qkv_ref, p_ref, normed_ref, ctx_ref):
    del sc_ref, nb_in, cb_in
    width = ctx_ref.shape[1]
    pair_w = 2 * HEAD_DIM
    scale = 1.0 / math.sqrt(HEAD_DIM)
    x = x_ref[...].astype(F32)
    mean = jnp.mean(x, axis=-1, keepdims=True)
    cen = x - mean
    inv = lax.rsqrt(jnp.mean(cen * cen, axis=-1, keepdims=True) + EPS)
    normed = (cen * inv * gain_ref[...]).astype(BF16)
    normed_ref[...] = normed
    qkv_ref[...] = jnp.dot(normed, wqkv_ref[...], preferred_element_type=F32).astype(BF16)
    lane = lax.broadcasted_iota(jnp.int32, (1, pair_w), 1)
    low = lane < HEAD_DIM
    for pair in range(width // pair_w):
        q2 = qkv_ref[:, pl.ds(pair * pair_w, pair_w)]
        k2 = qkv_ref[:, pl.ds(width + pair * pair_w, pair_w)]
        v2 = qkv_ref[:, pl.ds(2 * width + pair * pair_w, pair_w)]
        ctxs = []
        for half in range(2):
            mine = low if half == 0 else jnp.logical_not(low)
            qh = jnp.where(mine, q2, jnp.zeros_like(q2))
            s = lax.dot_general(qh, k2, NT, preferred_element_type=F32) * scale
            s = s + bias_ref[2 * pair + half]
            m = jnp.max(s, axis=-1, keepdims=True)
            e = jnp.exp(s - m)
            p = e / jnp.sum(e, axis=-1, keepdims=True)
            p_ref[2 * pair + half] = p
            ctxs.append(jnp.dot(p.astype(BF16), v2, preferred_element_type=F32))
        ctx_ref[:, pl.ds(pair * pair_w, pair_w)] = jnp.where(low, ctxs[0], ctxs[1]).astype(BF16)


def backward_kernel(sc_ref, x_ref, cot_ref, recv_ref, gain_ref, wqkv_ref, wout_ref, qkv_ref, p_ref,
                    gx_in, rb_in, ub_in,
                    gin_ref, gx_ref, rows_ref, upper_ref, pgain_ref, gctx_scr):
    del gx_in, rb_in, ub_in
    width = gctx_scr.shape[1]
    pair_w = 2 * HEAD_DIM
    scale = 1.0 / math.sqrt(HEAD_DIM)
    gy = jnp.where(sc_ref[3] > 0, cot_ref[...], recv_ref[...])
    upper_ref[...] = gy
    gctx_scr[...] = lax.dot_general(
        gy, wout_ref[...], NT, preferred_element_type=F32).astype(BF16)
    lane = lax.broadcasted_iota(jnp.int32, (1, pair_w), 1)
    low = lane < HEAD_DIM
    for pair in range(width // pair_w):
        cols = pl.ds(pair * pair_w, pair_w)
        q2 = qkv_ref[:, pl.ds(pair * pair_w, pair_w)]
        k2 = qkv_ref[:, pl.ds(width + pair * pair_w, pair_w)]
        v2 = qkv_ref[:, pl.ds(2 * width + pair * pair_w, pair_w)]
        g2 = gctx_scr[:, cols]
        outs = []
        for half in range(2):
            mine = low if half == 0 else jnp.logical_not(low)
            gh = jnp.where(mine, g2, jnp.zeros_like(g2))
            p = p_ref[2 * pair + half]
            pb = p.astype(BF16)
            dp = lax.dot_general(gh, v2, NT, preferred_element_type=F32).astype(BF16).astype(F32)
            rd = jnp.sum(dp * p, axis=-1, keepdims=True)
            ds = (p * (dp - rd) * scale).astype(BF16)
            dq = jnp.dot(ds, k2, preferred_element_type=F32)
            dk = lax.dot_general(ds, q2, TN, preferred_element_type=F32)
            dv = lax.dot_general(pb, g2, TN, preferred_element_type=F32)
            outs.append((dq, dk, dv))
        lo, hi = outs
        rows_ref[:, pl.ds(pair * pair_w, pair_w)] = jnp.where(low, lo[0], hi[0]).astype(BF16)
        rows_ref[:, pl.ds(width + pair * pair_w, pair_w)] = jnp.where(low, lo[1], hi[1]).astype(BF16)
        rows_ref[:, pl.ds(2 * width + pair * pair_w, pair_w)] = jnp.where(low, lo[2], hi[2]).astype(BF16)
    gn = lax.dot_general(rows_ref[...], wqkv_ref[...], NT, preferred_element_type=F32)
    x = x_ref[...].astype(F32)
    mean = jnp.mean(x, axis=-1, keepdims=True)
    cen = x - mean
    inv = lax.rsqrt(jnp.mean(cen * cen, axis=-1, keepdims=True) + EPS)
    xn = cen * inv
    pgain_ref[...] = jnp.sum(gn * xn, axis=0, keepdims=True)
    gh = gn * gain_ref[...]
    gin = gy.astype(F32) + inv * (
        gh
        - jnp.mean(gh, axis=-1, keepdims=True)
        - xn * jnp.mean(gh * xn, axis=-1, keepdims=True)
    )
    gin = gin.astype(BF16)
    gin_ref[...] = gin
    gx_ref[...] = gin


def full_spec(shape):
    return pl.BlockSpec(shape, lambda i, sc: (0,) * len(shape))


def slot_spec(k, rows, cols):
    return pl.BlockSpec((None, rows, cols), lambda i, sc: (sc[k], 0, 0))


def attention_forward(sc, layer_in, gain_row, qkv_weight, bias, bufs, buf_shapes):
    micro, seq_len, width_model = layer_in.shape
    qkv_cols = qkv_weight.shape[1]
    ctx_cols = buf_shapes[1][2]
    heads = bias.shape[0]
    anyspec = pl.BlockSpec(memory_space=pl.ANY)
    flops = 2 * seq_len * width_model * qkv_cols + 4 * 2 * seq_len * seq_len * ctx_cols
    grid_spec = pltpu.PrefetchScalarGridSpec(
        num_scalar_prefetch=1,
        grid=(1,),
        in_specs=[
            slot_spec(1, seq_len, width_model),
            full_spec((1, width_model)),
            full_spec(qkv_weight.shape),
            full_spec(bias.shape),
        ] + ([anyspec, anyspec] if bufs is not None else []),
        out_specs=[
            full_spec((seq_len, qkv_cols)),
            full_spec((heads, seq_len, seq_len)),
            slot_spec(0, seq_len, width_model),
            slot_spec(0, seq_len, ctx_cols),
        ],
    )
    if bufs is None:
        kernel = lambda a, b, c, d, e, *outs: forward_kernel(a, b, c, d, e, None, None, *outs)
        extra, aliases = (), {}
    else:
        kernel, extra, aliases = forward_kernel, tuple(bufs), {5: 2, 6: 3}
    return pl.pallas_call(
        kernel,
        grid_spec=grid_spec,
        out_shape=(
            jax.ShapeDtypeStruct((seq_len, qkv_cols), BF16),
            jax.ShapeDtypeStruct((heads, seq_len, seq_len), F32),
            *[jax.ShapeDtypeStruct(shape, BF16) for shape in buf_shapes],
        ),
        input_output_aliases=aliases,
        cost_estimate=pl.CostEstimate(
            flops=flops, transcendentals=bias.size, bytes_accessed=8 * 1024 * 1024),
        name="attention_forward",
    )(sc, layer_in, gain_row, qkv_weight, bias, *extra)


def attention_backward(sc, layer_in, cotangent, received, gain_row, qkv_weight, out_weight,
                       qkv, probs, bufs, buf_shapes):
    micro, seq_len, width_model = layer_in.shape
    qkv_cols = qkv_weight.shape[1]
    ctx_cols = out_weight.shape[0]
    anyspec = pl.BlockSpec(memory_space=pl.ANY)
    flops = 2 * seq_len * width_model * (qkv_cols + ctx_cols) + 8 * 2 * seq_len * seq_len * ctx_cols
    grid_spec = pltpu.PrefetchScalarGridSpec(
        num_scalar_prefetch=1,
        grid=(1,),
        in_specs=[
            slot_spec(1, seq_len, width_model),
            slot_spec(2, seq_len, width_model),
            full_spec((seq_len, width_model)),
            full_spec((1, width_model)),
            full_spec(qkv_weight.shape),
            full_spec(out_weight.shape),
            full_spec(qkv.shape),
            full_spec(probs.shape),
        ] + ([anyspec, anyspec, anyspec] if bufs is not None else []),
        out_specs=[
            full_spec((seq_len, width_model)),
            slot_spec(0, seq_len, width_model),
            slot_spec(0, seq_len, qkv_cols),
            slot_spec(0, seq_len, width_model),
            full_spec((1, width_model)),
        ],
        scratch_shapes=[pltpu.VMEM((seq_len, ctx_cols), BF16)],
    )
    if bufs is None:
        kernel = lambda *refs: backward_kernel(*refs[:9], None, None, None, *refs[9:])
        extra, aliases = (), {}
    else:
        kernel, extra, aliases = backward_kernel, tuple(bufs), {9: 1, 10: 2, 11: 3}
    return pl.pallas_call(
        kernel,
        grid_spec=grid_spec,
        out_shape=(
            jax.ShapeDtypeStruct((seq_len, width_model), BF16),
            *[jax.ShapeDtypeStruct(shape, BF16) for shape in buf_shapes],
            jax.ShapeDtypeStruct((1, width_model), F32),
        ),
        input_output_aliases=aliases,
        name="attention_backward",
        cost_estimate=pl.CostEstimate(
            flops=flops, transcendentals=0, bytes_accessed=10 * 1024 * 1024),
    )(sc, layer_in, cotangent, received, gain_row, qkv_weight, out_weight, qkv, probs, *extra)


def on_device(
    segment_inputs, cotangent, order, norm_gain, w_qkv, w_out, global_blocks, random_blocks
):
    segments = lax.axis_size("segment")
    my_segment = lax.axis_index("segment")
    layer_in = segment_inputs[0]
    micro_count = layer_in.shape[0]
    seq_len = layer_in.shape[1]
    width_model = layer_in.shape[2]
    gain_row = norm_gain[0][None, :]
    qkv_weight = w_qkv[0]
    out_weight = w_out[0]
    slot_order = order[0]
    block_total = seq_len // BLOCK
    block_index, usable = block_ids(global_blocks[0], random_blocks[0], block_total)
    bias = dense_bias(block_index, usable, block_total, seq_len)
    dp_size = lax.axis_size("z") * lax.axis_size("y") * lax.axis_size("core")
    grad_scale = 1.0 / math.sqrt(dp_size * micro_count * seq_len)
    qkv_cols = qkv_weight.shape[1]
    ctx_cols = out_weight.shape[0]

    slots = micro_count + 1
    fwd_shapes = ((slots, seq_len, width_model), (slots, seq_len, ctx_cols))
    bwd_shapes = ((slots, seq_len, width_model), (slots, seq_len, qkv_cols), (slots, seq_len, width_model))
    fwd_bufs = None
    bwd_bufs = None
    gain_total = jnp.zeros((1, width_model), F32)
    received = cotangent[0]
    last_tick = micro_count + segments - 1
    use_cot = (my_segment == segments - 1).astype(jnp.int32)
    for timestep in range(last_tick):
        slot_now = timestep - (segments - 1) + my_segment
        active = (slot_now >= 0) & (slot_now < micro_count)
        slot_clip = jnp.clip(slot_now, 0, micro_count - 1)
        batch_id = slot_order[slot_clip]
        write_id = jnp.where(active, batch_id, jnp.int32(micro_count))
        sc = jnp.stack([write_id, batch_id, slot_clip, use_cot]).astype(jnp.int32)
        qkv, probs, normed_buf, ctx_buf = attention_forward(
            sc, layer_in, gain_row, qkv_weight, bias, fwd_bufs, fwd_shapes)
        fwd_bufs = (normed_buf, ctx_buf)
        grad_in, grad_x, rows_buf, upper_buf, part_gain = attention_backward(
            sc, layer_in, cotangent, received, gain_row, qkv_weight, out_weight, qkv, probs,
            bwd_bufs, bwd_shapes,
        )
        bwd_bufs = (grad_x, rows_buf, upper_buf)
        gain_total = gain_total + jnp.where(active, part_gain, jnp.zeros_like(part_gain))
        if timestep + 1 < last_tick:
            received = from_behind(grad_in, "segment", -1)
    all_normed = normed_buf[:micro_count].reshape(micro_count * seq_len, width_model)
    all_rows = rows_buf[:micro_count].reshape(micro_count * seq_len, qkv_cols)
    all_ctx = ctx_buf[:micro_count].reshape(micro_count * seq_len, ctx_cols)
    all_upper = upper_buf[:micro_count].reshape(micro_count * seq_len, width_model)
    sum_qkv = lax.dot_general(all_normed, all_rows, TN, preferred_element_type=F32)
    sum_out = lax.dot_general(all_ctx, all_upper, TN, preferred_element_type=F32)
    rows_total = qkv_weight.shape[0]
    fold = rows_total // ctx_cols
    out_folded = sum_out.reshape(rows_total, ctx_cols * width_model // rows_total)
    gain_col = gain_total.reshape(rows_total, width_model // rows_total)
    pad = jnp.zeros((rows_total, 128 - gain_col.shape[1]), BF16)
    out_gain = jnp.concatenate(
        [(out_folded * grad_scale).astype(BF16), (gain_col * grad_scale).astype(BF16), pad], axis=1)
    qkv_share, out_gain_share = dp_reduce_scatter((sum_qkv * grad_scale).astype(BF16), out_gain)
    share = jnp.concatenate([qkv_share, out_gain_share], axis=1)
    share_rows = share.shape[0]
    qkv_share = share[:, :qkv_cols]
    out_share = share[:, qkv_cols:qkv_cols + out_folded.shape[1]].reshape(share_rows // fold, width_model)
    gain_share = share[:, qkv_cols + out_folded.shape[1]:qkv_cols + out_folded.shape[1] + gain_col.shape[1]].reshape(-1)
    return (grad_x[:micro_count][None], qkv_share[None], out_share[None], gain_share[None])


def solution(mesh):
    dp = ("z", "y", "core")
    segs = mesh.shape["segment"]
    cores = 2
    ys = 4
    zs = mesh.shape["dp"] // (cores * ys)
    mesh4 = Mesh(mesh.devices.reshape(segs, zs, ys, cores), ("segment", "z", "y", "core"))
    in_specs = (
        P("segment", dp, None, None),
        P(dp, None, None),
        P(dp, None),
        P("segment", None),
        P("segment", None, None),
        P("segment", None, None),
        P("segment", None),
        P("segment", None, None, None),
    )
    out_specs = (
        P("segment", dp, None, None),
        P("segment", dp, None),
        P("segment", dp, None),
        P("segment", dp),
    )
    return jax.shard_map(
        on_device, mesh=mesh4, in_specs=in_specs, out_specs=out_specs, check_vma=False
    )
```

```python
import math

import jax
import jax.numpy as jnp
from jax import lax
from jax.experimental import pallas as pl
from jax.experimental.pallas import tpu as pltpu
from jax.sharding import Mesh, PartitionSpec as P

BLOCK = 64
HEAD_DIM = 64
EPS = 1e-05
F32 = jnp.float32
BF16 = jnp.bfloat16
NT = (((1,), (1,)), ((), ()))
TN = (((0,), (0,)), ((), ()))


def from_behind(value, axis, by):
    count = lax.axis_size(axis)
    pairs = [(i, i + by) for i in range(count) if 0 <= i + by < count]
    return lax.ppermute(value, axis, pairs)


def block_ids(glob_ids, rand_ids, block_count):
    head_count = rand_ids.shape[0]
    block_rows = jnp.arange(block_count, dtype=jnp.int32)
    window = block_rows[:, None] + jnp.arange(-1, 2, dtype=jnp.int32)[None, :]
    inside = (window >= 0) & (window < block_count)
    window_ids = jnp.where(inside, window, jnp.int32(-1))
    global_ids = jnp.broadcast_to(glob_ids[None, :], (block_count, glob_ids.shape[0]))
    fixed_ids = jnp.concatenate([window_ids, global_ids], axis=1)
    fixed_ids = jnp.broadcast_to(fixed_ids[None], (head_count, block_count, fixed_ids.shape[1]))
    listed_blocks = jnp.concatenate([fixed_ids, rand_ids], axis=2)
    list_len = listed_blocks.shape[2]
    earlier = (
        jnp.arange(list_len, dtype=jnp.int32)[:, None]
        > jnp.arange(list_len, dtype=jnp.int32)[None, :]
    )
    equal_prior = (listed_blocks[..., :, None] == listed_blocks[..., None, :]) & earlier
    repeated = jnp.any(equal_prior, axis=-1)
    usable = (listed_blocks >= 0) & jnp.logical_not(repeated)
    block_index = jnp.clip(listed_blocks, 0, block_count - 1)
    return (block_index, usable)


def halving(cur, steps):
    for axis, dim, bit in steps:
        n = lax.axis_size(axis)
        half = cur.shape[dim] // 2
        mybit = (lax.axis_index(axis) // bit) % 2
        keep = lax.dynamic_slice_in_dim(cur, mybit * half, half, axis=dim)
        send = lax.dynamic_slice_in_dim(cur, (1 - mybit) * half, half, axis=dim)
        recv = lax.ppermute(send.astype(BF16), axis, [(i, i ^ bit) for i in range(n)])
        cur = keep.astype(F32) + recv.astype(F32)
    return cur


def dp_reduce_scatter(first, second):
    cores = lax.axis_size("core")
    ys = lax.axis_size("y")
    zs = lax.axis_size("z")
    chunk = first.shape[0] // (zs * ys * cores)
    z_steps = [("z", 0, zs // 2 ** (k + 1)) for k in range(int(math.log2(zs)))]
    y_steps = [("y", 1, ys // 2 ** (k + 1)) for k in range(int(math.log2(ys)))]
    views = [part.reshape(zs, ys, cores, chunk, part.shape[1]) for part in (first, second)]
    mybit = lax.axis_index("core") % 2
    keeps = [lax.dynamic_slice_in_dim(v, mybit, 1, axis=2) for v in views]
    sends = tuple(lax.dynamic_slice_in_dim(v, 1 - mybit, 1, axis=2).astype(BF16) for v in views)
    recvs = lax.ppermute(sends, "core", [(i, i ^ 1) for i in range(cores)])
    outs = []
    for keep, recv, steps in zip(keeps, recvs, (z_steps + y_steps, y_steps + z_steps)):
        cur = keep.astype(F32) + recv.astype(F32)
        outs.append(halving(cur, steps).reshape(chunk, cur.shape[-1]))
    return outs


def dense_bias(block_index, usable, block_count, seq_len):
    names = block_index[..., None] == jnp.arange(block_count, dtype=jnp.int32)
    allowed = jnp.any(names & usable[..., None], axis=2)
    small = jnp.where(allowed, F32(0.0), F32(-1e30)).astype(BF16)
    extent = seq_len // block_count
    return jnp.repeat(jnp.repeat(small, extent, axis=1), extent, axis=2)


def forward_kernel(sc_ref, x_ref, gain_ref, wqkv_ref, bias_ref, nb_in, cb_in,
                   qkv_ref, p_ref, normed_ref, ctx_ref):
    del sc_ref, nb_in, cb_in
    width = ctx_ref.shape[1]
    pair_w = 2 * HEAD_DIM
    scale = 1.0 / math.sqrt(HEAD_DIM)
    x = x_ref[...].astype(F32)
    mean = jnp.mean(x, axis=-1, keepdims=True)
    cen = x - mean
    inv = lax.rsqrt(jnp.mean(cen * cen, axis=-1, keepdims=True) + EPS)
    normed = (cen * inv * gain_ref[...]).astype(BF16)
    normed_ref[...] = normed
    qkv_ref[...] = jnp.dot(normed, wqkv_ref[...], preferred_element_type=F32).astype(BF16)
    lane = lax.broadcasted_iota(jnp.int32, (1, pair_w), 1)
    low = lane < HEAD_DIM
    for pair in range(width // pair_w):
        q2 = qkv_ref[:, pl.ds(pair * pair_w, pair_w)]
        k2 = qkv_ref[:, pl.ds(width + pair * pair_w, pair_w)]
        v2 = qkv_ref[:, pl.ds(2 * width + pair * pair_w, pair_w)]
        ctxs = []
        for half in range(2):
            mine = low if half == 0 else jnp.logical_not(low)
            qh = jnp.where(mine, q2, jnp.zeros_like(q2))
            s = lax.dot_general(qh, k2, NT, preferred_element_type=F32) * scale
            s = s + bias_ref[2 * pair + half]
            m = jnp.max(s, axis=-1, keepdims=True)
            e = jnp.exp(s - m)
            p = e / jnp.sum(e, axis=-1, keepdims=True)
            p_ref[2 * pair + half] = p
            ctxs.append(jnp.dot(p.astype(BF16), v2, preferred_element_type=F32))
        ctx_ref[:, pl.ds(pair * pair_w, pair_w)] = jnp.where(low, ctxs[0], ctxs[1]).astype(BF16)


def backward_kernel(sc_ref, x_ref, cot_ref, recv_ref, gain_ref, wqkv_ref, wout_ref, qkv_ref, p_ref,
                    gx_in, rb_in, ub_in,
                    gin_ref, gx_ref, rows_ref, upper_ref, pgain_ref, gctx_scr):
    del gx_in, rb_in, ub_in
    width = gctx_scr.shape[1]
    pair_w = 2 * HEAD_DIM
    scale = 1.0 / math.sqrt(HEAD_DIM)
    gy = jnp.where(sc_ref[3] > 0, cot_ref[...], recv_ref[...])
    upper_ref[...] = gy
    gctx_scr[...] = lax.dot_general(
        gy, wout_ref[...], NT, preferred_element_type=F32).astype(BF16)
    lane = lax.broadcasted_iota(jnp.int32, (1, pair_w), 1)
    low = lane < HEAD_DIM
    for pair in range(width // pair_w):
        cols = pl.ds(pair * pair_w, pair_w)
        q2 = qkv_ref[:, pl.ds(pair * pair_w, pair_w)]
        k2 = qkv_ref[:, pl.ds(width + pair * pair_w, pair_w)]
        v2 = qkv_ref[:, pl.ds(2 * width + pair * pair_w, pair_w)]
        g2 = gctx_scr[:, cols]
        outs = []
        for half in range(2):
            mine = low if half == 0 else jnp.logical_not(low)
            gh = jnp.where(mine, g2, jnp.zeros_like(g2))
            p = p_ref[2 * pair + half]
            pb = p.astype(BF16)
            dp = lax.dot_general(gh, v2, NT, preferred_element_type=F32).astype(BF16).astype(F32)
            rd = jnp.sum(dp * p, axis=-1, keepdims=True)
            ds = (p * (dp - rd) * scale).astype(BF16)
            dq = jnp.dot(ds, k2, preferred_element_type=F32)
            dk = lax.dot_general(ds, q2, TN, preferred_element_type=F32)
            dv = lax.dot_general(pb, g2, TN, preferred_element_type=F32)
            outs.append((dq, dk, dv))
        lo, hi = outs
        rows_ref[:, pl.ds(pair * pair_w, pair_w)] = jnp.where(low, lo[0], hi[0]).astype(BF16)
        rows_ref[:, pl.ds(width + pair * pair_w, pair_w)] = jnp.where(low, lo[1], hi[1]).astype(BF16)
        rows_ref[:, pl.ds(2 * width + pair * pair_w, pair_w)] = jnp.where(low, lo[2], hi[2]).astype(BF16)
    gn = lax.dot_general(rows_ref[...], wqkv_ref[...], NT, preferred_element_type=F32)
    x = x_ref[...].astype(F32)
    mean = jnp.mean(x, axis=-1, keepdims=True)
    cen = x - mean
    inv = lax.rsqrt(jnp.mean(cen * cen, axis=-1, keepdims=True) + EPS)
    xn = cen * inv
    pgain_ref[...] = jnp.sum(gn * xn, axis=0, keepdims=True)
    gh = gn * gain_ref[...]
    gin = gy.astype(F32) + inv * (
        gh
        - jnp.mean(gh, axis=-1, keepdims=True)
        - xn * jnp.mean(gh * xn, axis=-1, keepdims=True)
    )
    gin = gin.astype(BF16)
    gin_ref[...] = gin
    gx_ref[...] = gin


def full_spec(shape):
    return pl.BlockSpec(shape, lambda i, sc: (0,) * len(shape))


def slot_spec(k, rows, cols):
    return pl.BlockSpec((None, rows, cols), lambda i, sc: (sc[k], 0, 0))


def attention_forward(sc, layer_in, gain_row, qkv_weight, bias, bufs, buf_shapes):
    micro, seq_len, width_model = layer_in.shape
    qkv_cols = qkv_weight.shape[1]
    ctx_cols = buf_shapes[1][2]
    heads = bias.shape[0]
    anyspec = pl.BlockSpec(memory_space=pl.ANY)
    flops = 2 * seq_len * width_model * qkv_cols + 4 * 2 * seq_len * seq_len * ctx_cols
    grid_spec = pltpu.PrefetchScalarGridSpec(
        num_scalar_prefetch=1,
        grid=(1,),
        in_specs=[
            slot_spec(1, seq_len, width_model),
            full_spec((1, width_model)),
            full_spec(qkv_weight.shape),
            full_spec(bias.shape),
        ] + ([anyspec, anyspec] if bufs is not None else []),
        out_specs=[
            full_spec((seq_len, qkv_cols)),
            full_spec((heads, seq_len, seq_len)),
            slot_spec(0, seq_len, width_model),
            slot_spec(0, seq_len, ctx_cols),
        ],
    )
    if bufs is None:
        kernel = lambda a, b, c, d, e, *outs: forward_kernel(a, b, c, d, e, None, None, *outs)
        extra, aliases = (), {}
    else:
        kernel, extra, aliases = forward_kernel, tuple(bufs), {5: 2, 6: 3}
    return pl.pallas_call(
        kernel,
        grid_spec=grid_spec,
        out_shape=(
            jax.ShapeDtypeStruct((seq_len, qkv_cols), BF16),
            jax.ShapeDtypeStruct((heads, seq_len, seq_len), F32),
            *[jax.ShapeDtypeStruct(shape, BF16) for shape in buf_shapes],
        ),
        input_output_aliases=aliases,
        cost_estimate=pl.CostEstimate(
            flops=flops, transcendentals=bias.size, bytes_accessed=8 * 1024 * 1024),
        name="attention_forward",
    )(sc, layer_in, gain_row, qkv_weight, bias, *extra)


def attention_backward(sc, layer_in, cotangent, received, gain_row, qkv_weight, out_weight,
                       qkv, probs, bufs, buf_shapes):
    micro, seq_len, width_model = layer_in.shape
    qkv_cols = qkv_weight.shape[1]
    ctx_cols = out_weight.shape[0]
    anyspec = pl.BlockSpec(memory_space=pl.ANY)
    flops = 2 * seq_len * width_model * (qkv_cols + ctx_cols) + 8 * 2 * seq_len * seq_len * ctx_cols
    grid_spec = pltpu.PrefetchScalarGridSpec(
        num_scalar_prefetch=1,
        grid=(1,),
        in_specs=[
            slot_spec(1, seq_len, width_model),
            slot_spec(2, seq_len, width_model),
            full_spec((seq_len, width_model)),
            full_spec((1, width_model)),
            full_spec(qkv_weight.shape),
            full_spec(out_weight.shape),
            full_spec(qkv.shape),
            full_spec(probs.shape),
        ] + ([anyspec, anyspec, anyspec] if bufs is not None else []),
        out_specs=[
            full_spec((seq_len, width_model)),
            slot_spec(0, seq_len, width_model),
            slot_spec(0, seq_len, qkv_cols),
            slot_spec(0, seq_len, width_model),
            full_spec((1, width_model)),
        ],
        scratch_shapes=[pltpu.VMEM((seq_len, ctx_cols), BF16)],
    )
    if bufs is None:
        kernel = lambda *refs: backward_kernel(*refs[:9], None, None, None, *refs[9:])
        extra, aliases = (), {}
    else:
        kernel, extra, aliases = backward_kernel, tuple(bufs), {9: 1, 10: 2, 11: 3}
    return pl.pallas_call(
        kernel,
        grid_spec=grid_spec,
        out_shape=(
            jax.ShapeDtypeStruct((seq_len, width_model), BF16),
            *[jax.ShapeDtypeStruct(shape, BF16) for shape in buf_shapes],
            jax.ShapeDtypeStruct((1, width_model), F32),
        ),
        input_output_aliases=aliases,
        name="attention_backward",
        cost_estimate=pl.CostEstimate(
            flops=flops, transcendentals=0, bytes_accessed=10 * 1024 * 1024),
    )(sc, layer_in, cotangent, received, gain_row, qkv_weight, out_weight, qkv, probs, *extra)


def on_device(
    segment_inputs, cotangent, order, norm_gain, w_qkv, w_out, global_blocks, random_blocks
):
    segments = lax.axis_size("segment")
    my_segment = lax.axis_index("segment")
    layer_in = segment_inputs[0]
    micro_count = layer_in.shape[0]
    seq_len = layer_in.shape[1]
    width_model = layer_in.shape[2]
    gain_row = norm_gain[0][None, :]
    qkv_weight = w_qkv[0]
    out_weight = w_out[0]
    slot_order = order[0]
    block_total = seq_len // BLOCK
    block_index, usable = block_ids(global_blocks[0], random_blocks[0], block_total)
    bias = dense_bias(block_index, usable, block_total, seq_len)
    dp_size = lax.axis_size("z") * lax.axis_size("y") * lax.axis_size("core")
    grad_scale = 1.0 / math.sqrt(dp_size * micro_count * seq_len)
    qkv_cols = qkv_weight.shape[1]
    ctx_cols = out_weight.shape[0]

    slots = micro_count + 1
    fwd_shapes = ((slots, seq_len, width_model), (slots, seq_len, ctx_cols))
    bwd_shapes = ((slots, seq_len, width_model), (slots, seq_len, qkv_cols), (slots, seq_len, width_model))
    fwd_bufs = None
    bwd_bufs = None
    gain_total = jnp.zeros((1, width_model), F32)
    received = cotangent[0]
    last_tick = micro_count + segments - 1
    use_cot = (my_segment == segments - 1).astype(jnp.int32)
    for timestep in range(last_tick):
        slot_now = timestep - (segments - 1) + my_segment
        active = (slot_now >= 0) & (slot_now < micro_count)
        slot_clip = jnp.clip(slot_now, 0, micro_count - 1)
        batch_id = slot_order[slot_clip]
        write_id = jnp.where(active, batch_id, jnp.int32(micro_count))
        sc = jnp.stack([write_id, batch_id, slot_clip, use_cot]).astype(jnp.int32)
        qkv, probs, normed_buf, ctx_buf = attention_forward(
            sc, layer_in, gain_row, qkv_weight, bias, fwd_bufs, fwd_shapes)
        fwd_bufs = (normed_buf, ctx_buf)
        grad_in, grad_x, rows_buf, upper_buf, part_gain = attention_backward(
            sc, layer_in, cotangent, received, gain_row, qkv_weight, out_weight, qkv, probs,
            bwd_bufs, bwd_shapes,
        )
        bwd_bufs = (grad_x, rows_buf, upper_buf)
        gain_total = gain_total + jnp.where(active, part_gain, jnp.zeros_like(part_gain))
        if timestep + 1 < last_tick:
            received = from_behind(grad_in, "segment", -1)
    all_normed = normed_buf[:micro_count].reshape(micro_count * seq_len, width_model)
    all_rows = rows_buf[:micro_count].reshape(micro_count * seq_len, qkv_cols)
    all_ctx = ctx_buf[:micro_count].reshape(micro_count * seq_len, ctx_cols)
    all_upper = upper_buf[:micro_count].reshape(micro_count * seq_len, width_model)
    sum_qkv = lax.dot_general(all_normed, all_rows, TN, preferred_element_type=F32)
    sum_out = lax.dot_general(all_ctx, all_upper, TN, preferred_element_type=F32)
    rows_total = qkv_weight.shape[0]
    fold = rows_total // ctx_cols
    out_folded = sum_out.reshape(rows_total, ctx_cols * width_model // rows_total)
    gain_col = gain_total.reshape(rows_total, width_model // rows_total)
    pad = jnp.zeros((rows_total, 128 - gain_col.shape[1]), BF16)
    out_gain = jnp.concatenate(
        [(out_folded * grad_scale).astype(BF16), (gain_col * grad_scale).astype(BF16), pad], axis=1)
    qkv_share, out_gain_share = dp_reduce_scatter((sum_qkv * grad_scale).astype(BF16), out_gain)
    share = jnp.concatenate([qkv_share, out_gain_share], axis=1)
    share_rows = share.shape[0]
    qkv_share = share[:, :qkv_cols]
    out_share = share[:, qkv_cols:qkv_cols + out_folded.shape[1]].reshape(share_rows // fold, width_model)
    gain_share = share[:, qkv_cols + out_folded.shape[1]:qkv_cols + out_folded.shape[1] + gain_col.shape[1]].reshape(-1)
    return (grad_x[:micro_count][None], qkv_share[None], out_share[None], gain_share[None])


def solution(mesh):
    dp = ("z", "y", "core")
    segs = mesh.shape["segment"]
    cores = 2
    ys = 4
    zs = mesh.shape["dp"] // (cores * ys)
    mesh4 = Mesh(mesh.devices.reshape(segs, zs, ys, cores), ("segment", "z", "y", "core"))
    in_specs = (
        P("segment", dp, None, None),
        P(dp, None, None),
        P(dp, None),
        P("segment", None),
        P("segment", None, None),
        P("segment", None, None),
        P("segment", None),
        P("segment", None, None, None),
    )
    out_specs = (
        P("segment", dp, None, None),
        P("segment", dp, None),
        P("segment", dp, None),
        P("segment", dp),
    )
    return jax.shard_map(
        on_device, mesh=mesh4, in_specs=in_specs, out_specs=out_specs, check_vma=False
    )
```

```python
import math

import jax
import jax.numpy as jnp
from jax import lax
from jax.experimental import pallas as pl
from jax.experimental.pallas import tpu as pltpu
from jax.sharding import Mesh, PartitionSpec as P

BLOCK = 64
HEAD_DIM = 64
EPS = 1e-05
F32 = jnp.float32
BF16 = jnp.bfloat16
NT = (((1,), (1,)), ((), ()))
TN = (((0,), (0,)), ((), ()))


def from_behind(value, axis, by):
    count = lax.axis_size(axis)
    pairs = [(i, i + by) for i in range(count) if 0 <= i + by < count]
    return lax.ppermute(value, axis, pairs)


def block_ids(glob_ids, rand_ids, block_count):
    head_count = rand_ids.shape[0]
    block_rows = jnp.arange(block_count, dtype=jnp.int32)
    window = block_rows[:, None] + jnp.arange(-1, 2, dtype=jnp.int32)[None, :]
    inside = (window >= 0) & (window < block_count)
    window_ids = jnp.where(inside, window, jnp.int32(-1))
    global_ids = jnp.broadcast_to(glob_ids[None, :], (block_count, glob_ids.shape[0]))
    fixed_ids = jnp.concatenate([window_ids, global_ids], axis=1)
    fixed_ids = jnp.broadcast_to(fixed_ids[None], (head_count, block_count, fixed_ids.shape[1]))
    listed_blocks = jnp.concatenate([fixed_ids, rand_ids], axis=2)
    list_len = listed_blocks.shape[2]
    earlier = (
        jnp.arange(list_len, dtype=jnp.int32)[:, None]
        > jnp.arange(list_len, dtype=jnp.int32)[None, :]
    )
    equal_prior = (listed_blocks[..., :, None] == listed_blocks[..., None, :]) & earlier
    repeated = jnp.any(equal_prior, axis=-1)
    usable = (listed_blocks >= 0) & jnp.logical_not(repeated)
    block_index = jnp.clip(listed_blocks, 0, block_count - 1)
    return (block_index, usable)


def halving(cur, steps):
    for axis, dim, bit in steps:
        n = lax.axis_size(axis)
        half = cur.shape[dim] // 2
        mybit = (lax.axis_index(axis) // bit) % 2
        keep = lax.dynamic_slice_in_dim(cur, mybit * half, half, axis=dim)
        send = lax.dynamic_slice_in_dim(cur, (1 - mybit) * half, half, axis=dim)
        recv = lax.ppermute(send.astype(BF16), axis, [(i, i ^ bit) for i in range(n)])
        cur = keep.astype(F32) + recv.astype(F32)
    return cur


def dp_reduce_scatter(first, second):
    cores = lax.axis_size("core")
    ys = lax.axis_size("y")
    zs = lax.axis_size("z")
    chunk = first.shape[0] // (zs * ys * cores)
    z_steps = [("z", 0, zs // 2 ** (k + 1)) for k in range(int(math.log2(zs)))]
    y_steps = [("y", 1, ys // 2 ** (k + 1)) for k in range(int(math.log2(ys)))]
    views = [part.reshape(zs, ys, cores, chunk, part.shape[1]) for part in (first, second)]
    mybit = lax.axis_index("core") % 2
    keeps = [lax.dynamic_slice_in_dim(v, mybit, 1, axis=2) for v in views]
    sends = tuple(lax.dynamic_slice_in_dim(v, 1 - mybit, 1, axis=2).astype(BF16) for v in views)
    recvs = lax.ppermute(sends, "core", [(i, i ^ 1) for i in range(cores)])
    outs = []
    for keep, recv, steps in zip(keeps, recvs, (z_steps + y_steps, y_steps + z_steps)):
        cur = keep.astype(F32) + recv.astype(F32)
        outs.append(halving(cur, steps).reshape(chunk, cur.shape[-1]))
    return outs


def dense_bias(block_index, usable, block_count, seq_len):
    names = block_index[..., None] == jnp.arange(block_count, dtype=jnp.int32)
    allowed = jnp.any(names & usable[..., None], axis=2)
    small = jnp.where(allowed, F32(0.0), F32(-1e30)).astype(BF16)
    extent = seq_len // block_count
    return jnp.repeat(jnp.repeat(small, extent, axis=1), extent, axis=2)


def forward_kernel(sc_ref, x_ref, gain_ref, wqkv_ref, bias_ref, nb_in, cb_in,
                   qkv_ref, p_ref, normed_ref, ctx_ref):
    del sc_ref, nb_in, cb_in
    width = ctx_ref.shape[1]
    pair_w = 2 * HEAD_DIM
    scale = 1.0 / math.sqrt(HEAD_DIM)
    x = x_ref[...].astype(F32)
    mean = jnp.mean(x, axis=-1, keepdims=True)
    cen = x - mean
    inv = lax.rsqrt(jnp.mean(cen * cen, axis=-1, keepdims=True) + EPS)
    normed = (cen * inv * gain_ref[...]).astype(BF16)
    normed_ref[...] = normed
    qkv_ref[...] = jnp.dot(normed, wqkv_ref[...], preferred_element_type=F32).astype(BF16)
    lane = lax.broadcasted_iota(jnp.int32, (1, pair_w), 1)
    low = lane < HEAD_DIM
    for pair in range(width // pair_w):
        q2 = qkv_ref[:, pl.ds(pair * pair_w, pair_w)]
        k2 = qkv_ref[:, pl.ds(width + pair * pair_w, pair_w)]
        v2 = qkv_ref[:, pl.ds(2 * width + pair * pair_w, pair_w)]
        ctxs = []
        for half in range(2):
            mine = low if half == 0 else jnp.logical_not(low)
            qh = jnp.where(mine, q2, jnp.zeros_like(q2))
            s = lax.dot_general(qh, k2, NT, preferred_element_type=F32) * scale
            s = s + bias_ref[2 * pair + half]
            m = jnp.max(s, axis=-1, keepdims=True)
            e = jnp.exp(s - m)
            p = e / jnp.sum(e, axis=-1, keepdims=True)
            p_ref[2 * pair + half] = p
            ctxs.append(jnp.dot(p.astype(BF16), v2, preferred_element_type=F32))
        ctx_ref[:, pl.ds(pair * pair_w, pair_w)] = jnp.where(low, ctxs[0], ctxs[1]).astype(BF16)


def backward_kernel(sc_ref, x_ref, cot_ref, recv_ref, gain_ref, wqkv_ref, wout_ref, qkv_ref, p_ref,
                    gx_in, rb_in, ub_in,
                    gin_ref, gx_ref, rows_ref, upper_ref, pgain_ref, gctx_scr):
    del gx_in, rb_in, ub_in
    width = gctx_scr.shape[1]
    pair_w = 2 * HEAD_DIM
    scale = 1.0 / math.sqrt(HEAD_DIM)
    gy = jnp.where(sc_ref[3] > 0, cot_ref[...], recv_ref[...])
    upper_ref[...] = gy
    gctx_scr[...] = lax.dot_general(
        gy, wout_ref[...], NT, preferred_element_type=F32).astype(BF16)
    lane = lax.broadcasted_iota(jnp.int32, (1, pair_w), 1)
    low = lane < HEAD_DIM
    for pair in range(width // pair_w):
        cols = pl.ds(pair * pair_w, pair_w)
        q2 = qkv_ref[:, pl.ds(pair * pair_w, pair_w)]
        k2 = qkv_ref[:, pl.ds(width + pair * pair_w, pair_w)]
        v2 = qkv_ref[:, pl.ds(2 * width + pair * pair_w, pair_w)]
        g2 = gctx_scr[:, cols]
        outs = []
        for half in range(2):
            mine = low if half == 0 else jnp.logical_not(low)
            gh = jnp.where(mine, g2, jnp.zeros_like(g2))
            p = p_ref[2 * pair + half]
            pb = p.astype(BF16)
            dp = lax.dot_general(gh, v2, NT, preferred_element_type=F32).astype(BF16).astype(F32)
            rd = jnp.sum(dp * p, axis=-1, keepdims=True)
            ds = (p * (dp - rd) * scale).astype(BF16)
            dq = jnp.dot(ds, k2, preferred_element_type=F32)
            dk = lax.dot_general(ds, q2, TN, preferred_element_type=F32)
            dv = lax.dot_general(pb, g2, TN, preferred_element_type=F32)
            outs.append((dq, dk, dv))
        lo, hi = outs
        rows_ref[:, pl.ds(pair * pair_w, pair_w)] = jnp.where(low, lo[0], hi[0]).astype(BF16)
        rows_ref[:, pl.ds(width + pair * pair_w, pair_w)] = jnp.where(low, lo[1], hi[1]).astype(BF16)
        rows_ref[:, pl.ds(2 * width + pair * pair_w, pair_w)] = jnp.where(low, lo[2], hi[2]).astype(BF16)
    gn = lax.dot_general(rows_ref[...], wqkv_ref[...], NT, preferred_element_type=F32)
    x = x_ref[...].astype(F32)
    mean = jnp.mean(x, axis=-1, keepdims=True)
    cen = x - mean
    inv = lax.rsqrt(jnp.mean(cen * cen, axis=-1, keepdims=True) + EPS)
    xn = cen * inv
    pgain_ref[...] = jnp.sum(gn * xn, axis=0, keepdims=True)
    gh = gn * gain_ref[...]
    gin = gy.astype(F32) + inv * (
        gh
        - jnp.mean(gh, axis=-1, keepdims=True)
        - xn * jnp.mean(gh * xn, axis=-1, keepdims=True)
    )
    gin = gin.astype(BF16)
    gin_ref[...] = gin
    gx_ref[...] = gin


def full_spec(shape):
    return pl.BlockSpec(shape, lambda i, sc: (0,) * len(shape))


def slot_spec(k, rows, cols):
    return pl.BlockSpec((None, rows, cols), lambda i, sc: (sc[k], 0, 0))


def attention_forward(sc, layer_in, gain_row, qkv_weight, bias, bufs, buf_shapes):
    micro, seq_len, width_model = layer_in.shape
    qkv_cols = qkv_weight.shape[1]
    ctx_cols = buf_shapes[1][2]
    heads = bias.shape[0]
    anyspec = pl.BlockSpec(memory_space=pl.ANY)
    flops = 2 * seq_len * width_model * qkv_cols + 4 * 2 * seq_len * seq_len * ctx_cols
    grid_spec = pltpu.PrefetchScalarGridSpec(
        num_scalar_prefetch=1,
        grid=(1,),
        in_specs=[
            slot_spec(1, seq_len, width_model),
            full_spec((1, width_model)),
            full_spec(qkv_weight.shape),
            full_spec(bias.shape),
        ] + ([anyspec, anyspec] if bufs is not None else []),
        out_specs=[
            full_spec((seq_len, qkv_cols)),
            full_spec((heads, seq_len, seq_len)),
            slot_spec(0, seq_len, width_model),
            slot_spec(0, seq_len, ctx_cols),
        ],
    )
    if bufs is None:
        kernel = lambda a, b, c, d, e, *outs: forward_kernel(a, b, c, d, e, None, None, *outs)
        extra, aliases = (), {}
    else:
        kernel, extra, aliases = forward_kernel, tuple(bufs), {5: 2, 6: 3}
    return pl.pallas_call(
        kernel,
        grid_spec=grid_spec,
        out_shape=(
            jax.ShapeDtypeStruct((seq_len, qkv_cols), BF16),
            jax.ShapeDtypeStruct((heads, seq_len, seq_len), F32),
            *[jax.ShapeDtypeStruct(shape, BF16) for shape in buf_shapes],
        ),
        input_output_aliases=aliases,
        cost_estimate=pl.CostEstimate(
            flops=flops, transcendentals=bias.size, bytes_accessed=8 * 1024 * 1024),
        name="attention_forward",
    )(sc, layer_in, gain_row, qkv_weight, bias, *extra)


def attention_backward(sc, layer_in, cotangent, received, gain_row, qkv_weight, out_weight,
                       qkv, probs, bufs, buf_shapes):
    micro, seq_len, width_model = layer_in.shape
    qkv_cols = qkv_weight.shape[1]
    ctx_cols = out_weight.shape[0]
    anyspec = pl.BlockSpec(memory_space=pl.ANY)
    flops = 2 * seq_len * width_model * (qkv_cols + ctx_cols) + 8 * 2 * seq_len * seq_len * ctx_cols
    grid_spec = pltpu.PrefetchScalarGridSpec(
        num_scalar_prefetch=1,
        grid=(1,),
        in_specs=[
            slot_spec(1, seq_len, width_model),
            slot_spec(2, seq_len, width_model),
            full_spec((seq_len, width_model)),
            full_spec((1, width_model)),
            full_spec(qkv_weight.shape),
            full_spec(out_weight.shape),
            full_spec(qkv.shape),
            full_spec(probs.shape),
        ] + ([anyspec, anyspec, anyspec] if bufs is not None else []),
        out_specs=[
            full_spec((seq_len, width_model)),
            slot_spec(0, seq_len, width_model),
            slot_spec(0, seq_len, qkv_cols),
            slot_spec(0, seq_len, width_model),
            full_spec((1, width_model)),
        ],
        scratch_shapes=[pltpu.VMEM((seq_len, ctx_cols), BF16)],
    )
    if bufs is None:
        kernel = lambda *refs: backward_kernel(*refs[:9], None, None, None, *refs[9:])
        extra, aliases = (), {}
    else:
        kernel, extra, aliases = backward_kernel, tuple(bufs), {9: 1, 10: 2, 11: 3}
    return pl.pallas_call(
        kernel,
        grid_spec=grid_spec,
        out_shape=(
            jax.ShapeDtypeStruct((seq_len, width_model), BF16),
            *[jax.ShapeDtypeStruct(shape, BF16) for shape in buf_shapes],
            jax.ShapeDtypeStruct((1, width_model), F32),
        ),
        input_output_aliases=aliases,
        name="attention_backward",
        cost_estimate=pl.CostEstimate(
            flops=flops, transcendentals=0, bytes_accessed=10 * 1024 * 1024),
    )(sc, layer_in, cotangent, received, gain_row, qkv_weight, out_weight, qkv, probs, *extra)


def on_device(
    segment_inputs, cotangent, order, norm_gain, w_qkv, w_out, global_blocks, random_blocks
):
    segments = lax.axis_size("segment")
    my_segment = lax.axis_index("segment")
    layer_in = segment_inputs[0]
    micro_count = layer_in.shape[0]
    seq_len = layer_in.shape[1]
    width_model = layer_in.shape[2]
    gain_row = norm_gain[0][None, :]
    qkv_weight = w_qkv[0]
    out_weight = w_out[0]
    slot_order = order[0]
    block_total = seq_len // BLOCK
    block_index, usable = block_ids(global_blocks[0], random_blocks[0], block_total)
    bias = dense_bias(block_index, usable, block_total, seq_len)
    dp_size = lax.axis_size("z") * lax.axis_size("y") * lax.axis_size("core")
    grad_scale = 1.0 / math.sqrt(dp_size * micro_count * seq_len)
    qkv_cols = qkv_weight.shape[1]
    ctx_cols = out_weight.shape[0]

    slots = micro_count + 1
    fwd_shapes = ((slots, seq_len, width_model), (slots, seq_len, ctx_cols))
    bwd_shapes = ((slots, seq_len, width_model), (slots, seq_len, qkv_cols), (slots, seq_len, width_model))
    fwd_bufs = None
    bwd_bufs = None
    gain_total = jnp.zeros((1, width_model), F32)
    received = cotangent[0]
    last_tick = micro_count + segments - 1
    use_cot = (my_segment == segments - 1).astype(jnp.int32)
    for timestep in range(last_tick):
        slot_now = timestep - (segments - 1) + my_segment
        active = (slot_now >= 0) & (slot_now < micro_count)
        slot_clip = jnp.clip(slot_now, 0, micro_count - 1)
        batch_id = slot_order[slot_clip]
        write_id = jnp.where(active, batch_id, jnp.int32(micro_count))
        sc = jnp.stack([write_id, batch_id, slot_clip, use_cot]).astype(jnp.int32)
        qkv, probs, normed_buf, ctx_buf = attention_forward(
            sc, layer_in, gain_row, qkv_weight, bias, fwd_bufs, fwd_shapes)
        fwd_bufs = (normed_buf, ctx_buf)
        grad_in, grad_x, rows_buf, upper_buf, part_gain = attention_backward(
            sc, layer_in, cotangent, received, gain_row, qkv_weight, out_weight, qkv, probs,
            bwd_bufs, bwd_shapes,
        )
        bwd_bufs = (grad_x, rows_buf, upper_buf)
        gain_total = gain_total + jnp.where(active, part_gain, jnp.zeros_like(part_gain))
        if timestep + 1 < last_tick:
            received = from_behind(grad_in, "segment", -1)
    tokens = micro_count * seq_len
    all_normed = normed_buf[:micro_count].reshape(tokens, width_model)
    all_rows = rows_buf[:micro_count].reshape(tokens, qkv_cols)
    all_ctx = ctx_buf[:micro_count].reshape(tokens, ctx_cols)
    all_upper = upper_buf[:micro_count].reshape(tokens, width_model)
    zs, ys, cores = lax.axis_size("z"), lax.axis_size("y"), lax.axis_size("core")
    groups = zs * ys
    rows_total = qkv_weight.shape[0]
    chunk = rows_total // (groups * cores)
    out_chunk = ctx_cols // (groups * cores)
    mybit = lax.axis_index("core") % cores
    gain_cols = gain_total.reshape(groups, cores, chunk)
    normed_view = all_normed.reshape(tokens, groups, cores, chunk)
    ctx_view = all_ctx.reshape(tokens, groups, cores, out_chunk)

    def half_of(bit):
        n_part = lax.dynamic_index_in_dim(normed_view, bit, 2, keepdims=False).reshape(tokens, groups * chunk)
        c_part = lax.dynamic_index_in_dim(ctx_view, bit, 2, keepdims=False).reshape(tokens, groups * out_chunk)
        qkv_part = lax.dot_general(n_part, all_rows, TN, preferred_element_type=F32) * grad_scale
        out_part = lax.dot_general(c_part, all_upper, TN, preferred_element_type=F32) * grad_scale
        out_part = out_part.reshape(groups, chunk, out_chunk * width_model // chunk)
        g_part = lax.dynamic_index_in_dim(gain_cols, bit, 1, keepdims=False)[..., None] * grad_scale
        pad = jnp.zeros((groups, chunk, 128 - 1), F32)
        og = jnp.concatenate([out_part, g_part, pad], axis=-1)
        return (qkv_part.reshape(zs, ys, 1, chunk, qkv_cols), og.reshape(zs, ys, 1, chunk, og.shape[-1]))

    sends = tuple(x.astype(BF16) for x in half_of(1 - mybit))
    keeps = half_of(mybit)
    recvs = lax.ppermute(sends, "core", [(i, i ^ 1) for i in range(cores)])
    z_steps = [("z", 0, zs // 2 ** (k + 1)) for k in range(int(math.log2(zs)))]
    y_steps = [("y", 1, ys // 2 ** (k + 1)) for k in range(int(math.log2(ys)))]
    outs = []
    for keep, recv, steps in zip(keeps, recvs, (z_steps + y_steps, y_steps + z_steps)):
        cur = keep + recv.astype(F32)
        outs.append(halving(cur, steps).reshape(chunk, cur.shape[-1]))
    qkv_share, og_share = outs
    half_w = og_share.shape[1] - 128
    out_share = og_share[:, :half_w].reshape(out_chunk, width_model)
    gain_share = og_share[:, half_w]
    return (grad_x[:micro_count][None], qkv_share[None], out_share[None], gain_share[None])


def solution(mesh):
    dp = ("z", "y", "core")
    segs = mesh.shape["segment"]
    cores = 2
    ys = 4
    zs = mesh.shape["dp"] // (cores * ys)
    mesh4 = Mesh(mesh.devices.reshape(segs, zs, ys, cores), ("segment", "z", "y", "core"))
    in_specs = (
        P("segment", dp, None, None),
        P(dp, None, None),
        P(dp, None),
        P("segment", None),
        P("segment", None, None),
        P("segment", None, None),
        P("segment", None),
        P("segment", None, None, None),
    )
    out_specs = (
        P("segment", dp, None, None),
        P("segment", dp, None),
        P("segment", dp, None),
        P("segment", dp),
    )
    return jax.shard_map(
        on_device, mesh=mesh4, in_specs=in_specs, out_specs=out_specs, check_vma=False
    )
```

```python
import functools
import math

import jax
import jax.numpy as jnp
from jax import lax
from jax.experimental import pallas as pl
from jax.experimental.pallas import tpu as pltpu
from jax.sharding import Mesh, PartitionSpec as P

BLOCK = 64
HEAD_DIM = 64
EPS = 1e-05
F32 = jnp.float32
BF16 = jnp.bfloat16
NT = (((1,), (1,)), ((), ()))
TN = (((0,), (0,)), ((), ()))


def from_behind(value, axis, by):
    count = lax.axis_size(axis)
    pairs = [(i, i + by) for i in range(count) if 0 <= i + by < count]
    return lax.ppermute(value, axis, pairs)


def block_ids(glob_ids, rand_ids, block_count):
    head_count = rand_ids.shape[0]
    block_rows = jnp.arange(block_count, dtype=jnp.int32)
    window = block_rows[:, None] + jnp.arange(-1, 2, dtype=jnp.int32)[None, :]
    inside = (window >= 0) & (window < block_count)
    window_ids = jnp.where(inside, window, jnp.int32(-1))
    global_ids = jnp.broadcast_to(glob_ids[None, :], (block_count, glob_ids.shape[0]))
    fixed_ids = jnp.concatenate([window_ids, global_ids], axis=1)
    fixed_ids = jnp.broadcast_to(fixed_ids[None], (head_count, block_count, fixed_ids.shape[1]))
    listed_blocks = jnp.concatenate([fixed_ids, rand_ids], axis=2)
    list_len = listed_blocks.shape[2]
    earlier = (
        jnp.arange(list_len, dtype=jnp.int32)[:, None]
        > jnp.arange(list_len, dtype=jnp.int32)[None, :]
    )
    equal_prior = (listed_blocks[..., :, None] == listed_blocks[..., None, :]) & earlier
    repeated = jnp.any(equal_prior, axis=-1)
    usable = (listed_blocks >= 0) & jnp.logical_not(repeated)
    block_index = jnp.clip(listed_blocks, 0, block_count - 1)
    return (block_index, usable)


def halving(cur, steps):
    for axis, dim, bit in steps:
        n = lax.axis_size(axis)
        half = cur.shape[dim] // 2
        mybit = (lax.axis_index(axis) // bit) % 2
        keep = lax.dynamic_slice_in_dim(cur, mybit * half, half, axis=dim)
        send = lax.dynamic_slice_in_dim(cur, (1 - mybit) * half, half, axis=dim)
        recv = lax.ppermute(send.astype(BF16), axis, [(i, i ^ bit) for i in range(n)])
        cur = keep.astype(F32) + recv.astype(F32)
    return cur


def dp_reduce_scatter(first, second):
    cores = lax.axis_size("core")
    ys = lax.axis_size("y")
    zs = lax.axis_size("z")
    chunk = first.shape[0] // (zs * ys * cores)
    z_steps = [("z", 0, zs // 2 ** (k + 1)) for k in range(int(math.log2(zs)))]
    y_steps = [("y", 1, ys // 2 ** (k + 1)) for k in range(int(math.log2(ys)))]
    views = [part.reshape(zs, ys, cores, chunk, part.shape[1]) for part in (first, second)]
    mybit = lax.axis_index("core") % 2
    keeps = [lax.dynamic_slice_in_dim(v, mybit, 1, axis=2) for v in views]
    sends = tuple(lax.dynamic_slice_in_dim(v, 1 - mybit, 1, axis=2).astype(BF16) for v in views)
    recvs = lax.ppermute(sends, "core", [(i, i ^ 1) for i in range(cores)])
    outs = []
    for keep, recv, steps in zip(keeps, recvs, (z_steps + y_steps, y_steps + z_steps)):
        cur = keep.astype(F32) + recv.astype(F32)
        outs.append(halving(cur, steps).reshape(chunk, cur.shape[-1]))
    return outs


def dense_bias(block_index, usable, block_count, seq_len):
    names = block_index[..., None] == jnp.arange(block_count, dtype=jnp.int32)
    allowed = jnp.any(names & usable[..., None], axis=2)
    small = jnp.where(allowed, F32(0.0), F32(-1e30)).astype(BF16)
    extent = seq_len // block_count
    return jnp.repeat(jnp.repeat(small, extent, axis=1), extent, axis=2)


def forward_kernel(sc_ref, x_ref, gain_ref, wqkv_ref, bias_ref, nb_in, cb_in,
                   qkv_ref, p_ref, normed_ref, ctx_ref):
    del sc_ref, nb_in, cb_in
    width = ctx_ref.shape[1]
    pair_w = 2 * HEAD_DIM
    scale = 1.0 / math.sqrt(HEAD_DIM)
    x = x_ref[...].astype(F32)
    mean = jnp.mean(x, axis=-1, keepdims=True)
    cen = x - mean
    inv = lax.rsqrt(jnp.mean(cen * cen, axis=-1, keepdims=True) + EPS)
    normed = (cen * inv * gain_ref[...]).astype(BF16)
    normed_ref[...] = normed
    qkv_ref[...] = jnp.dot(normed, wqkv_ref[...], preferred_element_type=F32).astype(BF16)
    lane = lax.broadcasted_iota(jnp.int32, (1, pair_w), 1)
    low = lane < HEAD_DIM
    for pair in range(width // pair_w):
        q2 = qkv_ref[:, pl.ds(pair * pair_w, pair_w)]
        k2 = qkv_ref[:, pl.ds(width + pair * pair_w, pair_w)]
        v2 = qkv_ref[:, pl.ds(2 * width + pair * pair_w, pair_w)]
        ctxs = []
        for half in range(2):
            mine = low if half == 0 else jnp.logical_not(low)
            qh = jnp.where(mine, q2, jnp.zeros_like(q2))
            s = lax.dot_general(qh, k2, NT, preferred_element_type=F32) * scale
            s = s + bias_ref[2 * pair + half]
            m = jnp.max(s, axis=-1, keepdims=True)
            e = jnp.exp(s - m)
            p = e / jnp.sum(e, axis=-1, keepdims=True)
            p_ref[2 * pair + half] = p
            ctxs.append(jnp.dot(p.astype(BF16), v2, preferred_element_type=F32))
        ctx_ref[:, pl.ds(pair * pair_w, pair_w)] = jnp.where(low, ctxs[0], ctxs[1]).astype(BF16)


def backward_kernel(tick, sc_ref, x_ref, cot_ref, recv_ref, gain_ref, wqkv_ref, wout_ref, qkv_ref, p_ref,
                    gx_in, rb_in, ub_in,
                    gin_ref, gx_ref, rows_ref, upper_ref, pgain_ref, gctx_scr):
    del gx_in, rb_in, ub_in
    width = gctx_scr.shape[1]
    pair_w = 2 * HEAD_DIM
    scale = 1.0 / math.sqrt(HEAD_DIM)
    gy = jnp.where(sc_ref[tick, 3] > 0, cot_ref[...], recv_ref[...])
    upper_ref[...] = gy
    gctx_scr[...] = lax.dot_general(
        gy, wout_ref[...], NT, preferred_element_type=F32).astype(BF16)
    lane = lax.broadcasted_iota(jnp.int32, (1, pair_w), 1)
    low = lane < HEAD_DIM
    for pair in range(width // pair_w):
        cols = pl.ds(pair * pair_w, pair_w)
        q2 = qkv_ref[:, pl.ds(pair * pair_w, pair_w)]
        k2 = qkv_ref[:, pl.ds(width + pair * pair_w, pair_w)]
        v2 = qkv_ref[:, pl.ds(2 * width + pair * pair_w, pair_w)]
        g2 = gctx_scr[:, cols]
        outs = []
        for half in range(2):
            mine = low if half == 0 else jnp.logical_not(low)
            gh = jnp.where(mine, g2, jnp.zeros_like(g2))
            p = p_ref[2 * pair + half]
            pb = p.astype(BF16)
            dp = lax.dot_general(gh, v2, NT, preferred_element_type=F32).astype(BF16).astype(F32)
            rd = jnp.sum(dp * p, axis=-1, keepdims=True)
            ds = (p * (dp - rd) * scale).astype(BF16)
            dq = jnp.dot(ds, k2, preferred_element_type=F32)
            dk = lax.dot_general(ds, q2, TN, preferred_element_type=F32)
            dv = lax.dot_general(pb, g2, TN, preferred_element_type=F32)
            outs.append((dq, dk, dv))
        lo, hi = outs
        rows_ref[:, pl.ds(pair * pair_w, pair_w)] = jnp.where(low, lo[0], hi[0]).astype(BF16)
        rows_ref[:, pl.ds(width + pair * pair_w, pair_w)] = jnp.where(low, lo[1], hi[1]).astype(BF16)
        rows_ref[:, pl.ds(2 * width + pair * pair_w, pair_w)] = jnp.where(low, lo[2], hi[2]).astype(BF16)
    gn = lax.dot_general(rows_ref[...], wqkv_ref[...], NT, preferred_element_type=F32)
    x = x_ref[...].astype(F32)
    mean = jnp.mean(x, axis=-1, keepdims=True)
    cen = x - mean
    inv = lax.rsqrt(jnp.mean(cen * cen, axis=-1, keepdims=True) + EPS)
    xn = cen * inv
    pgain_ref[...] = jnp.sum(gn * xn, axis=0, keepdims=True)
    gh = gn * gain_ref[...]
    gin = gy.astype(F32) + inv * (
        gh
        - jnp.mean(gh, axis=-1, keepdims=True)
        - xn * jnp.mean(gh * xn, axis=-1, keepdims=True)
    )
    gin = gin.astype(BF16)
    gin_ref[...] = gin
    gx_ref[...] = gin


def full_spec(shape):
    return pl.BlockSpec(shape, lambda i, sc: (0,) * len(shape))


def slot_spec(tick, k, rows, cols):
    return pl.BlockSpec((None, rows, cols), lambda i, sc: (sc[tick, k], 0, 0))


def attention_forward(tick, sc, layer_in, gain_row, qkv_weight, bias, bufs, buf_shapes):
    micro, seq_len, width_model = layer_in.shape
    qkv_cols = qkv_weight.shape[1]
    ctx_cols = buf_shapes[1][2]
    heads = bias.shape[0]
    anyspec = pl.BlockSpec(memory_space=pl.ANY)
    flops = 2 * seq_len * width_model * qkv_cols + 4 * 2 * seq_len * seq_len * ctx_cols
    grid_spec = pltpu.PrefetchScalarGridSpec(
        num_scalar_prefetch=1,
        grid=(1,),
        in_specs=[
            slot_spec(tick, 1, seq_len, width_model),
            full_spec((1, width_model)),
            full_spec(qkv_weight.shape),
            full_spec(bias.shape),
        ] + ([anyspec, anyspec] if bufs is not None else []),
        out_specs=[
            full_spec((seq_len, qkv_cols)),
            full_spec((heads, seq_len, seq_len)),
            slot_spec(tick, 0, seq_len, width_model),
            slot_spec(tick, 0, seq_len, ctx_cols),
        ],
    )
    if bufs is None:
        kernel = lambda a, b, c, d, e, *outs: forward_kernel(a, b, c, d, e, None, None, *outs)
        extra, aliases = (), {}
    else:
        kernel, extra, aliases = forward_kernel, tuple(bufs), {5: 2, 6: 3}
    return pl.pallas_call(
        kernel,
        grid_spec=grid_spec,
        out_shape=(
            jax.ShapeDtypeStruct((seq_len, qkv_cols), BF16),
            jax.ShapeDtypeStruct((heads, seq_len, seq_len), F32),
            *[jax.ShapeDtypeStruct(shape, BF16) for shape in buf_shapes],
        ),
        input_output_aliases=aliases,
        cost_estimate=pl.CostEstimate(
            flops=flops, transcendentals=bias.size, bytes_accessed=8 * 1024 * 1024),
        name="attention_forward",
    )(sc, layer_in, gain_row, qkv_weight, bias, *extra)


def attention_backward(tick, sc, layer_in, cotangent, received, gain_row, qkv_weight, out_weight,
                       qkv, probs, bufs, buf_shapes):
    micro, seq_len, width_model = layer_in.shape
    qkv_cols = qkv_weight.shape[1]
    ctx_cols = out_weight.shape[0]
    anyspec = pl.BlockSpec(memory_space=pl.ANY)
    flops = 2 * seq_len * width_model * (qkv_cols + ctx_cols) + 8 * 2 * seq_len * seq_len * ctx_cols
    grid_spec = pltpu.PrefetchScalarGridSpec(
        num_scalar_prefetch=1,
        grid=(1,),
        in_specs=[
            slot_spec(tick, 1, seq_len, width_model),
            slot_spec(tick, 2, seq_len, width_model),
            full_spec((seq_len, width_model)),
            full_spec((1, width_model)),
            full_spec(qkv_weight.shape),
            full_spec(out_weight.shape),
            full_spec(qkv.shape),
            full_spec(probs.shape),
        ] + ([anyspec, anyspec, anyspec] if bufs is not None else []),
        out_specs=[
            full_spec((seq_len, width_model)),
            slot_spec(tick, 0, seq_len, width_model),
            slot_spec(tick, 0, seq_len, qkv_cols),
            slot_spec(tick, 0, seq_len, width_model),
            full_spec((1, width_model)),
        ],
        scratch_shapes=[pltpu.VMEM((seq_len, ctx_cols), BF16)],
    )
    if bufs is None:
        kernel = lambda *refs: backward_kernel(tick, *refs[:9], None, None, None, *refs[9:])
        extra, aliases = (), {}
    else:
        kernel, extra, aliases = functools.partial(backward_kernel, tick), tuple(bufs), {9: 1, 10: 2, 11: 3}
    return pl.pallas_call(
        kernel,
        grid_spec=grid_spec,
        out_shape=(
            jax.ShapeDtypeStruct((seq_len, width_model), BF16),
            *[jax.ShapeDtypeStruct(shape, BF16) for shape in buf_shapes],
            jax.ShapeDtypeStruct((1, width_model), F32),
        ),
        input_output_aliases=aliases,
        name="attention_backward",
        cost_estimate=pl.CostEstimate(
            flops=flops, transcendentals=0, bytes_accessed=10 * 1024 * 1024),
    )(sc, layer_in, cotangent, received, gain_row, qkv_weight, out_weight, qkv, probs, *extra)


def on_device(
    segment_inputs, cotangent, order, norm_gain, w_qkv, w_out, global_blocks, random_blocks
):
    segments = lax.axis_size("segment")
    my_segment = lax.axis_index("segment")
    layer_in = segment_inputs[0]
    micro_count = layer_in.shape[0]
    seq_len = layer_in.shape[1]
    width_model = layer_in.shape[2]
    gain_row = norm_gain[0][None, :]
    qkv_weight = w_qkv[0]
    out_weight = w_out[0]
    slot_order = order[0]
    block_total = seq_len // BLOCK
    block_index, usable = block_ids(global_blocks[0], random_blocks[0], block_total)
    bias = dense_bias(block_index, usable, block_total, seq_len)
    dp_size = lax.axis_size("z") * lax.axis_size("y") * lax.axis_size("core")
    grad_scale = 1.0 / math.sqrt(dp_size * micro_count * seq_len)
    qkv_cols = qkv_weight.shape[1]
    ctx_cols = out_weight.shape[0]

    slots = micro_count + 1
    fwd_shapes = ((slots, seq_len, width_model), (slots, seq_len, ctx_cols))
    bwd_shapes = ((slots, seq_len, width_model), (slots, seq_len, qkv_cols), (slots, seq_len, width_model))
    fwd_bufs = None
    bwd_bufs = None
    gain_total = jnp.zeros((1, width_model), F32)
    received = cotangent[0]
    last_tick = micro_count + segments - 1
    use_cot = (my_segment == segments - 1).astype(jnp.int32)
    ticks = jnp.arange(last_tick, dtype=jnp.int32)
    slot_all = ticks - (segments - 1) + my_segment
    active_all = (slot_all >= 0) & (slot_all < micro_count)
    clip_all = jnp.clip(slot_all, 0, micro_count - 1)
    batch_all = slot_order[clip_all]
    write_all = jnp.where(active_all, batch_all, jnp.int32(micro_count))
    sc = jnp.stack(
        [write_all, batch_all, clip_all, jnp.broadcast_to(use_cot, (last_tick,))], axis=1
    ).astype(jnp.int32)
    for timestep in range(last_tick):
        active = active_all[timestep]
        qkv, probs, normed_buf, ctx_buf = attention_forward(
            timestep, sc, layer_in, gain_row, qkv_weight, bias, fwd_bufs, fwd_shapes)
        fwd_bufs = (normed_buf, ctx_buf)
        grad_in, grad_x, rows_buf, upper_buf, part_gain = attention_backward(
            timestep, sc, layer_in, cotangent, received, gain_row, qkv_weight, out_weight, qkv, probs,
            bwd_bufs, bwd_shapes,
        )
        bwd_bufs = (grad_x, rows_buf, upper_buf)
        gain_total = gain_total + jnp.where(active, part_gain, jnp.zeros_like(part_gain))
        if timestep + 1 < last_tick:
            received = from_behind(grad_in, "segment", -1)
    all_normed = normed_buf[:micro_count].reshape(micro_count * seq_len, width_model)
    all_rows = rows_buf[:micro_count].reshape(micro_count * seq_len, qkv_cols)
    all_ctx = ctx_buf[:micro_count].reshape(micro_count * seq_len, ctx_cols)
    all_upper = upper_buf[:micro_count].reshape(micro_count * seq_len, width_model)
    sum_qkv = lax.dot_general(all_normed, all_rows, TN, preferred_element_type=F32)
    sum_out = lax.dot_general(all_ctx, all_upper, TN, preferred_element_type=F32)
    rows_total = qkv_weight.shape[0]
    fold = rows_total // ctx_cols
    out_folded = sum_out.reshape(rows_total, ctx_cols * width_model // rows_total)
    gain_col = gain_total.reshape(rows_total, width_model // rows_total)
    pad = jnp.zeros((rows_total, 128 - gain_col.shape[1]), BF16)
    out_gain = jnp.concatenate(
        [(out_folded * grad_scale).astype(BF16), (gain_col * grad_scale).astype(BF16), pad], axis=1)
    qkv_share, out_gain_share = dp_reduce_scatter((sum_qkv * grad_scale).astype(BF16), out_gain)
    share = jnp.concatenate([qkv_share, out_gain_share], axis=1)
    share_rows = share.shape[0]
    qkv_share = share[:, :qkv_cols]
    out_share = share[:, qkv_cols:qkv_cols + out_folded.shape[1]].reshape(share_rows // fold, width_model)
    gain_share = share[:, qkv_cols + out_folded.shape[1]:qkv_cols + out_folded.shape[1] + gain_col.shape[1]].reshape(-1)
    return (grad_x[:micro_count][None], qkv_share[None], out_share[None], gain_share[None])


def solution(mesh):
    dp = ("z", "y", "core")
    segs = mesh.shape["segment"]
    cores = 2
    ys = 4
    zs = mesh.shape["dp"] // (cores * ys)
    mesh4 = Mesh(mesh.devices.reshape(segs, zs, ys, cores), ("segment", "z", "y", "core"))
    in_specs = (
        P("segment", dp, None, None),
        P(dp, None, None),
        P(dp, None),
        P("segment", None),
        P("segment", None, None),
        P("segment", None, None),
        P("segment", None),
        P("segment", None, None, None),
    )
    out_specs = (
        P("segment", dp, None, None),
        P("segment", dp, None),
        P("segment", dp, None),
        P("segment", dp),
    )
    return jax.shard_map(
        on_device, mesh=mesh4, in_specs=in_specs, out_specs=out_specs, check_vma=False
    )
```

```python
import math

import jax
import jax.numpy as jnp
from jax import lax
from jax.experimental import pallas as pl
from jax.experimental.pallas import tpu as pltpu
from jax.sharding import Mesh, PartitionSpec as P

BLOCK = 64
HEAD_DIM = 64
EPS = 1e-05
F32 = jnp.float32
BF16 = jnp.bfloat16
NT = (((1,), (1,)), ((), ()))
TN = (((0,), (0,)), ((), ()))


def from_behind(value, axis, by):
    count = lax.axis_size(axis)
    pairs = [(i, i + by) for i in range(count) if 0 <= i + by < count]
    return lax.ppermute(value, axis, pairs)


def block_ids(glob_ids, rand_ids, block_count):
    head_count = rand_ids.shape[0]
    block_rows = jnp.arange(block_count, dtype=jnp.int32)
    window = block_rows[:, None] + jnp.arange(-1, 2, dtype=jnp.int32)[None, :]
    inside = (window >= 0) & (window < block_count)
    window_ids = jnp.where(inside, window, jnp.int32(-1))
    global_ids = jnp.broadcast_to(glob_ids[None, :], (block_count, glob_ids.shape[0]))
    fixed_ids = jnp.concatenate([window_ids, global_ids], axis=1)
    fixed_ids = jnp.broadcast_to(fixed_ids[None], (head_count, block_count, fixed_ids.shape[1]))
    listed_blocks = jnp.concatenate([fixed_ids, rand_ids], axis=2)
    list_len = listed_blocks.shape[2]
    earlier = (
        jnp.arange(list_len, dtype=jnp.int32)[:, None]
        > jnp.arange(list_len, dtype=jnp.int32)[None, :]
    )
    equal_prior = (listed_blocks[..., :, None] == listed_blocks[..., None, :]) & earlier
    repeated = jnp.any(equal_prior, axis=-1)
    usable = (listed_blocks >= 0) & jnp.logical_not(repeated)
    block_index = jnp.clip(listed_blocks, 0, block_count - 1)
    return (block_index, usable)


def halving(cur, steps):
    for axis, dim, bit in steps:
        n = lax.axis_size(axis)
        half = cur.shape[dim] // 2
        mybit = (lax.axis_index(axis) // bit) % 2
        keep = lax.dynamic_slice_in_dim(cur, mybit * half, half, axis=dim)
        send = lax.dynamic_slice_in_dim(cur, (1 - mybit) * half, half, axis=dim)
        recv = lax.ppermute(send.astype(BF16), axis, [(i, i ^ bit) for i in range(n)])
        cur = keep.astype(F32) + recv.astype(F32)
    return cur


def dp_reduce_scatter(first, second):
    cores = lax.axis_size("core")
    ys = lax.axis_size("y")
    zs = lax.axis_size("z")
    chunk = first.shape[0] // (zs * ys * cores)
    z_steps = [("z", 0, zs // 2 ** (k + 1)) for k in range(int(math.log2(zs)))]
    y_steps = [("y", 1, ys // 2 ** (k + 1)) for k in range(int(math.log2(ys)))]
    views = [part.reshape(zs, ys, cores, chunk, part.shape[1]) for part in (first, second)]
    mybit = lax.axis_index("core") % 2
    keeps = [lax.dynamic_slice_in_dim(v, mybit, 1, axis=2) for v in views]
    sends = tuple(lax.dynamic_slice_in_dim(v, 1 - mybit, 1, axis=2).astype(BF16) for v in views)
    recvs = lax.ppermute(sends, "core", [(i, i ^ 1) for i in range(cores)])
    outs = []
    for keep, recv, steps in zip(keeps, recvs, (z_steps + y_steps, y_steps + z_steps)):
        cur = keep.astype(F32) + recv.astype(F32)
        outs.append(halving(cur, steps).reshape(chunk, cur.shape[-1]))
    return outs


def dense_bias(block_index, usable, block_count, seq_len):
    names = block_index[..., None] == jnp.arange(block_count, dtype=jnp.int32)
    allowed = jnp.any(names & usable[..., None], axis=2)
    small = jnp.where(allowed, F32(0.0), F32(-1e30)).astype(BF16)
    extent = seq_len // block_count
    return jnp.repeat(jnp.repeat(small, extent, axis=1), extent, axis=2)


def forward_kernel(sc_ref, x_ref, gain_ref, wqkv_ref, bias_ref, nb_in, cb_in,
                   qkv_ref, p_ref, normed_ref, ctx_ref):
    del sc_ref, nb_in, cb_in
    width = ctx_ref.shape[1]
    pair_w = 2 * HEAD_DIM
    scale = 1.0 / math.sqrt(HEAD_DIM)
    x = x_ref[...].astype(F32)
    mean = jnp.mean(x, axis=-1, keepdims=True)
    cen = x - mean
    inv = lax.rsqrt(jnp.mean(cen * cen, axis=-1, keepdims=True) + EPS)
    normed = (cen * inv * gain_ref[...]).astype(BF16)
    normed_ref[...] = normed
    qkv_ref[...] = jnp.dot(normed, wqkv_ref[...], preferred_element_type=F32).astype(BF16)
    lane = lax.broadcasted_iota(jnp.int32, (1, pair_w), 1)
    low = lane < HEAD_DIM
    for pair in range(width // pair_w):
        q2 = qkv_ref[:, pl.ds(pair * pair_w, pair_w)]
        k2 = qkv_ref[:, pl.ds(width + pair * pair_w, pair_w)]
        v2 = qkv_ref[:, pl.ds(2 * width + pair * pair_w, pair_w)]
        ctxs = []
        for half in range(2):
            mine = low if half == 0 else jnp.logical_not(low)
            qh = jnp.where(mine, q2, jnp.zeros_like(q2))
            s = lax.dot_general(qh, k2, NT, preferred_element_type=F32) * scale
            s = s + bias_ref[2 * pair + half]
            m = jnp.max(s, axis=-1, keepdims=True)
            e = jnp.exp(s - m)
            p = e / jnp.sum(e, axis=-1, keepdims=True)
            pb = p.astype(BF16)
            p_ref[2 * pair + half] = pb
            ctxs.append(jnp.dot(pb, v2, preferred_element_type=F32))
        ctx_ref[:, pl.ds(pair * pair_w, pair_w)] = jnp.where(low, ctxs[0], ctxs[1]).astype(BF16)


def backward_kernel(sc_ref, x_ref, cot_ref, recv_ref, gain_ref, wqkv_ref, wout_ref, qkv_ref, p_ref,
                    gx_in, rb_in, ub_in,
                    gin_ref, gx_ref, rows_ref, upper_ref, pgain_ref, gctx_scr):
    del gx_in, rb_in, ub_in
    width = gctx_scr.shape[1]
    pair_w = 2 * HEAD_DIM
    scale = 1.0 / math.sqrt(HEAD_DIM)
    gy = jnp.where(sc_ref[3] > 0, cot_ref[...], recv_ref[...])
    upper_ref[...] = gy
    gctx_scr[...] = lax.dot_general(
        gy, wout_ref[...], NT, preferred_element_type=F32).astype(BF16)
    lane = lax.broadcasted_iota(jnp.int32, (1, pair_w), 1)
    low = lane < HEAD_DIM
    for pair in range(width // pair_w):
        cols = pl.ds(pair * pair_w, pair_w)
        q2 = qkv_ref[:, pl.ds(pair * pair_w, pair_w)]
        k2 = qkv_ref[:, pl.ds(width + pair * pair_w, pair_w)]
        v2 = qkv_ref[:, pl.ds(2 * width + pair * pair_w, pair_w)]
        g2 = gctx_scr[:, cols]
        outs = []
        for half in range(2):
            mine = low if half == 0 else jnp.logical_not(low)
            gh = jnp.where(mine, g2, jnp.zeros_like(g2))
            pb = p_ref[2 * pair + half]
            p = pb.astype(F32)
            dp = lax.dot_general(gh, v2, NT, preferred_element_type=F32).astype(BF16).astype(F32)
            rd = jnp.sum(dp * p, axis=-1, keepdims=True)
            ds = (p * (dp - rd) * scale).astype(BF16)
            dq = jnp.dot(ds, k2, preferred_element_type=F32)
            dk = lax.dot_general(ds, q2, TN, preferred_element_type=F32)
            dv = lax.dot_general(pb, g2, TN, preferred_element_type=F32)
            outs.append((dq, dk, dv))
        lo, hi = outs
        rows_ref[:, pl.ds(pair * pair_w, pair_w)] = jnp.where(low, lo[0], hi[0]).astype(BF16)
        rows_ref[:, pl.ds(width + pair * pair_w, pair_w)] = jnp.where(low, lo[1], hi[1]).astype(BF16)
        rows_ref[:, pl.ds(2 * width + pair * pair_w, pair_w)] = jnp.where(low, lo[2], hi[2]).astype(BF16)
    gn = lax.dot_general(rows_ref[...], wqkv_ref[...], NT, preferred_element_type=F32)
    x = x_ref[...].astype(F32)
    mean = jnp.mean(x, axis=-1, keepdims=True)
    cen = x - mean
    inv = lax.rsqrt(jnp.mean(cen * cen, axis=-1, keepdims=True) + EPS)
    xn = cen * inv
    pgain_ref[...] = jnp.sum(gn * xn, axis=0, keepdims=True)
    gh = gn * gain_ref[...]
    gin = gy.astype(F32) + inv * (
        gh
        - jnp.mean(gh, axis=-1, keepdims=True)
        - xn * jnp.mean(gh * xn, axis=-1, keepdims=True)
    )
    gin = gin.astype(BF16)
    gin_ref[...] = gin
    gx_ref[...] = gin


def full_spec(shape):
    return pl.BlockSpec(shape, lambda i, sc: (0,) * len(shape))


def slot_spec(k, rows, cols):
    return pl.BlockSpec((None, rows, cols), lambda i, sc: (sc[k], 0, 0))


def attention_forward(sc, layer_in, gain_row, qkv_weight, bias, bufs, buf_shapes):
    micro, seq_len, width_model = layer_in.shape
    qkv_cols = qkv_weight.shape[1]
    ctx_cols = buf_shapes[1][2]
    heads = bias.shape[0]
    anyspec = pl.BlockSpec(memory_space=pl.ANY)
    flops = 2 * seq_len * width_model * qkv_cols + 4 * 2 * seq_len * seq_len * ctx_cols
    grid_spec = pltpu.PrefetchScalarGridSpec(
        num_scalar_prefetch=1,
        grid=(1,),
        in_specs=[
            slot_spec(1, seq_len, width_model),
            full_spec((1, width_model)),
            full_spec(qkv_weight.shape),
            full_spec(bias.shape),
        ] + ([anyspec, anyspec] if bufs is not None else []),
        out_specs=[
            full_spec((seq_len, qkv_cols)),
            full_spec((heads, seq_len, seq_len)),
            slot_spec(0, seq_len, width_model),
            slot_spec(0, seq_len, ctx_cols),
        ],
    )
    if bufs is None:
        kernel = lambda a, b, c, d, e, *outs: forward_kernel(a, b, c, d, e, None, None, *outs)
        extra, aliases = (), {}
    else:
        kernel, extra, aliases = forward_kernel, tuple(bufs), {5: 2, 6: 3}
    return pl.pallas_call(
        kernel,
        grid_spec=grid_spec,
        out_shape=(
            jax.ShapeDtypeStruct((seq_len, qkv_cols), BF16),
            jax.ShapeDtypeStruct((heads, seq_len, seq_len), BF16),
            *[jax.ShapeDtypeStruct(shape, BF16) for shape in buf_shapes],
        ),
        input_output_aliases=aliases,
        cost_estimate=pl.CostEstimate(
            flops=flops, transcendentals=bias.size, bytes_accessed=8 * 1024 * 1024),
        name="attention_forward",
    )(sc, layer_in, gain_row, qkv_weight, bias, *extra)


def attention_backward(sc, layer_in, cotangent, received, gain_row, qkv_weight, out_weight,
                       qkv, probs, bufs, buf_shapes):
    micro, seq_len, width_model = layer_in.shape
    qkv_cols = qkv_weight.shape[1]
    ctx_cols = out_weight.shape[0]
    anyspec = pl.BlockSpec(memory_space=pl.ANY)
    flops = 2 * seq_len * width_model * (qkv_cols + ctx_cols) + 8 * 2 * seq_len * seq_len * ctx_cols
    grid_spec = pltpu.PrefetchScalarGridSpec(
        num_scalar_prefetch=1,
        grid=(1,),
        in_specs=[
            slot_spec(1, seq_len, width_model),
            slot_spec(2, seq_len, width_model),
            full_spec((seq_len, width_model)),
            full_spec((1, width_model)),
            full_spec(qkv_weight.shape),
            full_spec(out_weight.shape),
            full_spec(qkv.shape),
            full_spec(probs.shape),
        ] + ([anyspec, anyspec, anyspec] if bufs is not None else []),
        out_specs=[
            full_spec((seq_len, width_model)),
            slot_spec(0, seq_len, width_model),
            slot_spec(0, seq_len, qkv_cols),
            slot_spec(0, seq_len, width_model),
            full_spec((1, width_model)),
        ],
        scratch_shapes=[pltpu.VMEM((seq_len, ctx_cols), BF16)],
    )
    if bufs is None:
        kernel = lambda *refs: backward_kernel(*refs[:9], None, None, None, *refs[9:])
        extra, aliases = (), {}
    else:
        kernel, extra, aliases = backward_kernel, tuple(bufs), {9: 1, 10: 2, 11: 3}
    return pl.pallas_call(
        kernel,
        grid_spec=grid_spec,
        out_shape=(
            jax.ShapeDtypeStruct((seq_len, width_model), BF16),
            *[jax.ShapeDtypeStruct(shape, BF16) for shape in buf_shapes],
            jax.ShapeDtypeStruct((1, width_model), F32),
        ),
        input_output_aliases=aliases,
        name="attention_backward",
        cost_estimate=pl.CostEstimate(
            flops=flops, transcendentals=0, bytes_accessed=10 * 1024 * 1024),
    )(sc, layer_in, cotangent, received, gain_row, qkv_weight, out_weight, qkv, probs, *extra)


def on_device(
    segment_inputs, cotangent, order, norm_gain, w_qkv, w_out, global_blocks, random_blocks
):
    segments = lax.axis_size("segment")
    my_segment = lax.axis_index("segment")
    layer_in = segment_inputs[0]
    micro_count = layer_in.shape[0]
    seq_len = layer_in.shape[1]
    width_model = layer_in.shape[2]
    gain_row = norm_gain[0][None, :]
    qkv_weight = w_qkv[0]
    out_weight = w_out[0]
    slot_order = order[0]
    block_total = seq_len // BLOCK
    block_index, usable = block_ids(global_blocks[0], random_blocks[0], block_total)
    bias = dense_bias(block_index, usable, block_total, seq_len)
    dp_size = lax.axis_size("z") * lax.axis_size("y") * lax.axis_size("core")
    grad_scale = 1.0 / math.sqrt(dp_size * micro_count * seq_len)
    qkv_cols = qkv_weight.shape[1]
    ctx_cols = out_weight.shape[0]

    slots = micro_count + 1
    fwd_shapes = ((slots, seq_len, width_model), (slots, seq_len, ctx_cols))
    bwd_shapes = ((slots, seq_len, width_model), (slots, seq_len, qkv_cols), (slots, seq_len, width_model))
    fwd_bufs = None
    bwd_bufs = None
    gain_total = jnp.zeros((1, width_model), F32)
    received = cotangent[0]
    last_tick = micro_count + segments - 1
    use_cot = (my_segment == segments - 1).astype(jnp.int32)
    for timestep in range(last_tick):
        slot_now = timestep - (segments - 1) + my_segment
        active = (slot_now >= 0) & (slot_now < micro_count)
        slot_clip = jnp.clip(slot_now, 0, micro_count - 1)
        batch_id = slot_order[slot_clip]
        write_id = jnp.where(active, batch_id, jnp.int32(micro_count))
        sc = jnp.stack([write_id, batch_id, slot_clip, use_cot]).astype(jnp.int32)
        qkv, probs, normed_buf, ctx_buf = attention_forward(
            sc, layer_in, gain_row, qkv_weight, bias, fwd_bufs, fwd_shapes)
        fwd_bufs = (normed_buf, ctx_buf)
        grad_in, grad_x, rows_buf, upper_buf, part_gain = attention_backward(
            sc, layer_in, cotangent, received, gain_row, qkv_weight, out_weight, qkv, probs,
            bwd_bufs, bwd_shapes,
        )
        bwd_bufs = (grad_x, rows_buf, upper_buf)
        gain_total = gain_total + jnp.where(active, part_gain, jnp.zeros_like(part_gain))
        if timestep + 1 < last_tick:
            received = from_behind(grad_in, "segment", -1)
    all_normed = normed_buf[:micro_count].reshape(micro_count * seq_len, width_model)
    all_rows = rows_buf[:micro_count].reshape(micro_count * seq_len, qkv_cols)
    all_ctx = ctx_buf[:micro_count].reshape(micro_count * seq_len, ctx_cols)
    all_upper = upper_buf[:micro_count].reshape(micro_count * seq_len, width_model)
    sum_qkv = lax.dot_general(all_normed, all_rows, TN, preferred_element_type=F32)
    sum_out = lax.dot_general(all_ctx, all_upper, TN, preferred_element_type=F32)
    rows_total = qkv_weight.shape[0]
    fold = rows_total // ctx_cols
    out_folded = sum_out.reshape(rows_total, ctx_cols * width_model // rows_total)
    gain_col = gain_total.reshape(rows_total, width_model // rows_total)
    pad = jnp.zeros((rows_total, 128 - gain_col.shape[1]), BF16)
    out_gain = jnp.concatenate(
        [(out_folded * grad_scale).astype(BF16), (gain_col * grad_scale).astype(BF16), pad], axis=1)
    qkv_share, out_gain_share = dp_reduce_scatter((sum_qkv * grad_scale).astype(BF16), out_gain)
    share = jnp.concatenate([qkv_share, out_gain_share], axis=1)
    share_rows = share.shape[0]
    qkv_share = share[:, :qkv_cols]
    out_share = share[:, qkv_cols:qkv_cols + out_folded.shape[1]].reshape(share_rows // fold, width_model)
    gain_share = share[:, qkv_cols + out_folded.shape[1]:qkv_cols + out_folded.shape[1] + gain_col.shape[1]].reshape(-1)
    return (grad_x[:micro_count][None], qkv_share[None], out_share[None], gain_share[None])


def solution(mesh):
    dp = ("z", "y", "core")
    segs = mesh.shape["segment"]
    cores = 2
    ys = 4
    zs = mesh.shape["dp"] // (cores * ys)
    mesh4 = Mesh(mesh.devices.reshape(segs, zs, ys, cores), ("segment", "z", "y", "core"))
    in_specs = (
        P("segment", dp, None, None),
        P(dp, None, None),
        P(dp, None),
        P("segment", None),
        P("segment", None, None),
        P("segment", None, None),
        P("segment", None),
        P("segment", None, None, None),
    )
    out_specs = (
        P("segment", dp, None, None),
        P("segment", dp, None),
        P("segment", dp, None),
        P("segment", dp),
    )
    return jax.shard_map(
        on_device, mesh=mesh4, in_specs=in_specs, out_specs=out_specs, check_vma=False
    )
```

```python
import math

import jax
import jax.numpy as jnp
from jax import lax
from jax.experimental import pallas as pl
from jax.experimental.pallas import tpu as pltpu
from jax.sharding import Mesh, PartitionSpec as P

BLOCK = 64
HEAD_DIM = 64
EPS = 1e-05
F32 = jnp.float32
BF16 = jnp.bfloat16
NT = (((1,), (1,)), ((), ()))
TN = (((0,), (0,)), ((), ()))


def from_behind(value, axis, by):
    count = lax.axis_size(axis)
    pairs = [(i, i + by) for i in range(count) if 0 <= i + by < count]
    return lax.ppermute(value, axis, pairs)


def block_ids(glob_ids, rand_ids, block_count):
    head_count = rand_ids.shape[0]
    block_rows = jnp.arange(block_count, dtype=jnp.int32)
    window = block_rows[:, None] + jnp.arange(-1, 2, dtype=jnp.int32)[None, :]
    inside = (window >= 0) & (window < block_count)
    window_ids = jnp.where(inside, window, jnp.int32(-1))
    global_ids = jnp.broadcast_to(glob_ids[None, :], (block_count, glob_ids.shape[0]))
    fixed_ids = jnp.concatenate([window_ids, global_ids], axis=1)
    fixed_ids = jnp.broadcast_to(fixed_ids[None], (head_count, block_count, fixed_ids.shape[1]))
    listed_blocks = jnp.concatenate([fixed_ids, rand_ids], axis=2)
    list_len = listed_blocks.shape[2]
    earlier = (
        jnp.arange(list_len, dtype=jnp.int32)[:, None]
        > jnp.arange(list_len, dtype=jnp.int32)[None, :]
    )
    equal_prior = (listed_blocks[..., :, None] == listed_blocks[..., None, :]) & earlier
    repeated = jnp.any(equal_prior, axis=-1)
    usable = (listed_blocks >= 0) & jnp.logical_not(repeated)
    block_index = jnp.clip(listed_blocks, 0, block_count - 1)
    return (block_index, usable)


def halving(cur, steps):
    for axis, dim, bit in steps:
        n = lax.axis_size(axis)
        half = cur.shape[dim] // 2
        mybit = (lax.axis_index(axis) // bit) % 2
        keep = lax.dynamic_slice_in_dim(cur, mybit * half, half, axis=dim)
        send = lax.dynamic_slice_in_dim(cur, (1 - mybit) * half, half, axis=dim)
        recv = lax.ppermute(send.astype(BF16), axis, [(i, i ^ bit) for i in range(n)])
        cur = keep.astype(F32) + recv.astype(F32)
    return cur


def dp_reduce_scatter(first, second):
    cores = lax.axis_size("core")
    ys = lax.axis_size("y")
    zs = lax.axis_size("z")
    chunk = first.shape[0] // (zs * ys * cores)
    z_steps = [("z", 0, zs // 2 ** (k + 1)) for k in range(int(math.log2(zs)))]
    y_steps = [("y", 1, ys // 2 ** (k + 1)) for k in range(int(math.log2(ys)))]
    views = [part.reshape(zs, ys, cores, chunk, part.shape[1]) for part in (first, second)]
    mybit = lax.axis_index("core") % 2
    keeps = [lax.dynamic_slice_in_dim(v, mybit, 1, axis=2) for v in views]
    sends = tuple(lax.dynamic_slice_in_dim(v, 1 - mybit, 1, axis=2).astype(BF16) for v in views)
    recvs = lax.ppermute(sends, "core", [(i, i ^ 1) for i in range(cores)])
    outs = []
    for keep, recv, steps in zip(keeps, recvs, (z_steps + y_steps, y_steps + z_steps)):
        cur = keep.astype(F32) + recv.astype(F32)
        outs.append(halving(cur, steps).reshape(chunk, cur.shape[-1]))
    return outs


def dense_bias(block_index, usable, block_count, seq_len):
    names = block_index[..., None] == jnp.arange(block_count, dtype=jnp.int32)
    allowed = jnp.any(names & usable[..., None], axis=2)
    small = jnp.where(allowed, F32(0.0), F32(-1e30)).astype(BF16)
    extent = seq_len // block_count
    return jnp.repeat(jnp.repeat(small, extent, axis=1), extent, axis=2)


def forward_kernel(sc_ref, x_ref, gain_ref, wqkv_ref, bias_ref, nb_in, cb_in,
                   qkv_ref, p_ref, normed_ref, ctx_ref):
    del sc_ref, nb_in, cb_in
    width = ctx_ref.shape[1]
    pair_w = 2 * HEAD_DIM
    scale = 1.0 / math.sqrt(HEAD_DIM)
    x = x_ref[...].astype(F32)
    mean = jnp.mean(x, axis=-1, keepdims=True)
    cen = x - mean
    inv = lax.rsqrt(jnp.mean(cen * cen, axis=-1, keepdims=True) + EPS)
    normed = (cen * inv * gain_ref[...]).astype(BF16)
    normed_ref[...] = normed
    qkv_ref[...] = jnp.dot(normed, wqkv_ref[...], preferred_element_type=F32).astype(BF16)
    lane = lax.broadcasted_iota(jnp.int32, (1, pair_w), 1)
    low = lane < HEAD_DIM
    for pair in range(width // pair_w):
        q2 = qkv_ref[:, pl.ds(pair * pair_w, pair_w)]
        k2 = qkv_ref[:, pl.ds(width + pair * pair_w, pair_w)]
        v2 = qkv_ref[:, pl.ds(2 * width + pair * pair_w, pair_w)]
        ctxs = []
        for half in range(2):
            mine = low if half == 0 else jnp.logical_not(low)
            qh = jnp.where(mine, q2, jnp.zeros_like(q2))
            s = lax.dot_general(qh, k2, NT, preferred_element_type=F32) * scale
            s = s + bias_ref[2 * pair + half]
            m = jnp.max(s, axis=-1, keepdims=True)
            e = jnp.exp(s - m)
            p = e / jnp.sum(e, axis=-1, keepdims=True)
            pb = p.astype(BF16)
            p_ref[2 * pair + half] = pb
            ctxs.append(jnp.dot(pb, v2, preferred_element_type=F32))
        ctx_ref[:, pl.ds(pair * pair_w, pair_w)] = jnp.where(low, ctxs[0], ctxs[1]).astype(BF16)


def backward_kernel(sc_ref, x_ref, cot_ref, recv_ref, gain_ref, wqkv_ref, wout_ref, qkv_ref, p_ref,
                    gx_in, rb_in, ub_in,
                    gin_ref, gx_ref, rows_ref, upper_ref, pgain_ref, gctx_scr):
    del gx_in, rb_in, ub_in
    width = gctx_scr.shape[1]
    pair_w = 2 * HEAD_DIM
    scale = 1.0 / math.sqrt(HEAD_DIM)
    gy = jnp.where(sc_ref[3] > 0, cot_ref[...], recv_ref[...])
    upper_ref[...] = gy
    gctx_scr[...] = lax.dot_general(
        gy, wout_ref[...], NT, preferred_element_type=F32).astype(BF16)
    lane = lax.broadcasted_iota(jnp.int32, (1, pair_w), 1)
    low = lane < HEAD_DIM
    for pair in range(width // pair_w):
        cols = pl.ds(pair * pair_w, pair_w)
        q2 = qkv_ref[:, pl.ds(pair * pair_w, pair_w)]
        k2 = qkv_ref[:, pl.ds(width + pair * pair_w, pair_w)]
        v2 = qkv_ref[:, pl.ds(2 * width + pair * pair_w, pair_w)]
        g2 = gctx_scr[:, cols]
        outs = []
        for half in range(2):
            mine = low if half == 0 else jnp.logical_not(low)
            gh = jnp.where(mine, g2, jnp.zeros_like(g2))
            pb = p_ref[2 * pair + half]
            p = pb.astype(F32)
            dp = lax.dot_general(gh, v2, NT, preferred_element_type=F32).astype(BF16).astype(F32)
            rd = jnp.sum(dp * p, axis=-1, keepdims=True)
            ds = (p * (dp - rd) * scale).astype(BF16)
            dq = jnp.dot(ds, k2, preferred_element_type=F32)
            dk = lax.dot_general(ds, q2, TN, preferred_element_type=F32)
            dv = lax.dot_general(pb, g2, TN, preferred_element_type=F32)
            outs.append((dq, dk, dv))
        lo, hi = outs
        rows_ref[:, pl.ds(pair * pair_w, pair_w)] = jnp.where(low, lo[0], hi[0]).astype(BF16)
        rows_ref[:, pl.ds(width + pair * pair_w, pair_w)] = jnp.where(low, lo[1], hi[1]).astype(BF16)
        rows_ref[:, pl.ds(2 * width + pair * pair_w, pair_w)] = jnp.where(low, lo[2], hi[2]).astype(BF16)
    gn = lax.dot_general(rows_ref[...], wqkv_ref[...], NT, preferred_element_type=F32)
    x = x_ref[...].astype(F32)
    mean = jnp.mean(x, axis=-1, keepdims=True)
    cen = x - mean
    inv = lax.rsqrt(jnp.mean(cen * cen, axis=-1, keepdims=True) + EPS)
    xn = cen * inv
    pgain_ref[...] = jnp.sum(gn * xn, axis=0, keepdims=True)
    gh = gn * gain_ref[...]
    gin = gy.astype(F32) + inv * (
        gh
        - jnp.mean(gh, axis=-1, keepdims=True)
        - xn * jnp.mean(gh * xn, axis=-1, keepdims=True)
    )
    gin = gin.astype(BF16)
    gin_ref[...] = gin
    gx_ref[...] = gin


def full_spec(shape):
    return pl.BlockSpec(shape, lambda i, sc: (0,) * len(shape))


def slot_spec(k, rows, cols):
    return pl.BlockSpec((None, rows, cols), lambda i, sc: (sc[k], 0, 0))


def attention_forward(sc, layer_in, gain_row, qkv_weight, bias, bufs, buf_shapes):
    micro, seq_len, width_model = layer_in.shape
    qkv_cols = qkv_weight.shape[1]
    ctx_cols = buf_shapes[1][2]
    heads = bias.shape[0]
    anyspec = pl.BlockSpec(memory_space=pl.ANY)
    flops = 2 * seq_len * width_model * qkv_cols + 4 * 2 * seq_len * seq_len * ctx_cols
    grid_spec = pltpu.PrefetchScalarGridSpec(
        num_scalar_prefetch=1,
        grid=(1,),
        in_specs=[
            slot_spec(1, seq_len, width_model),
            full_spec((1, width_model)),
            full_spec(qkv_weight.shape),
            full_spec(bias.shape),
        ] + ([anyspec, anyspec] if bufs is not None else []),
        out_specs=[
            full_spec((seq_len, qkv_cols)),
            full_spec((heads, seq_len, seq_len)),
            slot_spec(0, seq_len, width_model),
            slot_spec(0, seq_len, ctx_cols),
        ],
    )
    if bufs is None:
        kernel = lambda a, b, c, d, e, *outs: forward_kernel(a, b, c, d, e, None, None, *outs)
        extra, aliases = (), {}
    else:
        kernel, extra, aliases = forward_kernel, tuple(bufs), {5: 2, 6: 3}
    return pl.pallas_call(
        kernel,
        grid_spec=grid_spec,
        out_shape=(
            jax.ShapeDtypeStruct((seq_len, qkv_cols), BF16),
            jax.ShapeDtypeStruct((heads, seq_len, seq_len), BF16),
            *[jax.ShapeDtypeStruct(shape, BF16) for shape in buf_shapes],
        ),
        input_output_aliases=aliases,
        cost_estimate=pl.CostEstimate(
            flops=flops, transcendentals=bias.size, bytes_accessed=8 * 1024 * 1024),
        name="attention_forward",
    )(sc, layer_in, gain_row, qkv_weight, bias, *extra)


def attention_backward(sc, layer_in, cotangent, received, gain_row, qkv_weight, out_weight,
                       qkv, probs, bufs, buf_shapes):
    micro, seq_len, width_model = layer_in.shape
    qkv_cols = qkv_weight.shape[1]
    ctx_cols = out_weight.shape[0]
    anyspec = pl.BlockSpec(memory_space=pl.ANY)
    flops = 2 * seq_len * width_model * (qkv_cols + ctx_cols) + 8 * 2 * seq_len * seq_len * ctx_cols
    grid_spec = pltpu.PrefetchScalarGridSpec(
        num_scalar_prefetch=1,
        grid=(1,),
        in_specs=[
            slot_spec(1, seq_len, width_model),
            slot_spec(2, seq_len, width_model),
            full_spec((seq_len, width_model)),
            full_spec((1, width_model)),
            full_spec(qkv_weight.shape),
            full_spec(out_weight.shape),
            full_spec(qkv.shape),
            full_spec(probs.shape),
        ] + ([anyspec, anyspec, anyspec] if bufs is not None else []),
        out_specs=[
            full_spec((seq_len, width_model)),
            slot_spec(0, seq_len, width_model),
            slot_spec(0, seq_len, qkv_cols),
            slot_spec(0, seq_len, width_model),
            full_spec((1, width_model)),
        ],
        scratch_shapes=[pltpu.VMEM((seq_len, ctx_cols), BF16)],
    )
    if bufs is None:
        kernel = lambda *refs: backward_kernel(*refs[:9], None, None, None, *refs[9:])
        extra, aliases = (), {}
    else:
        kernel, extra, aliases = backward_kernel, tuple(bufs), {9: 1, 10: 2, 11: 3}
    return pl.pallas_call(
        kernel,
        grid_spec=grid_spec,
        out_shape=(
            jax.ShapeDtypeStruct((seq_len, width_model), BF16),
            *[jax.ShapeDtypeStruct(shape, BF16) for shape in buf_shapes],
            jax.ShapeDtypeStruct((1, width_model), F32),
        ),
        input_output_aliases=aliases,
        name="attention_backward",
        cost_estimate=pl.CostEstimate(
            flops=flops, transcendentals=0, bytes_accessed=10 * 1024 * 1024),
    )(sc, layer_in, cotangent, received, gain_row, qkv_weight, out_weight, qkv, probs, *extra)


def slot_part(slot, normed_buf, rows_buf, ctx_buf, upper_buf):
    pick = lambda buf: lax.dynamic_index_in_dim(buf, slot, 0, keepdims=False)
    return (
        lax.dot_general(pick(normed_buf), pick(rows_buf), TN, preferred_element_type=F32),
        lax.dot_general(pick(ctx_buf), pick(upper_buf), TN, preferred_element_type=F32),
    )


def on_device(
    segment_inputs, cotangent, order, norm_gain, w_qkv, w_out, global_blocks, random_blocks
):
    segments = lax.axis_size("segment")
    my_segment = lax.axis_index("segment")
    layer_in = segment_inputs[0]
    micro_count = layer_in.shape[0]
    seq_len = layer_in.shape[1]
    width_model = layer_in.shape[2]
    gain_row = norm_gain[0][None, :]
    qkv_weight = w_qkv[0]
    out_weight = w_out[0]
    slot_order = order[0]
    block_total = seq_len // BLOCK
    block_index, usable = block_ids(global_blocks[0], random_blocks[0], block_total)
    bias = dense_bias(block_index, usable, block_total, seq_len)
    dp_size = lax.axis_size("z") * lax.axis_size("y") * lax.axis_size("core")
    grad_scale = 1.0 / math.sqrt(dp_size * micro_count * seq_len)
    qkv_cols = qkv_weight.shape[1]
    ctx_cols = out_weight.shape[0]

    slots = micro_count + 1
    fwd_shapes = ((slots, seq_len, width_model), (slots, seq_len, ctx_cols))
    bwd_shapes = ((slots, seq_len, width_model), (slots, seq_len, qkv_cols), (slots, seq_len, width_model))
    fwd_bufs = None
    bwd_bufs = None
    gain_total = jnp.zeros((1, width_model), F32)
    received = cotangent[0]
    last_tick = micro_count + segments - 1
    use_cot = (my_segment == segments - 1).astype(jnp.int32)
    for timestep in range(last_tick):
        slot_now = timestep - (segments - 1) + my_segment
        active = (slot_now >= 0) & (slot_now < micro_count)
        slot_clip = jnp.clip(slot_now, 0, micro_count - 1)
        batch_id = slot_order[slot_clip]
        write_id = jnp.where(active, batch_id, jnp.int32(micro_count))
        sc = jnp.stack([write_id, batch_id, slot_clip, use_cot]).astype(jnp.int32)
        qkv, probs, normed_buf, ctx_buf = attention_forward(
            sc, layer_in, gain_row, qkv_weight, bias, fwd_bufs, fwd_shapes)
        fwd_bufs = (normed_buf, ctx_buf)
        grad_in, grad_x, rows_buf, upper_buf, part_gain = attention_backward(
            sc, layer_in, cotangent, received, gain_row, qkv_weight, out_weight, qkv, probs,
            bwd_bufs, bwd_shapes,
        )
        bwd_bufs = (grad_x, rows_buf, upper_buf)
        gain_total = gain_total + jnp.where(active, part_gain, jnp.zeros_like(part_gain))
        if timestep == last_tick - 2:
            early = slot_part(slot_order[0], normed_buf, rows_buf, ctx_buf, upper_buf)
        if timestep + 1 < last_tick:
            received = from_behind(grad_in, "segment", -1)
    late = slot_part(slot_order[1], normed_buf, rows_buf, ctx_buf, upper_buf)
    sum_qkv = early[0] + late[0]
    sum_out = early[1] + late[1]
    rows_total = qkv_weight.shape[0]
    fold = rows_total // ctx_cols
    out_folded = sum_out.reshape(rows_total, ctx_cols * width_model // rows_total)
    gain_col = gain_total.reshape(rows_total, width_model // rows_total)
    pad = jnp.zeros((rows_total, 128 - gain_col.shape[1]), BF16)
    out_gain = jnp.concatenate(
        [(out_folded * grad_scale).astype(BF16), (gain_col * grad_scale).astype(BF16), pad], axis=1)
    qkv_share, out_gain_share = dp_reduce_scatter((sum_qkv * grad_scale).astype(BF16), out_gain)
    share = jnp.concatenate([qkv_share, out_gain_share], axis=1)
    share_rows = share.shape[0]
    qkv_share = share[:, :qkv_cols]
    out_share = share[:, qkv_cols:qkv_cols + out_folded.shape[1]].reshape(share_rows // fold, width_model)
    gain_share = share[:, qkv_cols + out_folded.shape[1]:qkv_cols + out_folded.shape[1] + gain_col.shape[1]].reshape(-1)
    return (grad_x[:micro_count][None], qkv_share[None], out_share[None], gain_share[None])


def solution(mesh):
    dp = ("z", "y", "core")
    segs = mesh.shape["segment"]
    cores = 2
    ys = 4
    zs = mesh.shape["dp"] // (cores * ys)
    mesh4 = Mesh(mesh.devices.reshape(segs, zs, ys, cores), ("segment", "z", "y", "core"))
    in_specs = (
        P("segment", dp, None, None),
        P(dp, None, None),
        P(dp, None),
        P("segment", None),
        P("segment", None, None),
        P("segment", None, None),
        P("segment", None),
        P("segment", None, None, None),
    )
    out_specs = (
        P("segment", dp, None, None),
        P("segment", dp, None),
        P("segment", dp, None),
        P("segment", dp),
    )
    return jax.shard_map(
        on_device, mesh=mesh4, in_specs=in_specs, out_specs=out_specs, check_vma=False
    )
```
